32 devices in a mesh: gx: 8 (over z, x), gy: 4 (over y, core).
Axes of the slice: x: 2, y: 2, z: 4, core: 2. Of those that a mesh axis runs over, the one named last changes fastest.
Arguments:
- inputs: bfloat16 [3, 256, 8192], P(None, 'gy', 'gx'), may hold values from -600 to 600
- norm_gain: bfloat16 [8192], P('gx'), may hold values from 0.099609375 to 1.8984375
- query_weight: bfloat16 [8192, 8192], P('gx', 'gy'), may hold values from -0.0625 to 0.0625
- key_weight: bfloat16 [8192, 1024], P('gx', 'gy'), may hold values from -0.0625 to 0.0625
- value_weight: bfloat16 [8192, 1024], P('gx', 'gy'), may hold values from -0.0625 to 0.0625
- output_weight: bfloat16 [8192, 8192], P('gy', 'gx'), may hold values from -0.0625 to 0.0625
- query_down: bfloat16 [256, 8192, 64], P('gy', 'gx'), may hold values from -0.0625 to 0.0625
- query_up: bfloat16 [256, 64, 8192], P('gx', None, 'gy'), may hold values from -0.75 to 0.75
- output_down: bfloat16 [256, 8192, 64], P('gx', 'gy'), may hold values from -0.0625 to 0.0625
- output_up: bfloat16 [256, 64, 8192], P('gy', None, 'gx'), may hold values from -0.75 to 0.75
- block_adapter: int32 [2], replicated, may hold values from 0 to 255
- cache_lengths: int32 [256], P(('gx', 'gy')), may hold values from 1 to 256, as said below
- cache_keys: bfloat16 [256, 256, 1024], P(('gx', 'gy')), may hold values from -160 to 160
- cache_values: bfloat16 [256, 256, 1024], P(('gx', 'gy')), may hold values from -6 to 6
Outputs:
- block_output: bfloat16 [3, 256, 8192], P(None, 'gy', 'gx')
The draws below stay inside these ranges and needn't reach their ends.
Inputs may be any that keep to these rules, and one draw needn't show every extreme that they name: `cache_lengths`: some request has exactly 256 cached positions.
All inputs are finite; a program needn't handle non-finite values.
Results may differ from the reference program's by a relative error of at most 0.012.
The reference program's roundings to bfloat16 on the way count: a program that leaves them out, or rounds other values in their place, can miss the bound.
Values may be sent and summed in bfloat16 or wider, within the bound.
No kernel may reach another device: no remote copies, remote signals or barrier semaphores. Data moves between devices by JAX's collectives and lax.ppermute only.
A program may use at most 192 MiB of HBM per device.

```python
import math
import jax
import jax.numpy as jnp
import numpy as np
from jax import lax

D = 8192
QUERY_HEADS = 64
KEY_VALUE_HEADS = 8
HEAD_FEATURES = 128
RANK = 64
ADAPTERS = 256
BLOCK = 128
STEPS = 3
CONTEXT_SLOTS = 256
REQUEST_TOTAL = 256
QD = 8192
KVD = 1024
BLOCKS = 2


def draw_inputs(key, part):
    key_one, key_two = jax.random.split(key, 2)
    complete_shape = (STEPS, REQUEST_TOTAL, D)
    column = 10.0 ** (jnp.arange(D, dtype=jnp.float32) / D)
    base_part = jnp.clip(jax.random.normal(key_one, complete_shape, jnp.float32), -6.0, 6.0)
    row_scale = 10.0 ** jax.random.uniform(key_two, (STEPS, REQUEST_TOTAL, 1), jnp.float32, 0.0, 1.0)
    return (base_part * row_scale * column[None, None, :]).astype(jnp.bfloat16)


def draw_cache_lengths(key, part):
    key_one, key_two = jax.random.split(key)
    lengths = jax.random.randint(key_one, (REQUEST_TOTAL,), 1, CONTEXT_SLOTS + 1)
    chosen = jax.random.randint(key_two, (), 0, REQUEST_TOTAL)
    return jnp.where(jnp.arange(REQUEST_TOTAL) == chosen, CONTEXT_SLOTS, lengths).astype(jnp.int32)


def draw_cache_keys(key, part):
    key_one = jax.random.fold_in(key, 0)
    complete_shape = (REQUEST_TOTAL, CONTEXT_SLOTS, KEY_VALUE_HEADS * HEAD_FEATURES)
    base_part = jnp.clip(jax.random.normal(key_one, complete_shape, jnp.float32), -6.0, 6.0)
    return base_part.astype(jnp.bfloat16)


def level_of(rng, shape, cuts, low, top_value):
    level, own = 1.0, jax.random.fold_in(rng, 6)
    for dim, blocks in cuts:
        draws = jnp.exp(jax.random.uniform(jax.random.fold_in(own, dim), (blocks,), jnp.float32, low / len(cuts), top_value / len(cuts)))
        level = level * jnp.repeat(draws, shape[dim] // blocks).reshape([-1 if axis == dim else 1 for axis in range(len(shape))])
    return level


def rank_table(amount, lean):
    portions = [(1 << 20) // math.isqrt(grade ** lean) + 1 for grade in range(1, amount + 1)]
    scale = 1 + sum(portions) // (1 << 30)
    return np.cumsum(np.array([max(1, weight // scale) for weight in portions]))


def ranked(own_key, dims, amount, slope):
    table = rank_table(amount, slope)
    lot = jax.random.randint(jax.random.fold_in(own_key, 1), dims, 0, int(table[amount - 1]))
    standing = jnp.searchsorted(jnp.asarray(table, jnp.int32), lot, side="right")
    return jax.random.permutation(jax.random.fold_in(own_key, 2), amount)[standing].astype(jnp.int32)


def gaussian(stream_key, shape, scale, bound, cuts=(), kind=jnp.bfloat16):
    drawn = scale * jax.random.normal(stream_key, shape, jnp.float32)
    if cuts:
        drawn = drawn * level_of(stream_key, shape, cuts, -0.22, 0.18)
    return jnp.clip(drawn, -bound, bound).astype(kind)


def setup_inputs(seed: int = 0) -> dict:
    arg_keys = jax.random.split(jax.random.key(seed), 15)
    return {
        "inputs": draw_inputs(jax.random.fold_in(arg_keys[14], 71), 0),
        "norm_gain": jnp.clip(1.0 + 0.18 * jax.random.normal(arg_keys[1], (D,), jnp.float32), 0.099609375, 1.8984375).astype(jnp.bfloat16),
        "query_weight": gaussian(arg_keys[2], (D, QD), D ** -0.5, 0.0625, ((0, 8), (1, 4))),
        "key_weight": gaussian(arg_keys[3], (D, KVD), D ** -0.5, 0.0625, ((0, 8), (1, 4))),
        "value_weight": gaussian(arg_keys[4], (D, KVD), D ** -0.5, 0.0625, ((0, 8), (1, 4))),
        "output_weight": gaussian(arg_keys[5], (QD, D), QD ** -0.5, 0.0625, ((0, 4), (1, 8))),
        "query_down": gaussian(arg_keys[6], (ADAPTERS, D, RANK), D ** -0.5, 0.0625, ((0, 4), (1, 8))),
        "query_up": gaussian(arg_keys[7], (ADAPTERS, RANK, QD), RANK ** -0.5, 0.75, ((0, 8), (2, 4))),
        "output_down": gaussian(arg_keys[8], (ADAPTERS, QD, RANK), QD ** -0.5, 0.0625, ((0, 8), (1, 4))),
        "output_up": gaussian(arg_keys[9], (ADAPTERS, RANK, D), RANK ** -0.5, 0.75, ((0, 4), (2, 8))),
        "block_adapter": ranked(arg_keys[10], (BLOCKS,), ADAPTERS, 2),
        "cache_lengths": draw_cache_lengths(jax.random.fold_in(arg_keys[14], 71), 0),
        "cache_keys": draw_cache_keys(jax.random.fold_in(arg_keys[14], 71), 0),
        "cache_values": gaussian(arg_keys[13], (REQUEST_TOTAL, CONTEXT_SLOTS, KVD), 1.0, 6.0, ((0, 32),)),
    }


EPS = 1e-05
THETA = 500000.0

def rotary_embedding(values_in, token_positions):
    half_size = values_in.shape[-1] // 2
    exponent = jnp.arange(half_size, dtype=jnp.float32) * 2.0 / values_in.shape[-1]
    frequency = THETA ** (-exponent)
    angles = token_positions.astype(jnp.float32)[:, None] * frequency[None, :]
    cosine = jnp.cos(angles)[:, None, :]
    sine_part = jnp.sin(angles)[:, None, :]
    lower = values_in[..., :half_size]
    upper = values_in[..., half_size:]
    return jnp.concatenate([lower * cosine - upper * sine_part, upper * cosine + lower * sine_part], axis=-1)

def attend(query_rows, previous_keys, previous_values, incoming_keys, incoming_values, lengths, step_index):
    count_of_rows = query_rows.shape[0]
    context_window = previous_keys.shape[1]
    grouped_heads = query_rows.astype(jnp.float32).reshape(count_of_rows, KEY_VALUE_HEADS, QUERY_HEADS // KEY_VALUE_HEADS, HEAD_FEATURES)
    keys_previous = previous_keys.astype(jnp.float32).reshape(count_of_rows, context_window, KEY_VALUE_HEADS, HEAD_FEATURES)
    values_previous = previous_values.astype(jnp.float32).reshape(count_of_rows, context_window, KEY_VALUE_HEADS, HEAD_FEATURES)
    keys_incoming = incoming_keys.astype(jnp.float32).reshape(count_of_rows, -1, KEY_VALUE_HEADS, HEAD_FEATURES)
    values_incoming = incoming_values.astype(jnp.float32).reshape(count_of_rows, -1, KEY_VALUE_HEADS, HEAD_FEATURES)
    factor = HEAD_FEATURES ** (-0.5)
    score_old = jnp.einsum('rhgd,rchd->rhgc', grouped_heads, keys_previous) * factor
    score_new = jnp.einsum('rhgd,rshd->rhgs', grouped_heads, keys_incoming) * factor
    live_old = (jnp.arange(context_window, dtype=jnp.int32)[None, :] < lengths[:, None])[:, None, None, :]
    live_new = (jnp.arange(keys_incoming.shape[1], dtype=jnp.int32) <= step_index)[None, None, None, :]
    score_old = jnp.where(live_old, score_old, -1e+30)
    score_new = jnp.where(live_new, score_new, -1e+30)
    peak_score = jnp.maximum(lax.optimization_barrier(jnp.max(score_old, axis=-1)), lax.optimization_barrier(jnp.max(score_new, axis=-1)))
    weight_old = jnp.where(live_old, jnp.exp(score_old - peak_score[..., None]), 0.0)
    weight_new = jnp.where(live_new, jnp.exp(score_new - peak_score[..., None]), 0.0)
    weight_sum = lax.optimization_barrier(jnp.sum(weight_old, axis=-1)) + lax.optimization_barrier(jnp.sum(weight_new, axis=-1))
    rounded_old = weight_old.astype(jnp.bfloat16).astype(jnp.float32)
    rounded_new = weight_new.astype(jnp.bfloat16).astype(jnp.float32)
    mixed_out = jnp.einsum('rhgc,rchd->rhgd', rounded_old, values_previous) + jnp.einsum('rhgs,rshd->rhgd', rounded_new, values_incoming)
    return (mixed_out / weight_sum[..., None]).reshape(count_of_rows, -1).astype(jnp.bfloat16)

def reference(inputs, norm_gain, query_weight, key_weight, value_weight, output_weight, query_down, query_up, output_down, output_up, block_adapter, cache_lengths, cache_keys, cache_values):
    incoming_keys = jnp.zeros((REQUEST_TOTAL, STEPS, KVD), jnp.bfloat16)
    incoming_values = jnp.zeros((REQUEST_TOTAL, STEPS, KVD), jnp.bfloat16)
    query_first = query_down[block_adapter].astype(jnp.float32)
    query_second = query_up[block_adapter].astype(jnp.float32)
    output_first = output_down[block_adapter].astype(jnp.float32)
    output_second = output_up[block_adapter].astype(jnp.float32)
    norm_scale = norm_gain.astype(jnp.float32)
    results = []
    for step_index in range(STEPS):
        rows_all = inputs[step_index].astype(jnp.float32)
        mean_square = lax.optimization_barrier(jnp.mean(rows_all * rows_all, axis=-1))
        normed = (rows_all * lax.rsqrt(mean_square + EPS)[:, None] * norm_scale[None, :]).astype(jnp.bfloat16)
        rank_query = jnp.einsum('bnd,bdr->bnr', normed.reshape(BLOCKS, BLOCK, D).astype(jnp.float32), query_first).astype(jnp.bfloat16)
        delta_query = jnp.einsum('bnr,bre->bne', rank_query.astype(jnp.float32), query_second).reshape(REQUEST_TOTAL, QD)
        query_full = (jnp.dot(normed, query_weight, preferred_element_type=jnp.float32) + delta_query).astype(jnp.bfloat16)
        key_complete = jnp.dot(normed, key_weight, preferred_element_type=jnp.float32).astype(jnp.bfloat16)
        value_full = jnp.dot(normed, value_weight, preferred_element_type=jnp.float32).astype(jnp.bfloat16)
        token_positions = cache_lengths + step_index
        query_rot = rotary_embedding(query_full.astype(jnp.float32).reshape(REQUEST_TOTAL, QUERY_HEADS, HEAD_FEATURES), token_positions).astype(jnp.bfloat16)
        key_rotated = rotary_embedding(key_complete.astype(jnp.float32).reshape(REQUEST_TOTAL, KEY_VALUE_HEADS, HEAD_FEATURES), token_positions).astype(jnp.bfloat16)
        incoming_keys = incoming_keys.at[:, step_index].set(key_rotated.reshape(REQUEST_TOTAL, KVD))
        incoming_values = incoming_values.at[:, step_index].set(value_full)

        def one_block(pieces, step_now=step_index):
            return attend(pieces[0], pieces[1], pieces[2], pieces[3], pieces[4], pieces[5], step_now)
        mixed_heads = lax.map(one_block, (query_rot.reshape(BLOCKS, BLOCK, QD), cache_keys.reshape(BLOCKS, BLOCK, CONTEXT_SLOTS, KVD), cache_values.reshape(BLOCKS, BLOCK, CONTEXT_SLOTS, KVD), incoming_keys.reshape(BLOCKS, BLOCK, STEPS, KVD), incoming_values.reshape(BLOCKS, BLOCK, STEPS, KVD), cache_lengths.reshape(BLOCKS, BLOCK))).reshape(REQUEST_TOTAL, QD)
        rank_output = jnp.einsum('bnq,bqr->bnr', mixed_heads.reshape(BLOCKS, BLOCK, QD).astype(jnp.float32), output_first).astype(jnp.bfloat16)
        delta_output = jnp.einsum('bnr,bre->bne', rank_output.astype(jnp.float32), output_second).reshape(REQUEST_TOTAL, D)
        results.append((jnp.dot(mixed_heads, output_weight, preferred_element_type=jnp.float32) + delta_output).astype(jnp.bfloat16))
    return jnp.stack(results)
```

```python
import jax
import jax.numpy as jnp
from jax import lax
from jax.sharding import PartitionSpec as P

QUERY_HEADS = 64
KEY_VALUE_HEADS = 8
HEAD_FEATURES = 128
BLOCK = 128


EPS = 1e-05
THETA = 500000.0


def rotary_embedding(values_in, token_positions):
    half_size = values_in.shape[-1] // 2
    exponent = jnp.arange(half_size, dtype=jnp.float32) * 2.0 / values_in.shape[-1]
    frequency = THETA ** (-exponent)
    angles = token_positions.astype(jnp.float32)[:, None] * frequency[None, :]
    cosine = jnp.cos(angles)[:, None, :]
    sine_part = jnp.sin(angles)[:, None, :]
    lower = values_in[..., :half_size]
    upper = values_in[..., half_size:]
    return jnp.concatenate(
        [lower * cosine - upper * sine_part, upper * cosine + lower * sine_part], axis=-1
    )


def pick_adapters(table, adapter_ids, owner_index):
    table_count = table.shape[0]
    picked = []
    for block in range(adapter_ids.shape[0]):
        wanted = adapter_ids[block]
        owned = (wanted // table_count) == owner_index
        entry = lax.dynamic_index_in_dim(table, wanted % table_count, axis=0, keepdims=False)
        picked.append(jnp.where(owned, entry, jnp.zeros_like(entry)))
    return jnp.stack(picked)


def attend(query_rows, previous_keys, previous_values, incoming_keys, incoming_values, lengths):
    steps, count_of_rows = query_rows.shape[0], query_rows.shape[1]
    groups = QUERY_HEADS // KEY_VALUE_HEADS
    context_window = previous_keys.shape[1]
    grouped_heads = query_rows.reshape(
        steps, count_of_rows, KEY_VALUE_HEADS, groups, HEAD_FEATURES
    ).transpose(1, 2, 0, 3, 4).reshape(count_of_rows, KEY_VALUE_HEADS, steps * groups, HEAD_FEATURES)
    keys_previous = previous_keys.reshape(
        count_of_rows, context_window, KEY_VALUE_HEADS, HEAD_FEATURES
    )
    values_previous = previous_values.reshape(
        count_of_rows, context_window, KEY_VALUE_HEADS, HEAD_FEATURES
    )
    keys_incoming = incoming_keys.reshape(
        steps, count_of_rows, KEY_VALUE_HEADS, HEAD_FEATURES
    ).transpose(1, 0, 2, 3)
    values_incoming = incoming_values.reshape(
        steps, count_of_rows, KEY_VALUE_HEADS, HEAD_FEATURES
    ).transpose(1, 0, 2, 3)
    factor = HEAD_FEATURES ** (-0.5)
    score_old = (
        jnp.einsum(
            "rhqd,rchd->rhqc", grouped_heads, keys_previous, preferred_element_type=jnp.float32
        )
        * factor
    )
    score_new = (
        jnp.einsum(
            "rhqd,rshd->rhqs", grouped_heads, keys_incoming, preferred_element_type=jnp.float32
        )
        * factor
    )
    live_old = (jnp.arange(context_window, dtype=jnp.int32)[None, :] < lengths[:, None])[
        :, None, None, :
    ]
    query_step = jnp.arange(steps * groups, dtype=jnp.int32) // groups
    live_new = (jnp.arange(steps, dtype=jnp.int32)[None, :] <= query_step[:, None])[
        None, None, :, :
    ]
    score_old = jnp.where(live_old, score_old, -1e30)
    score_new = jnp.where(live_new, score_new, -1e30)
    peak_score = jnp.maximum(jnp.max(score_old, axis=-1), jnp.max(score_new, axis=-1))
    weight_old = jnp.where(live_old, jnp.exp(score_old - peak_score[..., None]), 0.0)
    weight_new = jnp.where(live_new, jnp.exp(score_new - peak_score[..., None]), 0.0)
    weight_sum = jnp.sum(weight_old, axis=-1) + jnp.sum(weight_new, axis=-1)
    mixed_out = jnp.einsum(
        "rhqc,rchd->rhqd",
        weight_old.astype(jnp.bfloat16),
        values_previous,
        preferred_element_type=jnp.float32,
    )
    mixed_out = mixed_out + jnp.einsum(
        "rhqs,rshd->rhqd",
        weight_new.astype(jnp.bfloat16),
        values_incoming,
        preferred_element_type=jnp.float32,
    )
    mixed_out = (mixed_out / weight_sum[..., None]).astype(jnp.bfloat16)
    return mixed_out.reshape(
        count_of_rows, KEY_VALUE_HEADS, steps, groups, HEAD_FEATURES
    ).transpose(2, 0, 1, 3, 4).reshape(steps, count_of_rows, -1)


def local(
    inputs,
    norm_gain,
    query_weight,
    key_weight,
    value_weight,
    output_weight,
    query_down,
    query_up,
    output_down,
    output_up,
    block_adapter,
    cache_lengths,
    cache_keys,
    cache_values,
):
    across_first = lax.axis_size("gx")
    across_second = lax.axis_size("gy")
    index_first = lax.axis_index("gx")
    index_second = lax.axis_index("gy")
    steps = inputs.shape[0]
    request_count = inputs.shape[1] * across_second
    width = inputs.shape[2] * across_first
    local_rows = cache_keys.shape[0]
    block_count = block_adapter.shape[0]
    block_rows = request_count // block_count
    query_width = query_weight.shape[1]
    key_width = key_weight.shape[1]
    norm_scale = norm_gain.astype(jnp.float32)
    query_first = pick_adapters(query_down, block_adapter, index_second)
    query_second = pick_adapters(query_up, block_adapter, index_first)
    output_first = pick_adapters(output_down, block_adapter, index_first)
    output_second = pick_adapters(output_up, block_adapter, index_second)

    rows_all = lax.all_gather(inputs, "gy", axis=1, tiled=True)
    rows_wide = rows_all.astype(jnp.float32)
    squares = lax.psum(jnp.sum(rows_wide * rows_wide, axis=2), "gx")
    factor_rows = lax.rsqrt(squares / width + EPS)
    normed = (rows_wide * factor_rows[..., None] * norm_scale).astype(jnp.bfloat16)

    blocked = normed.reshape(steps, block_count, block_rows, -1)
    rank_part = jnp.einsum(
        "tbnd,bdr->tbnr", blocked, query_first, preferred_element_type=jnp.float32
    )
    rank_query = lax.psum(rank_part, ("gx", "gy")).astype(jnp.bfloat16)
    delta_query = jnp.einsum(
        "tbnr,bre->tbne", rank_query, query_second, preferred_element_type=jnp.float32
    ).reshape(steps, request_count, -1)
    part_query = (
        jnp.einsum("tnd,de->tne", normed, query_weight, preferred_element_type=jnp.float32)
        + delta_query
    )
    part_key = jnp.einsum("tnd,de->tne", normed, key_weight, preferred_element_type=jnp.float32)
    part_value = jnp.einsum(
        "tnd,de->tne", normed, value_weight, preferred_element_type=jnp.float32
    )
    joined = jnp.concatenate([part_query, part_key, part_value], axis=-1)
    summed = lax.psum_scatter(joined, "gx", scatter_dimension=1, tiled=True).astype(jnp.bfloat16)
    chunk_rows = summed.shape[1] // across_second
    spread = lax.all_to_all(
        summed.reshape(steps, across_second, chunk_rows, -1), "gy", 1, 2, tiled=False
    )
    query_full = spread[..., :query_width].reshape(steps, local_rows, -1)
    key_full = spread[..., query_width : query_width + key_width].reshape(steps, local_rows, -1)
    value_full = spread[..., query_width + key_width :].reshape(steps, local_rows, -1)

    token_positions = (
        cache_lengths[None, :] + jnp.arange(steps, dtype=jnp.int32)[:, None]
    ).reshape(-1)
    query_rot = rotary_embedding(
        query_full.astype(jnp.float32).reshape(steps * local_rows, QUERY_HEADS, HEAD_FEATURES),
        token_positions,
    ).astype(jnp.bfloat16)
    key_rot = rotary_embedding(
        key_full.astype(jnp.float32).reshape(steps * local_rows, KEY_VALUE_HEADS, HEAD_FEATURES),
        token_positions,
    ).astype(jnp.bfloat16)
    mixed_local = attend(
        query_rot.reshape(steps, local_rows, -1),
        cache_keys,
        cache_values,
        key_rot.reshape(steps, local_rows, -1),
        value_full,
        cache_lengths,
    )
    head_group = lax.all_to_all(
        mixed_local.reshape(steps, local_rows, across_second, -1), "gy", 2, 1, tiled=False
    ).reshape(steps, across_second * local_rows, -1)
    mixed_all = lax.all_gather(head_group, "gx", axis=1, tiled=True)
    rank_part_out = jnp.einsum(
        "tbnq,bqr->tbnr",
        mixed_all.reshape(steps, block_count, block_rows, -1),
        output_first,
        preferred_element_type=jnp.float32,
    )
    rank_output = lax.psum(rank_part_out, ("gx", "gy")).astype(jnp.bfloat16)
    delta_output = jnp.einsum(
        "tbnr,bre->tbne", rank_output, output_second, preferred_element_type=jnp.float32
    ).reshape(steps, request_count, -1)
    partial_out = (
        jnp.einsum("tnq,qe->tne", mixed_all, output_weight, preferred_element_type=jnp.float32)
        + delta_output
    )
    return lax.psum_scatter(partial_out, "gy", scatter_dimension=1, tiled=True).astype(
        jnp.bfloat16
    )


def solution(mesh):
    in_specs = (
        P(None, "gy", "gx"),
        P("gx"),
        P("gx", "gy"),
        P("gx", "gy"),
        P("gx", "gy"),
        P("gy", "gx"),
        P("gy", "gx", None),
        P("gx", None, "gy"),
        P("gx", "gy", None),
        P("gy", None, "gx"),
        P(),
        P(("gx", "gy")),
        P(("gx", "gy"), None, None),
        P(("gx", "gy"), None, None),
    )
    out_specs = P(None, "gy", "gx")
    return jax.shard_map(local, mesh=mesh, in_specs=in_specs, out_specs=out_specs, check_vma=False)
```

```python
import jax
import jax.numpy as jnp
from jax import lax
from jax.sharding import PartitionSpec as P

QUERY_HEADS = 64
KEY_VALUE_HEADS = 8
HEAD_FEATURES = 128
BLOCK = 128


EPS = 1e-05
THETA = 500000.0


def rotary_embedding(values_in, token_positions):
    half_size = values_in.shape[-1] // 2
    exponent = jnp.arange(half_size, dtype=jnp.float32) * 2.0 / values_in.shape[-1]
    frequency = THETA ** (-exponent)
    angles = token_positions.astype(jnp.float32)[:, None] * frequency[None, :]
    cosine = jnp.cos(angles)[:, None, :]
    sine_part = jnp.sin(angles)[:, None, :]
    lower = values_in[..., :half_size]
    upper = values_in[..., half_size:]
    return jnp.concatenate(
        [lower * cosine - upper * sine_part, upper * cosine + lower * sine_part], axis=-1
    )


def pick_adapters(table, adapter_ids, owner_index):
    table_count = table.shape[0]
    picked = []
    for block in range(adapter_ids.shape[0]):
        wanted = adapter_ids[block]
        owned = (wanted // table_count) == owner_index
        entry = lax.dynamic_index_in_dim(table, wanted % table_count, axis=0, keepdims=False)
        picked.append(jnp.where(owned, entry, jnp.zeros_like(entry)))
    return jnp.stack(picked)


def reduce_scatter_rows(partial, axis_name, axis_size):
    steps, rows, columns = partial.shape
    pieces = partial.astype(jnp.bfloat16).reshape(steps, axis_size, rows // axis_size, columns)
    received = lax.all_to_all(pieces, axis_name, 1, 1, tiled=False)
    return jnp.sum(received.astype(jnp.float32), axis=1)


def attend(query_rows, previous_keys, previous_values, incoming_keys, incoming_values, lengths):
    steps, count_of_rows = query_rows.shape[0], query_rows.shape[1]
    groups = QUERY_HEADS // KEY_VALUE_HEADS
    context_window = previous_keys.shape[1]
    grouped_heads = query_rows.reshape(
        steps, count_of_rows, KEY_VALUE_HEADS, groups, HEAD_FEATURES
    ).transpose(1, 2, 0, 3, 4).reshape(count_of_rows, KEY_VALUE_HEADS, steps * groups, HEAD_FEATURES)
    keys_previous = previous_keys.reshape(
        count_of_rows, context_window, KEY_VALUE_HEADS, HEAD_FEATURES
    )
    values_previous = previous_values.reshape(
        count_of_rows, context_window, KEY_VALUE_HEADS, HEAD_FEATURES
    )
    keys_incoming = incoming_keys.reshape(
        steps, count_of_rows, KEY_VALUE_HEADS, HEAD_FEATURES
    ).transpose(1, 0, 2, 3)
    values_incoming = incoming_values.reshape(
        steps, count_of_rows, KEY_VALUE_HEADS, HEAD_FEATURES
    ).transpose(1, 0, 2, 3)
    factor = HEAD_FEATURES ** (-0.5)
    score_old = (
        jnp.einsum(
            "rhqd,rchd->rhqc", grouped_heads, keys_previous, preferred_element_type=jnp.float32
        )
        * factor
    )
    score_new = (
        jnp.einsum(
            "rhqd,rshd->rhqs", grouped_heads, keys_incoming, preferred_element_type=jnp.float32
        )
        * factor
    )
    live_old = (jnp.arange(context_window, dtype=jnp.int32)[None, :] < lengths[:, None])[
        :, None, None, :
    ]
    query_step = jnp.arange(steps * groups, dtype=jnp.int32) // groups
    live_new = (jnp.arange(steps, dtype=jnp.int32)[None, :] <= query_step[:, None])[
        None, None, :, :
    ]
    score_old = jnp.where(live_old, score_old, -1e30)
    score_new = jnp.where(live_new, score_new, -1e30)
    peak_score = jnp.maximum(jnp.max(score_old, axis=-1), jnp.max(score_new, axis=-1))
    weight_old = jnp.where(live_old, jnp.exp(score_old - peak_score[..., None]), 0.0)
    weight_new = jnp.where(live_new, jnp.exp(score_new - peak_score[..., None]), 0.0)
    weight_sum = jnp.sum(weight_old, axis=-1) + jnp.sum(weight_new, axis=-1)
    mixed_out = jnp.einsum(
        "rhqc,rchd->rhqd",
        weight_old.astype(jnp.bfloat16),
        values_previous,
        preferred_element_type=jnp.float32,
    )
    mixed_out = mixed_out + jnp.einsum(
        "rhqs,rshd->rhqd",
        weight_new.astype(jnp.bfloat16),
        values_incoming,
        preferred_element_type=jnp.float32,
    )
    mixed_out = (mixed_out / weight_sum[..., None]).astype(jnp.bfloat16)
    return mixed_out.reshape(
        count_of_rows, KEY_VALUE_HEADS, steps, groups, HEAD_FEATURES
    ).transpose(2, 0, 1, 3, 4).reshape(steps, count_of_rows, -1)


def local(
    inputs,
    norm_gain,
    query_weight,
    key_weight,
    value_weight,
    output_weight,
    query_down,
    query_up,
    output_down,
    output_up,
    block_adapter,
    cache_lengths,
    cache_keys,
    cache_values,
):
    across_first = lax.axis_size("gx")
    across_second = lax.axis_size("gy")
    index_first = lax.axis_index("gx")
    index_second = lax.axis_index("gy")
    steps = inputs.shape[0]
    request_count = inputs.shape[1] * across_second
    width = inputs.shape[2] * across_first
    local_rows = cache_keys.shape[0]
    block_count = block_adapter.shape[0]
    block_rows = request_count // block_count
    query_width = query_weight.shape[1]
    key_width = key_weight.shape[1]
    norm_scale = norm_gain.astype(jnp.float32)
    query_first = pick_adapters(query_down, block_adapter, index_second)
    query_second = pick_adapters(query_up, block_adapter, index_first)
    output_first = pick_adapters(output_down, block_adapter, index_first)
    output_second = pick_adapters(output_up, block_adapter, index_second)

    rows_all = lax.all_gather(inputs, "gy", axis=1, tiled=True)
    rows_wide = rows_all.astype(jnp.float32)
    squares = lax.psum(jnp.sum(rows_wide * rows_wide, axis=2), "gx")
    factor_rows = lax.rsqrt(squares / width + EPS)
    normed = (rows_wide * factor_rows[..., None] * norm_scale).astype(jnp.bfloat16)

    blocked = normed.reshape(steps, block_count, block_rows, -1)
    rank_part = jnp.einsum(
        "tbnd,bdr->tbnr", blocked, query_first, preferred_element_type=jnp.float32
    )
    rank_query = lax.psum(rank_part, ("gx", "gy")).astype(jnp.bfloat16)
    delta_query = jnp.einsum(
        "tbnr,bre->tbne", rank_query, query_second, preferred_element_type=jnp.float32
    ).reshape(steps, request_count, -1)
    part_query = (
        jnp.einsum("tnd,de->tne", normed, query_weight, preferred_element_type=jnp.float32)
        + delta_query
    )
    part_key = jnp.einsum("tnd,de->tne", normed, key_weight, preferred_element_type=jnp.float32)
    part_value = jnp.einsum(
        "tnd,de->tne", normed, value_weight, preferred_element_type=jnp.float32
    )
    joined = jnp.concatenate([part_query, part_key, part_value], axis=-1)
    summed = reduce_scatter_rows(joined, "gx", across_first).astype(jnp.bfloat16)
    chunk_rows = summed.shape[1] // across_second
    spread = lax.all_to_all(
        summed.reshape(steps, across_second, chunk_rows, -1), "gy", 1, 2, tiled=False
    )
    query_full = spread[..., :query_width].reshape(steps, local_rows, -1)
    key_full = spread[..., query_width : query_width + key_width].reshape(steps, local_rows, -1)
    value_full = spread[..., query_width + key_width :].reshape(steps, local_rows, -1)

    token_positions = (
        cache_lengths[None, :] + jnp.arange(steps, dtype=jnp.int32)[:, None]
    ).reshape(-1)
    query_rot = rotary_embedding(
        query_full.astype(jnp.float32).reshape(steps * local_rows, QUERY_HEADS, HEAD_FEATURES),
        token_positions,
    ).astype(jnp.bfloat16)
    key_rot = rotary_embedding(
        key_full.astype(jnp.float32).reshape(steps * local_rows, KEY_VALUE_HEADS, HEAD_FEATURES),
        token_positions,
    ).astype(jnp.bfloat16)
    mixed_local = attend(
        query_rot.reshape(steps, local_rows, -1),
        cache_keys,
        cache_values,
        key_rot.reshape(steps, local_rows, -1),
        value_full,
        cache_lengths,
    )
    head_group = lax.all_to_all(
        mixed_local.reshape(steps, local_rows, across_second, -1), "gy", 2, 1, tiled=False
    ).reshape(steps, across_second * local_rows, -1)
    mixed_all = lax.all_gather(head_group, "gx", axis=1, tiled=True)
    rank_part_out = jnp.einsum(
        "tbnq,bqr->tbnr",
        mixed_all.reshape(steps, block_count, block_rows, -1),
        output_first,
        preferred_element_type=jnp.float32,
    )
    rank_output = lax.psum(rank_part_out, ("gx", "gy")).astype(jnp.bfloat16)
    delta_output = jnp.einsum(
        "tbnr,bre->tbne", rank_output, output_second, preferred_element_type=jnp.float32
    ).reshape(steps, request_count, -1)
    partial_out = (
        jnp.einsum("tnq,qe->tne", mixed_all, output_weight, preferred_element_type=jnp.float32)
        + delta_output
    )
    return reduce_scatter_rows(partial_out, "gy", across_second).astype(jnp.bfloat16)


def solution(mesh):
    in_specs = (
        P(None, "gy", "gx"),
        P("gx"),
        P("gx", "gy"),
        P("gx", "gy"),
        P("gx", "gy"),
        P("gy", "gx"),
        P("gy", "gx", None),
        P("gx", None, "gy"),
        P("gx", "gy", None),
        P("gy", None, "gx"),
        P(),
        P(("gx", "gy")),
        P(("gx", "gy"), None, None),
        P(("gx", "gy"), None, None),
    )
    out_specs = P(None, "gy", "gx")
    return jax.shard_map(local, mesh=mesh, in_specs=in_specs, out_specs=out_specs, check_vma=False)
```

```python
import jax
import jax.numpy as jnp
from jax import lax
from jax.sharding import PartitionSpec as P

QUERY_HEADS = 64
KEY_VALUE_HEADS = 8
HEAD_FEATURES = 128
BLOCK = 128


EPS = 1e-05
THETA = 500000.0


def rotary_embedding(values_in, token_positions):
    half_size = values_in.shape[-1] // 2
    exponent = jnp.arange(half_size, dtype=jnp.float32) * 2.0 / values_in.shape[-1]
    frequency = THETA ** (-exponent)
    angles = token_positions.astype(jnp.float32)[:, None] * frequency[None, :]
    cosine = jnp.cos(angles)[:, None, :]
    sine_part = jnp.sin(angles)[:, None, :]
    lower = values_in[..., :half_size]
    upper = values_in[..., half_size:]
    return jnp.concatenate(
        [lower * cosine - upper * sine_part, upper * cosine + lower * sine_part], axis=-1
    )


def pick_adapters(table, adapter_ids, owner_index):
    table_count = table.shape[0]
    picked = []
    for block in range(adapter_ids.shape[0]):
        wanted = adapter_ids[block]
        owned = (wanted // table_count) == owner_index
        entry = lax.dynamic_index_in_dim(table, wanted % table_count, axis=0, keepdims=False)
        picked.append(jnp.where(owned, entry, jnp.zeros_like(entry)))
    return jnp.stack(picked)


def reduce_scatter_rows(partial, axis_name, axis_size):
    steps, rows, columns = partial.shape
    pieces = partial.astype(jnp.bfloat16).reshape(steps, axis_size, rows // axis_size, columns)
    received = lax.all_to_all(pieces, axis_name, 1, 1, tiled=False)
    return jnp.sum(received.astype(jnp.float32), axis=1)


def tree_sum(value, axes):
    for axis_name in axes:
        size = lax.axis_size(axis_name)
        if size & (size - 1):
            value = lax.psum(value, axis_name)
            continue
        distance = 1
        while distance < size:
            pairs = [(i, i ^ distance) for i in range(size)]
            value = value + lax.ppermute(value, axis_name, pairs)
            distance *= 2
    return value


def halving_scatter(partial, axis_name, axis_size):
    steps, rows, columns = partial.shape
    if axis_size & (axis_size - 1):
        return lax.psum_scatter(partial, axis_name, scatter_dimension=1, tiled=True)
    me = lax.axis_index(axis_name)
    held = partial.reshape(steps, axis_size, rows // axis_size, columns)
    distance = 1
    while distance < axis_size:
        count = held.shape[1]
        pairs = held.reshape(steps, count // 2, 2, rows // axis_size, columns)
        mine = (me // distance) % 2
        keep = lax.dynamic_index_in_dim(pairs, mine, axis=2, keepdims=False)
        give = lax.dynamic_index_in_dim(pairs, 1 - mine, axis=2, keepdims=False)
        swap = [(i, i ^ distance) for i in range(axis_size)]
        held = keep + lax.ppermute(give, axis_name, swap)
        distance *= 2
    return held.reshape(steps, rows // axis_size, columns)


def attend(query_rows, previous_keys, previous_values, incoming_keys, incoming_values, lengths):
    steps, count_of_rows = query_rows.shape[0], query_rows.shape[1]
    groups = QUERY_HEADS // KEY_VALUE_HEADS
    context_window = previous_keys.shape[1]
    grouped_heads = query_rows.reshape(
        steps, count_of_rows, KEY_VALUE_HEADS, groups, HEAD_FEATURES
    ).transpose(1, 2, 0, 3, 4).reshape(count_of_rows, KEY_VALUE_HEADS, steps * groups, HEAD_FEATURES)
    keys_previous = previous_keys.reshape(
        count_of_rows, context_window, KEY_VALUE_HEADS, HEAD_FEATURES
    )
    values_previous = previous_values.reshape(
        count_of_rows, context_window, KEY_VALUE_HEADS, HEAD_FEATURES
    )
    keys_incoming = incoming_keys.reshape(
        steps, count_of_rows, KEY_VALUE_HEADS, HEAD_FEATURES
    ).transpose(1, 0, 2, 3)
    values_incoming = incoming_values.reshape(
        steps, count_of_rows, KEY_VALUE_HEADS, HEAD_FEATURES
    ).transpose(1, 0, 2, 3)
    factor = HEAD_FEATURES ** (-0.5)
    score_old = (
        jnp.einsum(
            "rhqd,rchd->rhqc", grouped_heads, keys_previous, preferred_element_type=jnp.float32
        )
        * factor
    )
    score_new = (
        jnp.einsum(
            "rhqd,rshd->rhqs", grouped_heads, keys_incoming, preferred_element_type=jnp.float32
        )
        * factor
    )
    live_old = (jnp.arange(context_window, dtype=jnp.int32)[None, :] < lengths[:, None])[
        :, None, None, :
    ]
    query_step = jnp.arange(steps * groups, dtype=jnp.int32) // groups
    live_new = (jnp.arange(steps, dtype=jnp.int32)[None, :] <= query_step[:, None])[
        None, None, :, :
    ]
    score_old = jnp.where(live_old, score_old, -1e30)
    score_new = jnp.where(live_new, score_new, -1e30)
    peak_score = jnp.maximum(jnp.max(score_old, axis=-1), jnp.max(score_new, axis=-1))
    weight_old = jnp.where(live_old, jnp.exp(score_old - peak_score[..., None]), 0.0)
    weight_new = jnp.where(live_new, jnp.exp(score_new - peak_score[..., None]), 0.0)
    weight_sum = jnp.sum(weight_old, axis=-1) + jnp.sum(weight_new, axis=-1)
    mixed_out = jnp.einsum(
        "rhqc,rchd->rhqd",
        weight_old.astype(jnp.bfloat16),
        values_previous,
        preferred_element_type=jnp.float32,
    )
    mixed_out = mixed_out + jnp.einsum(
        "rhqs,rshd->rhqd",
        weight_new.astype(jnp.bfloat16),
        values_incoming,
        preferred_element_type=jnp.float32,
    )
    mixed_out = (mixed_out / weight_sum[..., None]).astype(jnp.bfloat16)
    return mixed_out.reshape(
        count_of_rows, KEY_VALUE_HEADS, steps, groups, HEAD_FEATURES
    ).transpose(2, 0, 1, 3, 4).reshape(steps, count_of_rows, -1)


def local(
    inputs,
    norm_gain,
    query_weight,
    key_weight,
    value_weight,
    output_weight,
    query_down,
    query_up,
    output_down,
    output_up,
    block_adapter,
    cache_lengths,
    cache_keys,
    cache_values,
):
    across_first = lax.axis_size("gx")
    across_second = lax.axis_size("gy")
    index_first = lax.axis_index("gx")
    index_second = lax.axis_index("gy")
    steps = inputs.shape[0]
    request_count = inputs.shape[1] * across_second
    width = inputs.shape[2] * across_first
    local_rows = cache_keys.shape[0]
    block_count = block_adapter.shape[0]
    block_rows = request_count // block_count
    query_width = query_weight.shape[1]
    key_width = key_weight.shape[1]
    norm_scale = norm_gain.astype(jnp.float32)
    query_first = pick_adapters(query_down, block_adapter, index_second)
    query_second = pick_adapters(query_up, block_adapter, index_first)
    output_first = pick_adapters(output_down, block_adapter, index_first)
    output_second = pick_adapters(output_up, block_adapter, index_second)

    rows_all = lax.all_gather(inputs, "gy", axis=1, tiled=True)
    rows_wide = rows_all.astype(jnp.float32)
    squares = tree_sum(jnp.sum(rows_wide * rows_wide, axis=2), ("gx",))
    factor_rows = lax.rsqrt(squares / width + EPS)
    normed = (rows_wide * factor_rows[..., None] * norm_scale).astype(jnp.bfloat16)

    blocked = normed.reshape(steps, block_count, block_rows, -1)
    rank_part = jnp.einsum(
        "tbnd,bdr->tbnr", blocked, query_first, preferred_element_type=jnp.float32
    )
    rank_query = tree_sum(rank_part, ("gy", "gx")).astype(jnp.bfloat16)
    delta_query = jnp.einsum(
        "tbnr,bre->tbne", rank_query, query_second, preferred_element_type=jnp.float32
    ).reshape(steps, request_count, -1)
    part_query = (
        jnp.einsum("tnd,de->tne", normed, query_weight, preferred_element_type=jnp.float32)
        + delta_query
    )
    part_key = jnp.einsum("tnd,de->tne", normed, key_weight, preferred_element_type=jnp.float32)
    part_value = jnp.einsum(
        "tnd,de->tne", normed, value_weight, preferred_element_type=jnp.float32
    )
    joined = jnp.concatenate([part_query, part_key, part_value], axis=-1)
    summed = reduce_scatter_rows(joined, "gx", across_first).astype(jnp.bfloat16)
    chunk_rows = summed.shape[1] // across_second
    spread = lax.all_to_all(
        summed.reshape(steps, across_second, chunk_rows, -1), "gy", 1, 2, tiled=False
    )
    query_full = spread[..., :query_width].reshape(steps, local_rows, -1)
    key_full = spread[..., query_width : query_width + key_width].reshape(steps, local_rows, -1)
    value_full = spread[..., query_width + key_width :].reshape(steps, local_rows, -1)

    token_positions = (
        cache_lengths[None, :] + jnp.arange(steps, dtype=jnp.int32)[:, None]
    ).reshape(-1)
    query_rot = rotary_embedding(
        query_full.astype(jnp.float32).reshape(steps * local_rows, QUERY_HEADS, HEAD_FEATURES),
        token_positions,
    ).astype(jnp.bfloat16)
    key_rot = rotary_embedding(
        key_full.astype(jnp.float32).reshape(steps * local_rows, KEY_VALUE_HEADS, HEAD_FEATURES),
        token_positions,
    ).astype(jnp.bfloat16)
    mixed_local = attend(
        query_rot.reshape(steps, local_rows, -1),
        cache_keys,
        cache_values,
        key_rot.reshape(steps, local_rows, -1),
        value_full,
        cache_lengths,
    )
    head_group = lax.all_to_all(
        mixed_local.reshape(steps, local_rows, across_second, -1), "gy", 2, 1, tiled=False
    ).reshape(steps, across_second * local_rows, -1)
    mixed_all = lax.all_gather(head_group, "gx", axis=1, tiled=True)
    rank_part_out = jnp.einsum(
        "tbnq,bqr->tbnr",
        mixed_all.reshape(steps, block_count, block_rows, -1),
        output_first,
        preferred_element_type=jnp.float32,
    )
    rank_output = tree_sum(rank_part_out, ("gy", "gx")).astype(jnp.bfloat16)
    delta_output = jnp.einsum(
        "tbnr,bre->tbne", rank_output, output_second, preferred_element_type=jnp.float32
    ).reshape(steps, request_count, -1)
    partial_out = (
        jnp.einsum("tnq,qe->tne", mixed_all, output_weight, preferred_element_type=jnp.float32)
        + delta_output
    )
    return halving_scatter(partial_out, "gy", across_second).astype(jnp.bfloat16)


def solution(mesh):
    in_specs = (
        P(None, "gy", "gx"),
        P("gx"),
        P("gx", "gy"),
        P("gx", "gy"),
        P("gx", "gy"),
        P("gy", "gx"),
        P("gy", "gx", None),
        P("gx", None, "gy"),
        P("gx", "gy", None),
        P("gy", None, "gx"),
        P(),
        P(("gx", "gy")),
        P(("gx", "gy"), None, None),
        P(("gx", "gy"), None, None),
    )
    out_specs = P(None, "gy", "gx")
    return jax.shard_map(local, mesh=mesh, in_specs=in_specs, out_specs=out_specs, check_vma=False)
```

```python
import jax
import jax.numpy as jnp
from jax import lax
from jax.sharding import PartitionSpec as P

QUERY_HEADS = 64
KEY_VALUE_HEADS = 8
HEAD_FEATURES = 128
BLOCK = 128


EPS = 1e-05
THETA = 500000.0


def rotary_embedding(values_in, token_positions):
    half_size = values_in.shape[-1] // 2
    exponent = jnp.arange(half_size, dtype=jnp.float32) * 2.0 / values_in.shape[-1]
    frequency = THETA ** (-exponent)
    angles = token_positions.astype(jnp.float32)[:, None] * frequency[None, :]
    cosine = jnp.cos(angles)[:, None, :]
    sine_part = jnp.sin(angles)[:, None, :]
    lower = values_in[..., :half_size]
    upper = values_in[..., half_size:]
    return jnp.concatenate(
        [lower * cosine - upper * sine_part, upper * cosine + lower * sine_part], axis=-1
    )


def pick_adapters(table, adapter_ids, owner_index):
    table_count = table.shape[0]
    picked = []
    for block in range(adapter_ids.shape[0]):
        wanted = adapter_ids[block]
        owned = (wanted // table_count) == owner_index
        entry = lax.dynamic_index_in_dim(table, wanted % table_count, axis=0, keepdims=False)
        picked.append(jnp.where(owned, entry, jnp.zeros_like(entry)))
    return jnp.stack(picked)


def reduce_scatter_rows(partial, axis_name, axis_size):
    steps, rows, columns = partial.shape
    pieces = partial.astype(jnp.bfloat16).reshape(steps, axis_size, rows // axis_size, columns)
    received = lax.all_to_all(pieces, axis_name, 1, 1, tiled=False)
    return jnp.sum(received.astype(jnp.float32), axis=1)


def split_half_scatter(partial, axis_name, axis_size):
    steps, rows, columns = partial.shape
    if axis_size < 4 or axis_size & (axis_size - 1):
        return reduce_scatter_rows(partial, axis_name, axis_size)
    half = axis_size // 2
    me = lax.axis_index(axis_name)
    chunks = partial.reshape(steps, axis_size, rows // axis_size, columns)
    narrow = chunks.astype(jnp.bfloat16)
    own = lax.dynamic_index_in_dim(chunks, me, axis=1, keepdims=False)
    mirror = lax.dynamic_index_in_dim(chunks, me ^ half, axis=1, keepdims=False)
    for offset in range(1, half):
        peer = me ^ offset
        outgoing = jnp.stack(
            [
                lax.dynamic_index_in_dim(narrow, peer, axis=1, keepdims=False),
                lax.dynamic_index_in_dim(narrow, peer ^ half, axis=1, keepdims=False),
            ]
        )
        incoming = lax.ppermute(
            outgoing, axis_name, [(i, i ^ offset) for i in range(axis_size)]
        ).astype(jnp.float32)
        own = own + incoming[0]
        mirror = mirror + incoming[1]
    across = lax.ppermute(
        mirror.astype(jnp.bfloat16), axis_name, [(i, i ^ half) for i in range(axis_size)]
    )
    return own + across.astype(jnp.float32)


def tree_sum(value, axes):
    for axis_name in axes:
        size = lax.axis_size(axis_name)
        if size & (size - 1):
            value = lax.psum(value, axis_name)
            continue
        distance = 1
        while distance < size:
            pairs = [(i, i ^ distance) for i in range(size)]
            value = value + lax.ppermute(value, axis_name, pairs)
            distance *= 2
    return value


def halving_scatter(partial, axis_name, axis_size):
    steps, rows, columns = partial.shape
    if axis_size & (axis_size - 1):
        return lax.psum_scatter(partial, axis_name, scatter_dimension=1, tiled=True)
    me = lax.axis_index(axis_name)
    held = partial.reshape(steps, axis_size, rows // axis_size, columns)
    distance = 1
    while distance < axis_size:
        count = held.shape[1]
        pairs = held.reshape(steps, count // 2, 2, rows // axis_size, columns)
        mine = (me // distance) % 2
        keep = lax.dynamic_index_in_dim(pairs, mine, axis=2, keepdims=False)
        give = lax.dynamic_index_in_dim(pairs, 1 - mine, axis=2, keepdims=False)
        swap = [(i, i ^ distance) for i in range(axis_size)]
        if distance > 1:
            give = give.astype(jnp.bfloat16)
        held = keep + lax.ppermute(give, axis_name, swap).astype(jnp.float32)
        distance *= 2
    return held.reshape(steps, rows // axis_size, columns)


def attend(query_rows, previous_keys, previous_values, incoming_keys, incoming_values, lengths):
    steps, count_of_rows = query_rows.shape[0], query_rows.shape[1]
    groups = QUERY_HEADS // KEY_VALUE_HEADS
    context_window = previous_keys.shape[1]
    grouped_heads = query_rows.reshape(
        steps, count_of_rows, KEY_VALUE_HEADS, groups, HEAD_FEATURES
    ).transpose(1, 2, 0, 3, 4).reshape(count_of_rows, KEY_VALUE_HEADS, steps * groups, HEAD_FEATURES)
    keys_previous = previous_keys.reshape(
        count_of_rows, context_window, KEY_VALUE_HEADS, HEAD_FEATURES
    )
    values_previous = previous_values.reshape(
        count_of_rows, context_window, KEY_VALUE_HEADS, HEAD_FEATURES
    )
    keys_incoming = incoming_keys.reshape(
        steps, count_of_rows, KEY_VALUE_HEADS, HEAD_FEATURES
    ).transpose(1, 0, 2, 3)
    values_incoming = incoming_values.reshape(
        steps, count_of_rows, KEY_VALUE_HEADS, HEAD_FEATURES
    ).transpose(1, 0, 2, 3)
    factor = HEAD_FEATURES ** (-0.5)
    score_old = (
        jnp.einsum(
            "rhqd,rchd->rhqc", grouped_heads, keys_previous, preferred_element_type=jnp.float32
        )
        * factor
    )
    score_new = (
        jnp.einsum(
            "rhqd,rshd->rhqs", grouped_heads, keys_incoming, preferred_element_type=jnp.float32
        )
        * factor
    )
    live_old = (jnp.arange(context_window, dtype=jnp.int32)[None, :] < lengths[:, None])[
        :, None, None, :
    ]
    query_step = jnp.arange(steps * groups, dtype=jnp.int32) // groups
    live_new = (jnp.arange(steps, dtype=jnp.int32)[None, :] <= query_step[:, None])[
        None, None, :, :
    ]
    score_old = jnp.where(live_old, score_old, -1e30)
    score_new = jnp.where(live_new, score_new, -1e30)
    peak_score = jnp.maximum(jnp.max(score_old, axis=-1), jnp.max(score_new, axis=-1))
    weight_old = jnp.where(live_old, jnp.exp(score_old - peak_score[..., None]), 0.0)
    weight_new = jnp.where(live_new, jnp.exp(score_new - peak_score[..., None]), 0.0)
    weight_sum = jnp.sum(weight_old, axis=-1) + jnp.sum(weight_new, axis=-1)
    mixed_out = jnp.einsum(
        "rhqc,rchd->rhqd",
        weight_old.astype(jnp.bfloat16),
        values_previous,
        preferred_element_type=jnp.float32,
    )
    mixed_out = mixed_out + jnp.einsum(
        "rhqs,rshd->rhqd",
        weight_new.astype(jnp.bfloat16),
        values_incoming,
        preferred_element_type=jnp.float32,
    )
    mixed_out = (mixed_out / weight_sum[..., None]).astype(jnp.bfloat16)
    return mixed_out.reshape(
        count_of_rows, KEY_VALUE_HEADS, steps, groups, HEAD_FEATURES
    ).transpose(2, 0, 1, 3, 4).reshape(steps, count_of_rows, -1)


def local(
    inputs,
    norm_gain,
    query_weight,
    key_weight,
    value_weight,
    output_weight,
    query_down,
    query_up,
    output_down,
    output_up,
    block_adapter,
    cache_lengths,
    cache_keys,
    cache_values,
):
    across_first = lax.axis_size("gx")
    across_second = lax.axis_size("gy")
    index_first = lax.axis_index("gx")
    index_second = lax.axis_index("gy")
    steps = inputs.shape[0]
    request_count = inputs.shape[1] * across_second
    width = inputs.shape[2] * across_first
    local_rows = cache_keys.shape[0]
    block_count = block_adapter.shape[0]
    block_rows = request_count // block_count
    query_width = query_weight.shape[1]
    key_width = key_weight.shape[1]
    norm_scale = norm_gain.astype(jnp.float32)
    query_first = pick_adapters(query_down, block_adapter, index_second)
    query_second = pick_adapters(query_up, block_adapter, index_first)
    output_first = pick_adapters(output_down, block_adapter, index_first)
    output_second = pick_adapters(output_up, block_adapter, index_second)

    rows_all = lax.all_gather(inputs, "gy", axis=1, tiled=True)
    rows_wide = rows_all.astype(jnp.float32)
    squares = tree_sum(jnp.sum(rows_wide * rows_wide, axis=2), ("gx",))
    factor_rows = lax.rsqrt(squares / width + EPS)
    normed = (rows_wide * factor_rows[..., None] * norm_scale).astype(jnp.bfloat16)

    blocked = normed.reshape(steps, block_count, block_rows, -1)
    rank_part = jnp.einsum(
        "tbnd,bdr->tbnr", blocked, query_first, preferred_element_type=jnp.float32
    )
    rank_query = tree_sum(rank_part, ("gy", "gx")).astype(jnp.bfloat16)
    delta_query = jnp.einsum(
        "tbnr,bre->tbne", rank_query, query_second, preferred_element_type=jnp.float32
    ).reshape(steps, request_count, -1)
    part_query = (
        jnp.einsum("tnd,de->tne", normed, query_weight, preferred_element_type=jnp.float32)
        + delta_query
    )
    part_key = jnp.einsum("tnd,de->tne", normed, key_weight, preferred_element_type=jnp.float32)
    part_value = jnp.einsum(
        "tnd,de->tne", normed, value_weight, preferred_element_type=jnp.float32
    )
    joined = jnp.concatenate([part_query, part_key, part_value], axis=-1)
    summed = split_half_scatter(joined, "gx", across_first).astype(jnp.bfloat16)
    chunk_rows = summed.shape[1] // across_second
    spread = lax.all_to_all(
        summed.reshape(steps, across_second, chunk_rows, -1), "gy", 1, 2, tiled=False
    )
    query_full = spread[..., :query_width].reshape(steps, local_rows, -1)
    key_full = spread[..., query_width : query_width + key_width].reshape(steps, local_rows, -1)
    value_full = spread[..., query_width + key_width :].reshape(steps, local_rows, -1)

    token_positions = (
        cache_lengths[None, :] + jnp.arange(steps, dtype=jnp.int32)[:, None]
    ).reshape(-1)
    query_rot = rotary_embedding(
        query_full.astype(jnp.float32).reshape(steps * local_rows, QUERY_HEADS, HEAD_FEATURES),
        token_positions,
    ).astype(jnp.bfloat16)
    key_rot = rotary_embedding(
        key_full.astype(jnp.float32).reshape(steps * local_rows, KEY_VALUE_HEADS, HEAD_FEATURES),
        token_positions,
    ).astype(jnp.bfloat16)
    mixed_local = attend(
        query_rot.reshape(steps, local_rows, -1),
        cache_keys,
        cache_values,
        key_rot.reshape(steps, local_rows, -1),
        value_full,
        cache_lengths,
    )
    head_group = lax.all_to_all(
        mixed_local.reshape(steps, local_rows, across_second, -1), "gy", 2, 1, tiled=False
    ).reshape(steps, across_second * local_rows, -1)
    mixed_all = lax.all_gather(head_group, "gx", axis=1, tiled=True)
    rank_part_out = jnp.einsum(
        "tbnq,bqr->tbnr",
        mixed_all.reshape(steps, block_count, block_rows, -1),
        output_first,
        preferred_element_type=jnp.float32,
    )
    rank_output = tree_sum(rank_part_out, ("gy", "gx")).astype(jnp.bfloat16)
    delta_output = jnp.einsum(
        "tbnr,bre->tbne", rank_output, output_second, preferred_element_type=jnp.float32
    ).reshape(steps, request_count, -1)
    partial_out = (
        jnp.einsum("tnq,qe->tne", mixed_all, output_weight, preferred_element_type=jnp.float32)
        + delta_output
    )
    return halving_scatter(partial_out, "gy", across_second).astype(jnp.bfloat16)


def solution(mesh):
    in_specs = (
        P(None, "gy", "gx"),
        P("gx"),
        P("gx", "gy"),
        P("gx", "gy"),
        P("gx", "gy"),
        P("gy", "gx"),
        P("gy", "gx", None),
        P("gx", None, "gy"),
        P("gx", "gy", None),
        P("gy", None, "gx"),
        P(),
        P(("gx", "gy")),
        P(("gx", "gy"), None, None),
        P(("gx", "gy"), None, None),
    )
    out_specs = P(None, "gy", "gx")
    return jax.shard_map(local, mesh=mesh, in_specs=in_specs, out_specs=out_specs, check_vma=False)
```

```python
import jax
import jax.numpy as jnp
from jax import lax
from jax.sharding import PartitionSpec as P

QUERY_HEADS = 64
KEY_VALUE_HEADS = 8
HEAD_FEATURES = 128
BLOCK = 128


EPS = 1e-05
THETA = 500000.0


def rotary_embedding(values_in, token_positions):
    half_size = values_in.shape[-1] // 2
    exponent = jnp.arange(half_size, dtype=jnp.float32) * 2.0 / values_in.shape[-1]
    frequency = THETA ** (-exponent)
    angles = token_positions.astype(jnp.float32)[:, None] * frequency[None, :]
    cosine = jnp.cos(angles)[:, None, :]
    sine_part = jnp.sin(angles)[:, None, :]
    lower = values_in[..., :half_size]
    upper = values_in[..., half_size:]
    return jnp.concatenate(
        [lower * cosine - upper * sine_part, upper * cosine + lower * sine_part], axis=-1
    )


def pick_adapters(table, adapter_ids, owner_index):
    table_count = table.shape[0]
    picked = []
    for block in range(adapter_ids.shape[0]):
        wanted = adapter_ids[block]
        owned = (wanted // table_count) == owner_index
        entry = lax.dynamic_index_in_dim(table, wanted % table_count, axis=0, keepdims=False)
        picked.append(jnp.where(owned, entry, jnp.zeros_like(entry)))
    return jnp.stack(picked)


def reduce_scatter_rows(partial, axis_name, axis_size):
    steps, rows, columns = partial.shape
    pieces = partial.astype(jnp.bfloat16).reshape(steps, axis_size, rows // axis_size, columns)
    received = lax.all_to_all(pieces, axis_name, 1, 1, tiled=False)
    return jnp.sum(received.astype(jnp.float32), axis=1)


def split_half_scatter(partial, axis_name, axis_size):
    steps, rows, columns = partial.shape
    if axis_size < 4 or axis_size & (axis_size - 1):
        return reduce_scatter_rows(partial, axis_name, axis_size)
    half = axis_size // 2
    me = lax.axis_index(axis_name)
    chunks = partial.reshape(steps, axis_size, rows // axis_size, columns)
    narrow = chunks.astype(jnp.bfloat16)
    own = lax.dynamic_index_in_dim(chunks, me, axis=1, keepdims=False)
    mirror = lax.dynamic_index_in_dim(chunks, me ^ half, axis=1, keepdims=False)
    for offset in range(1, half):
        peer = me ^ offset
        outgoing = jnp.stack(
            [
                lax.dynamic_index_in_dim(narrow, peer, axis=1, keepdims=False),
                lax.dynamic_index_in_dim(narrow, peer ^ half, axis=1, keepdims=False),
            ]
        )
        incoming = lax.ppermute(
            outgoing, axis_name, [(i, i ^ offset) for i in range(axis_size)]
        ).astype(jnp.float32)
        own = own + incoming[0]
        mirror = mirror + incoming[1]
    across = lax.ppermute(
        mirror.astype(jnp.bfloat16), axis_name, [(i, i ^ half) for i in range(axis_size)]
    )
    return own + across.astype(jnp.float32)


def doubling_gather(value, axis_name, axis_size, axis):
    if axis_size & (axis_size - 1):
        return lax.all_gather(value, axis_name, axis=axis, tiled=True)
    me = lax.axis_index(axis_name)
    held = value
    distance = 1
    while distance < axis_size:
        other = lax.ppermute(held, axis_name, [(i, i ^ distance) for i in range(axis_size)])
        upper = (me // distance) % 2 == 1
        first = jnp.where(upper, other, held)
        second = jnp.where(upper, held, other)
        held = jnp.concatenate([first, second], axis=axis)
        distance *= 2
    return held


def split_half_gather(value, axis_name, axis_size):
    if axis_size < 4 or axis_size & (axis_size - 1):
        return lax.all_gather(value, axis_name, axis=1, tiled=True)
    half = axis_size // 2
    me = lax.axis_index(axis_name)
    mirror = lax.ppermute(value, axis_name, [(i, i ^ half) for i in range(axis_size)])
    pair = jnp.stack([value, mirror])
    slots = [None] * axis_size
    slots[0], slots[half] = value, mirror
    for offset in range(1, half):
        incoming = lax.ppermute(pair, axis_name, [(i, i ^ offset) for i in range(axis_size)])
        slots[offset], slots[offset + half] = incoming[0], incoming[1]
    stacked = jnp.stack(slots)
    order = jnp.arange(axis_size, dtype=jnp.int32) ^ me
    gathered = jnp.take(stacked, order, axis=0)
    steps, rows, columns = value.shape
    return gathered.transpose(1, 0, 2, 3).reshape(steps, axis_size * rows, columns)


def tree_sum(value, axes):
    for axis_name in axes:
        size = lax.axis_size(axis_name)
        if size & (size - 1):
            value = lax.psum(value, axis_name)
            continue
        distance = 1
        while distance < size:
            pairs = [(i, i ^ distance) for i in range(size)]
            value = value + lax.ppermute(value, axis_name, pairs)
            distance *= 2
    return value


def halving_scatter(partial, axis_name, axis_size):
    steps, rows, columns = partial.shape
    if axis_size & (axis_size - 1):
        return lax.psum_scatter(partial, axis_name, scatter_dimension=1, tiled=True)
    me = lax.axis_index(axis_name)
    held = partial.reshape(steps, axis_size, rows // axis_size, columns)
    distance = 1
    while distance < axis_size:
        count = held.shape[1]
        pairs = held.reshape(steps, count // 2, 2, rows // axis_size, columns)
        mine = (me // distance) % 2
        keep = lax.dynamic_index_in_dim(pairs, mine, axis=2, keepdims=False)
        give = lax.dynamic_index_in_dim(pairs, 1 - mine, axis=2, keepdims=False)
        swap = [(i, i ^ distance) for i in range(axis_size)]
        if distance > 1:
            give = give.astype(jnp.bfloat16)
        held = keep + lax.ppermute(give, axis_name, swap).astype(jnp.float32)
        distance *= 2
    return held.reshape(steps, rows // axis_size, columns)


def attend(query_rows, previous_keys, previous_values, incoming_keys, incoming_values, lengths):
    steps, count_of_rows = query_rows.shape[0], query_rows.shape[1]
    groups = QUERY_HEADS // KEY_VALUE_HEADS
    context_window = previous_keys.shape[1]
    grouped_heads = query_rows.reshape(
        steps, count_of_rows, KEY_VALUE_HEADS, groups, HEAD_FEATURES
    ).transpose(1, 2, 0, 3, 4).reshape(count_of_rows, KEY_VALUE_HEADS, steps * groups, HEAD_FEATURES)
    keys_previous = previous_keys.reshape(
        count_of_rows, context_window, KEY_VALUE_HEADS, HEAD_FEATURES
    )
    values_previous = previous_values.reshape(
        count_of_rows, context_window, KEY_VALUE_HEADS, HEAD_FEATURES
    )
    keys_incoming = incoming_keys.reshape(
        steps, count_of_rows, KEY_VALUE_HEADS, HEAD_FEATURES
    ).transpose(1, 0, 2, 3)
    values_incoming = incoming_values.reshape(
        steps, count_of_rows, KEY_VALUE_HEADS, HEAD_FEATURES
    ).transpose(1, 0, 2, 3)
    factor = HEAD_FEATURES ** (-0.5)
    score_old = (
        jnp.einsum(
            "rhqd,rchd->rhqc", grouped_heads, keys_previous, preferred_element_type=jnp.float32
        )
        * factor
    )
    score_new = (
        jnp.einsum(
            "rhqd,rshd->rhqs", grouped_heads, keys_incoming, preferred_element_type=jnp.float32
        )
        * factor
    )
    live_old = (jnp.arange(context_window, dtype=jnp.int32)[None, :] < lengths[:, None])[
        :, None, None, :
    ]
    query_step = jnp.arange(steps * groups, dtype=jnp.int32) // groups
    live_new = (jnp.arange(steps, dtype=jnp.int32)[None, :] <= query_step[:, None])[
        None, None, :, :
    ]
    score_old = jnp.where(live_old, score_old, -1e30)
    score_new = jnp.where(live_new, score_new, -1e30)
    peak_score = jnp.maximum(jnp.max(score_old, axis=-1), jnp.max(score_new, axis=-1))
    weight_old = jnp.where(live_old, jnp.exp(score_old - peak_score[..., None]), 0.0)
    weight_new = jnp.where(live_new, jnp.exp(score_new - peak_score[..., None]), 0.0)
    weight_sum = jnp.sum(weight_old, axis=-1) + jnp.sum(weight_new, axis=-1)
    mixed_out = jnp.einsum(
        "rhqc,rchd->rhqd",
        weight_old.astype(jnp.bfloat16),
        values_previous,
        preferred_element_type=jnp.float32,
    )
    mixed_out = mixed_out + jnp.einsum(
        "rhqs,rshd->rhqd",
        weight_new.astype(jnp.bfloat16),
        values_incoming,
        preferred_element_type=jnp.float32,
    )
    mixed_out = (mixed_out / weight_sum[..., None]).astype(jnp.bfloat16)
    return mixed_out.reshape(
        count_of_rows, KEY_VALUE_HEADS, steps, groups, HEAD_FEATURES
    ).transpose(2, 0, 1, 3, 4).reshape(steps, count_of_rows, -1)


def local(
    inputs,
    norm_gain,
    query_weight,
    key_weight,
    value_weight,
    output_weight,
    query_down,
    query_up,
    output_down,
    output_up,
    block_adapter,
    cache_lengths,
    cache_keys,
    cache_values,
):
    across_first = lax.axis_size("gx")
    across_second = lax.axis_size("gy")
    index_first = lax.axis_index("gx")
    index_second = lax.axis_index("gy")
    steps = inputs.shape[0]
    request_count = inputs.shape[1] * across_second
    width = inputs.shape[2] * across_first
    local_rows = cache_keys.shape[0]
    block_count = block_adapter.shape[0]
    block_rows = request_count // block_count
    query_width = query_weight.shape[1]
    key_width = key_weight.shape[1]
    norm_scale = norm_gain.astype(jnp.float32)
    query_first = pick_adapters(query_down, block_adapter, index_second)
    query_second = pick_adapters(query_up, block_adapter, index_first)
    output_first = pick_adapters(output_down, block_adapter, index_first)
    output_second = pick_adapters(output_up, block_adapter, index_second)

    rows_all = doubling_gather(inputs, "gy", across_second, 1)
    rows_wide = rows_all.astype(jnp.float32)
    squares = tree_sum(jnp.sum(rows_wide * rows_wide, axis=2), ("gx",))
    factor_rows = lax.rsqrt(squares / width + EPS)
    normed = (rows_wide * factor_rows[..., None] * norm_scale).astype(jnp.bfloat16)

    blocked = normed.reshape(steps, block_count, block_rows, -1)
    rank_part = jnp.einsum(
        "tbnd,bdr->tbnr", blocked, query_first, preferred_element_type=jnp.float32
    )
    rank_query = tree_sum(rank_part, ("gy", "gx")).astype(jnp.bfloat16)
    delta_query = jnp.einsum(
        "tbnr,bre->tbne", rank_query, query_second, preferred_element_type=jnp.float32
    ).reshape(steps, request_count, -1)
    part_query = (
        jnp.einsum("tnd,de->tne", normed, query_weight, preferred_element_type=jnp.float32)
        + delta_query
    )
    part_key = jnp.einsum("tnd,de->tne", normed, key_weight, preferred_element_type=jnp.float32)
    part_value = jnp.einsum(
        "tnd,de->tne", normed, value_weight, preferred_element_type=jnp.float32
    )
    joined = jnp.concatenate([part_query, part_key, part_value], axis=-1)
    summed = split_half_scatter(joined, "gx", across_first).astype(jnp.bfloat16)
    chunk_rows = summed.shape[1] // across_second
    spread = lax.all_to_all(
        summed.reshape(steps, across_second, chunk_rows, -1), "gy", 1, 2, tiled=False
    )
    query_full = spread[..., :query_width].reshape(steps, local_rows, -1)
    key_full = spread[..., query_width : query_width + key_width].reshape(steps, local_rows, -1)
    value_full = spread[..., query_width + key_width :].reshape(steps, local_rows, -1)

    token_positions = (
        cache_lengths[None, :] + jnp.arange(steps, dtype=jnp.int32)[:, None]
    ).reshape(-1)
    query_rot = rotary_embedding(
        query_full.astype(jnp.float32).reshape(steps * local_rows, QUERY_HEADS, HEAD_FEATURES),
        token_positions,
    ).astype(jnp.bfloat16)
    key_rot = rotary_embedding(
        key_full.astype(jnp.float32).reshape(steps * local_rows, KEY_VALUE_HEADS, HEAD_FEATURES),
        token_positions,
    ).astype(jnp.bfloat16)
    mixed_local = attend(
        query_rot.reshape(steps, local_rows, -1),
        cache_keys,
        cache_values,
        key_rot.reshape(steps, local_rows, -1),
        value_full,
        cache_lengths,
    )
    head_group = lax.all_to_all(
        mixed_local.reshape(steps, local_rows, across_second, -1), "gy", 2, 1, tiled=False
    ).reshape(steps, across_second * local_rows, -1)
    mixed_all = split_half_gather(head_group, "gx", across_first)
    rank_part_out = jnp.einsum(
        "tbnq,bqr->tbnr",
        mixed_all.reshape(steps, block_count, block_rows, -1),
        output_first,
        preferred_element_type=jnp.float32,
    )
    rank_output = tree_sum(rank_part_out, ("gy", "gx")).astype(jnp.bfloat16)
    delta_output = jnp.einsum(
        "tbnr,bre->tbne", rank_output, output_second, preferred_element_type=jnp.float32
    ).reshape(steps, request_count, -1)
    partial_out = (
        jnp.einsum("tnq,qe->tne", mixed_all, output_weight, preferred_element_type=jnp.float32)
        + delta_output
    )
    return halving_scatter(partial_out, "gy", across_second).astype(jnp.bfloat16)


def solution(mesh):
    in_specs = (
        P(None, "gy", "gx"),
        P("gx"),
        P("gx", "gy"),
        P("gx", "gy"),
        P("gx", "gy"),
        P("gy", "gx"),
        P("gy", "gx", None),
        P("gx", None, "gy"),
        P("gx", "gy", None),
        P("gy", None, "gx"),
        P(),
        P(("gx", "gy")),
        P(("gx", "gy"), None, None),
        P(("gx", "gy"), None, None),
    )
    out_specs = P(None, "gy", "gx")
    return jax.shard_map(local, mesh=mesh, in_specs=in_specs, out_specs=out_specs, check_vma=False)
```

```python
import jax
import jax.numpy as jnp
from jax import lax
from jax.sharding import PartitionSpec as P

QUERY_HEADS = 64
KEY_VALUE_HEADS = 8
HEAD_FEATURES = 128
BLOCK = 128


EPS = 1e-05
THETA = 500000.0


def rotary_embedding(values_in, token_positions):
    half_size = values_in.shape[-1] // 2
    exponent = jnp.arange(half_size, dtype=jnp.float32) * 2.0 / values_in.shape[-1]
    frequency = THETA ** (-exponent)
    angles = token_positions.astype(jnp.float32)[:, None] * frequency[None, :]
    cosine = jnp.cos(angles)[:, None, :]
    sine_part = jnp.sin(angles)[:, None, :]
    lower = values_in[..., :half_size]
    upper = values_in[..., half_size:]
    return jnp.concatenate(
        [lower * cosine - upper * sine_part, upper * cosine + lower * sine_part], axis=-1
    )


def pick_adapters(table, adapter_ids, owner_index):
    table_count = table.shape[0]
    picked = []
    for block in range(adapter_ids.shape[0]):
        wanted = adapter_ids[block]
        owned = (wanted // table_count) == owner_index
        entry = lax.dynamic_index_in_dim(table, wanted % table_count, axis=0, keepdims=False)
        picked.append(jnp.where(owned, entry, jnp.zeros_like(entry)))
    return jnp.stack(picked)


def reduce_scatter_rows(partial, axis_name, axis_size):
    steps, rows, columns = partial.shape
    pieces = partial.astype(jnp.bfloat16).reshape(steps, axis_size, rows // axis_size, columns)
    received = lax.all_to_all(pieces, axis_name, 1, 1, tiled=False)
    return jnp.sum(received.astype(jnp.float32), axis=1)


def split_half_scatter_steps(partial, axis_name, axis_size):
    return jnp.concatenate(
        [
            split_half_scatter(partial[step : step + 1], axis_name, axis_size)
            for step in range(partial.shape[0])
        ]
    )


def split_half_gather_steps(value, axis_name, axis_size):
    return jnp.concatenate(
        [
            split_half_gather(value[step : step + 1], axis_name, axis_size)
            for step in range(value.shape[0])
        ]
    )


def split_half_scatter(partial, axis_name, axis_size):
    steps, rows, columns = partial.shape
    if axis_size < 4 or axis_size & (axis_size - 1):
        return reduce_scatter_rows(partial, axis_name, axis_size)
    half = axis_size // 2
    me = lax.axis_index(axis_name)
    chunks = partial.reshape(steps, axis_size, rows // axis_size, columns)
    narrow = chunks.astype(jnp.bfloat16)
    own = lax.dynamic_index_in_dim(chunks, me, axis=1, keepdims=False)
    mirror = lax.dynamic_index_in_dim(chunks, me ^ half, axis=1, keepdims=False)
    for offset in range(1, half):
        peer = me ^ offset
        outgoing = jnp.stack(
            [
                lax.dynamic_index_in_dim(narrow, peer, axis=1, keepdims=False),
                lax.dynamic_index_in_dim(narrow, peer ^ half, axis=1, keepdims=False),
            ]
        )
        incoming = lax.ppermute(
            outgoing, axis_name, [(i, i ^ offset) for i in range(axis_size)]
        ).astype(jnp.float32)
        own = own + incoming[0]
        mirror = mirror + incoming[1]
    across = lax.ppermute(
        mirror.astype(jnp.bfloat16), axis_name, [(i, i ^ half) for i in range(axis_size)]
    )
    return own + across.astype(jnp.float32)


def doubling_gather(value, axis_name, axis_size, axis):
    if axis_size & (axis_size - 1):
        return lax.all_gather(value, axis_name, axis=axis, tiled=True)
    me = lax.axis_index(axis_name)
    held = value
    distance = 1
    while distance < axis_size:
        other = lax.ppermute(held, axis_name, [(i, i ^ distance) for i in range(axis_size)])
        upper = (me // distance) % 2 == 1
        first = jnp.where(upper, other, held)
        second = jnp.where(upper, held, other)
        held = jnp.concatenate([first, second], axis=axis)
        distance *= 2
    return held


def split_half_gather(value, axis_name, axis_size):
    if axis_size < 4 or axis_size & (axis_size - 1):
        return lax.all_gather(value, axis_name, axis=1, tiled=True)
    half = axis_size // 2
    me = lax.axis_index(axis_name)
    mirror = lax.ppermute(value, axis_name, [(i, i ^ half) for i in range(axis_size)])
    pair = jnp.stack([value, mirror])
    slots = [None] * axis_size
    slots[0], slots[half] = value, mirror
    for offset in range(1, half):
        incoming = lax.ppermute(pair, axis_name, [(i, i ^ offset) for i in range(axis_size)])
        slots[offset], slots[offset + half] = incoming[0], incoming[1]
    stacked = jnp.stack(slots)
    order = jnp.arange(axis_size, dtype=jnp.int32) ^ me
    gathered = jnp.take(stacked, order, axis=0)
    steps, rows, columns = value.shape
    return gathered.transpose(1, 0, 2, 3).reshape(steps, axis_size * rows, columns)


def tree_sum(value, axes):
    for axis_name in axes:
        size = lax.axis_size(axis_name)
        if size & (size - 1):
            value = lax.psum(value, axis_name)
            continue
        distance = 1
        while distance < size:
            pairs = [(i, i ^ distance) for i in range(size)]
            value = value + lax.ppermute(value, axis_name, pairs)
            distance *= 2
    return value


def halving_scatter(partial, axis_name, axis_size):
    steps, rows, columns = partial.shape
    if axis_size & (axis_size - 1):
        return lax.psum_scatter(partial, axis_name, scatter_dimension=1, tiled=True)
    me = lax.axis_index(axis_name)
    held = partial.reshape(steps, axis_size, rows // axis_size, columns)
    distance = 1
    while distance < axis_size:
        count = held.shape[1]
        pairs = held.reshape(steps, count // 2, 2, rows // axis_size, columns)
        mine = (me // distance) % 2
        keep = lax.dynamic_index_in_dim(pairs, mine, axis=2, keepdims=False)
        give = lax.dynamic_index_in_dim(pairs, 1 - mine, axis=2, keepdims=False)
        swap = [(i, i ^ distance) for i in range(axis_size)]
        if distance > 1:
            give = give.astype(jnp.bfloat16)
        held = keep + lax.ppermute(give, axis_name, swap).astype(jnp.float32)
        distance *= 2
    return held.reshape(steps, rows // axis_size, columns)


def attend(query_rows, previous_keys, previous_values, incoming_keys, incoming_values, lengths):
    steps, count_of_rows = query_rows.shape[0], query_rows.shape[1]
    groups = QUERY_HEADS // KEY_VALUE_HEADS
    context_window = previous_keys.shape[1]
    grouped_heads = query_rows.reshape(
        steps, count_of_rows, KEY_VALUE_HEADS, groups, HEAD_FEATURES
    ).transpose(1, 2, 0, 3, 4).reshape(count_of_rows, KEY_VALUE_HEADS, steps * groups, HEAD_FEATURES)
    keys_previous = previous_keys.reshape(
        count_of_rows, context_window, KEY_VALUE_HEADS, HEAD_FEATURES
    )
    values_previous = previous_values.reshape(
        count_of_rows, context_window, KEY_VALUE_HEADS, HEAD_FEATURES
    )
    keys_incoming = incoming_keys.reshape(
        steps, count_of_rows, KEY_VALUE_HEADS, HEAD_FEATURES
    ).transpose(1, 0, 2, 3)
    values_incoming = incoming_values.reshape(
        steps, count_of_rows, KEY_VALUE_HEADS, HEAD_FEATURES
    ).transpose(1, 0, 2, 3)
    factor = HEAD_FEATURES ** (-0.5)
    score_old = (
        jnp.einsum(
            "rhqd,rchd->rhqc", grouped_heads, keys_previous, preferred_element_type=jnp.float32
        )
        * factor
    )
    score_new = (
        jnp.einsum(
            "rhqd,rshd->rhqs", grouped_heads, keys_incoming, preferred_element_type=jnp.float32
        )
        * factor
    )
    live_old = (jnp.arange(context_window, dtype=jnp.int32)[None, :] < lengths[:, None])[
        :, None, None, :
    ]
    query_step = jnp.arange(steps * groups, dtype=jnp.int32) // groups
    live_new = (jnp.arange(steps, dtype=jnp.int32)[None, :] <= query_step[:, None])[
        None, None, :, :
    ]
    score_old = jnp.where(live_old, score_old, -1e30)
    score_new = jnp.where(live_new, score_new, -1e30)
    peak_score = jnp.maximum(jnp.max(score_old, axis=-1), jnp.max(score_new, axis=-1))
    weight_old = jnp.where(live_old, jnp.exp(score_old - peak_score[..., None]), 0.0)
    weight_new = jnp.where(live_new, jnp.exp(score_new - peak_score[..., None]), 0.0)
    weight_sum = jnp.sum(weight_old, axis=-1) + jnp.sum(weight_new, axis=-1)
    mixed_out = jnp.einsum(
        "rhqc,rchd->rhqd",
        weight_old.astype(jnp.bfloat16),
        values_previous,
        preferred_element_type=jnp.float32,
    )
    mixed_out = mixed_out + jnp.einsum(
        "rhqs,rshd->rhqd",
        weight_new.astype(jnp.bfloat16),
        values_incoming,
        preferred_element_type=jnp.float32,
    )
    mixed_out = (mixed_out / weight_sum[..., None]).astype(jnp.bfloat16)
    return mixed_out.reshape(
        count_of_rows, KEY_VALUE_HEADS, steps, groups, HEAD_FEATURES
    ).transpose(2, 0, 1, 3, 4).reshape(steps, count_of_rows, -1)


def local(
    inputs,
    norm_gain,
    query_weight,
    key_weight,
    value_weight,
    output_weight,
    query_down,
    query_up,
    output_down,
    output_up,
    block_adapter,
    cache_lengths,
    cache_keys,
    cache_values,
):
    across_first = lax.axis_size("gx")
    across_second = lax.axis_size("gy")
    index_first = lax.axis_index("gx")
    index_second = lax.axis_index("gy")
    steps = inputs.shape[0]
    request_count = inputs.shape[1] * across_second
    width = inputs.shape[2] * across_first
    local_rows = cache_keys.shape[0]
    block_count = block_adapter.shape[0]
    block_rows = request_count // block_count
    query_width = query_weight.shape[1]
    key_width = key_weight.shape[1]
    norm_scale = norm_gain.astype(jnp.float32)
    query_first = pick_adapters(query_down, block_adapter, index_second)
    query_second = pick_adapters(query_up, block_adapter, index_first)
    output_first = pick_adapters(output_down, block_adapter, index_first)
    output_second = pick_adapters(output_up, block_adapter, index_second)

    rows_all = doubling_gather(inputs, "gy", across_second, 1)
    rows_wide = rows_all.astype(jnp.float32)
    squares = tree_sum(jnp.sum(rows_wide * rows_wide, axis=2), ("gx",))
    factor_rows = lax.rsqrt(squares / width + EPS)
    normed = (rows_wide * factor_rows[..., None] * norm_scale).astype(jnp.bfloat16)

    blocked = normed.reshape(steps, block_count, block_rows, -1)
    rank_part = jnp.einsum(
        "tbnd,bdr->tbnr", blocked, query_first, preferred_element_type=jnp.float32
    )
    rank_query = tree_sum(rank_part, ("gy", "gx")).astype(jnp.bfloat16)
    delta_query = jnp.einsum(
        "tbnr,bre->tbne", rank_query, query_second, preferred_element_type=jnp.float32
    ).reshape(steps, request_count, -1)
    part_query = (
        jnp.einsum("tnd,de->tne", normed, query_weight, preferred_element_type=jnp.float32)
        + delta_query
    )
    part_key = jnp.einsum("tnd,de->tne", normed, key_weight, preferred_element_type=jnp.float32)
    part_value = jnp.einsum(
        "tnd,de->tne", normed, value_weight, preferred_element_type=jnp.float32
    )
    joined = jnp.concatenate([part_query, part_key, part_value], axis=-1)
    summed = split_half_scatter_steps(joined, "gx", across_first).astype(jnp.bfloat16)
    chunk_rows = summed.shape[1] // across_second
    spread = lax.all_to_all(
        summed.reshape(steps, across_second, chunk_rows, -1), "gy", 1, 2, tiled=False
    )
    query_full = spread[..., :query_width].reshape(steps, local_rows, -1)
    key_full = spread[..., query_width : query_width + key_width].reshape(steps, local_rows, -1)
    value_full = spread[..., query_width + key_width :].reshape(steps, local_rows, -1)

    token_positions = (
        cache_lengths[None, :] + jnp.arange(steps, dtype=jnp.int32)[:, None]
    ).reshape(-1)
    query_rot = rotary_embedding(
        query_full.astype(jnp.float32).reshape(steps * local_rows, QUERY_HEADS, HEAD_FEATURES),
        token_positions,
    ).astype(jnp.bfloat16)
    key_rot = rotary_embedding(
        key_full.astype(jnp.float32).reshape(steps * local_rows, KEY_VALUE_HEADS, HEAD_FEATURES),
        token_positions,
    ).astype(jnp.bfloat16)
    mixed_local = attend(
        query_rot.reshape(steps, local_rows, -1),
        cache_keys,
        cache_values,
        key_rot.reshape(steps, local_rows, -1),
        value_full,
        cache_lengths,
    )
    head_group = lax.all_to_all(
        mixed_local.reshape(steps, local_rows, across_second, -1), "gy", 2, 1, tiled=False
    ).reshape(steps, across_second * local_rows, -1)
    mixed_all = split_half_gather_steps(head_group, "gx", across_first)
    rank_part_out = jnp.einsum(
        "tbnq,bqr->tbnr",
        mixed_all.reshape(steps, block_count, block_rows, -1),
        output_first,
        preferred_element_type=jnp.float32,
    )
    rank_output = tree_sum(rank_part_out, ("gy", "gx")).astype(jnp.bfloat16)
    delta_output = jnp.einsum(
        "tbnr,bre->tbne", rank_output, output_second, preferred_element_type=jnp.float32
    ).reshape(steps, request_count, -1)
    partial_out = (
        jnp.einsum("tnq,qe->tne", mixed_all, output_weight, preferred_element_type=jnp.float32)
        + delta_output
    )
    return halving_scatter(partial_out, "gy", across_second).astype(jnp.bfloat16)


def solution(mesh):
    in_specs = (
        P(None, "gy", "gx"),
        P("gx"),
        P("gx", "gy"),
        P("gx", "gy"),
        P("gx", "gy"),
        P("gy", "gx"),
        P("gy", "gx", None),
        P("gx", None, "gy"),
        P("gx", "gy", None),
        P("gy", None, "gx"),
        P(),
        P(("gx", "gy")),
        P(("gx", "gy"), None, None),
        P(("gx", "gy"), None, None),
    )
    out_specs = P(None, "gy", "gx")
    return jax.shard_map(local, mesh=mesh, in_specs=in_specs, out_specs=out_specs, check_vma=False)
```

```python
import jax
import jax.numpy as jnp
from jax import lax
from jax.sharding import PartitionSpec as P

QUERY_HEADS = 64
KEY_VALUE_HEADS = 8
HEAD_FEATURES = 128
BLOCK = 128


EPS = 1e-05
THETA = 500000.0


def rotary_embedding(values_in, token_positions):
    half_size = values_in.shape[-1] // 2
    exponent = jnp.arange(half_size, dtype=jnp.float32) * 2.0 / values_in.shape[-1]
    frequency = THETA ** (-exponent)
    angles = token_positions.astype(jnp.float32)[:, None] * frequency[None, :]
    cosine = jnp.cos(angles)[:, None, :]
    sine_part = jnp.sin(angles)[:, None, :]
    lower = values_in[..., :half_size]
    upper = values_in[..., half_size:]
    return jnp.concatenate(
        [lower * cosine - upper * sine_part, upper * cosine + lower * sine_part], axis=-1
    )


def pick_adapters(table, adapter_ids, owner_index):
    table_count = table.shape[0]
    picked = []
    for block in range(adapter_ids.shape[0]):
        wanted = adapter_ids[block]
        owned = (wanted // table_count) == owner_index
        entry = lax.dynamic_index_in_dim(table, wanted % table_count, axis=0, keepdims=False)
        picked.append(jnp.where(owned, entry, jnp.zeros_like(entry)))
    return jnp.stack(picked)


def reduce_scatter_rows(partial, axis_name, axis_size):
    steps, rows, columns = partial.shape
    pieces = partial.astype(jnp.bfloat16).reshape(steps, axis_size, rows // axis_size, columns)
    received = lax.all_to_all(pieces, axis_name, 1, 1, tiled=False)
    return jnp.sum(received.astype(jnp.float32), axis=1)


def split_half_scatter_steps(partial, axis_name, axis_size):
    return jnp.concatenate(
        [
            split_half_scatter(partial[step : step + 1], axis_name, axis_size)
            for step in range(partial.shape[0])
        ]
    )


def split_half_gather_steps(value, axis_name, axis_size):
    return jnp.concatenate(
        [
            split_half_gather(value[step : step + 1], axis_name, axis_size)
            for step in range(value.shape[0])
        ]
    )


def split_half_scatter(partial, axis_name, axis_size):
    steps, rows, columns = partial.shape
    if axis_size < 4 or axis_size & (axis_size - 1):
        return reduce_scatter_rows(partial, axis_name, axis_size)
    half = axis_size // 2
    me = lax.axis_index(axis_name)
    chunks = partial.reshape(steps, axis_size, rows // axis_size, columns)
    narrow = chunks.astype(jnp.bfloat16)
    own = lax.dynamic_index_in_dim(chunks, me, axis=1, keepdims=False)
    mirror = lax.dynamic_index_in_dim(chunks, me ^ half, axis=1, keepdims=False)
    for offset in range(1, half):
        peer = me ^ offset
        outgoing = jnp.stack(
            [
                lax.dynamic_index_in_dim(narrow, peer, axis=1, keepdims=False),
                lax.dynamic_index_in_dim(narrow, peer ^ half, axis=1, keepdims=False),
            ]
        )
        incoming = lax.ppermute(
            outgoing, axis_name, [(i, i ^ offset) for i in range(axis_size)]
        ).astype(jnp.float32)
        own = own + incoming[0]
        mirror = mirror + incoming[1]
    across = lax.ppermute(
        mirror.astype(jnp.bfloat16), axis_name, [(i, i ^ half) for i in range(axis_size)]
    )
    return own + across.astype(jnp.float32)


def doubling_gather(value, axis_name, axis_size, axis):
    if axis_size & (axis_size - 1):
        return lax.all_gather(value, axis_name, axis=axis, tiled=True)
    me = lax.axis_index(axis_name)
    held = value
    distance = 1
    while distance < axis_size:
        other = lax.ppermute(held, axis_name, [(i, i ^ distance) for i in range(axis_size)])
        upper = (me // distance) % 2 == 1
        first = jnp.where(upper, other, held)
        second = jnp.where(upper, held, other)
        held = jnp.concatenate([first, second], axis=axis)
        distance *= 2
    return held


def split_half_gather(value, axis_name, axis_size):
    if axis_size < 4 or axis_size & (axis_size - 1):
        return lax.all_gather(value, axis_name, axis=1, tiled=True)
    half = axis_size // 2
    me = lax.axis_index(axis_name)
    mirror = lax.ppermute(value, axis_name, [(i, i ^ half) for i in range(axis_size)])
    pair = jnp.stack([value, mirror])
    slots = [None] * axis_size
    slots[0], slots[half] = value, mirror
    for offset in range(1, half):
        incoming = lax.ppermute(pair, axis_name, [(i, i ^ offset) for i in range(axis_size)])
        slots[offset], slots[offset + half] = incoming[0], incoming[1]
    stacked = jnp.stack(slots)
    order = jnp.arange(axis_size, dtype=jnp.int32) ^ me
    gathered = jnp.take(stacked, order, axis=0)
    steps, rows, columns = value.shape
    return gathered.transpose(1, 0, 2, 3).reshape(steps, axis_size * rows, columns)


def tree_sum(value, axes):
    for axis_name in axes:
        size = lax.axis_size(axis_name)
        if size & (size - 1):
            value = lax.psum(value, axis_name)
            continue
        distance = 1
        while distance < size:
            pairs = [(i, i ^ distance) for i in range(size)]
            value = value + lax.ppermute(value, axis_name, pairs)
            distance *= 2
    return value


def halving_scatter(partial, axis_name, axis_size):
    steps, rows, columns = partial.shape
    if axis_size & (axis_size - 1):
        return lax.psum_scatter(partial, axis_name, scatter_dimension=1, tiled=True)
    me = lax.axis_index(axis_name)
    held = partial.reshape(steps, axis_size, rows // axis_size, columns)
    distance = 1
    while distance < axis_size:
        count = held.shape[1]
        pairs = held.reshape(steps, count // 2, 2, rows // axis_size, columns)
        mine = (me // distance) % 2
        keep = lax.dynamic_index_in_dim(pairs, mine, axis=2, keepdims=False)
        give = lax.dynamic_index_in_dim(pairs, 1 - mine, axis=2, keepdims=False)
        swap = [(i, i ^ distance) for i in range(axis_size)]
        if distance > 1:
            give = give.astype(jnp.bfloat16)
        held = keep + lax.ppermute(give, axis_name, swap).astype(jnp.float32)
        distance *= 2
    return held.reshape(steps, rows // axis_size, columns)


def attend(query_rows, previous_keys, previous_values, incoming_keys, incoming_values, lengths):
    steps, count_of_rows = query_rows.shape[0], query_rows.shape[1]
    groups = QUERY_HEADS // KEY_VALUE_HEADS
    context_window = previous_keys.shape[1]
    grouped_heads = query_rows.reshape(
        steps, count_of_rows, KEY_VALUE_HEADS, groups, HEAD_FEATURES
    ).transpose(1, 2, 0, 3, 4).reshape(count_of_rows, KEY_VALUE_HEADS, steps * groups, HEAD_FEATURES)
    keys_previous = previous_keys.reshape(
        count_of_rows, context_window, KEY_VALUE_HEADS, HEAD_FEATURES
    )
    values_previous = previous_values.reshape(
        count_of_rows, context_window, KEY_VALUE_HEADS, HEAD_FEATURES
    )
    keys_incoming = incoming_keys.reshape(
        steps, count_of_rows, KEY_VALUE_HEADS, HEAD_FEATURES
    ).transpose(1, 0, 2, 3)
    values_incoming = incoming_values.reshape(
        steps, count_of_rows, KEY_VALUE_HEADS, HEAD_FEATURES
    ).transpose(1, 0, 2, 3)
    factor = HEAD_FEATURES ** (-0.5)
    score_old = (
        jnp.einsum(
            "rhqd,rchd->rhqc", grouped_heads, keys_previous, preferred_element_type=jnp.float32
        )
        * factor
    )
    score_new = (
        jnp.einsum(
            "rhqd,rshd->rhqs", grouped_heads, keys_incoming, preferred_element_type=jnp.float32
        )
        * factor
    )
    live_old = (jnp.arange(context_window, dtype=jnp.int32)[None, :] < lengths[:, None])[
        :, None, None, :
    ]
    query_step = jnp.arange(steps * groups, dtype=jnp.int32) // groups
    live_new = (jnp.arange(steps, dtype=jnp.int32)[None, :] <= query_step[:, None])[
        None, None, :, :
    ]
    score_old = jnp.where(live_old, score_old, -1e30)
    score_new = jnp.where(live_new, score_new, -1e30)
    peak_score = jnp.maximum(jnp.max(score_old, axis=-1), jnp.max(score_new, axis=-1))
    weight_old = jnp.where(live_old, jnp.exp(score_old - peak_score[..., None]), 0.0)
    weight_new = jnp.where(live_new, jnp.exp(score_new - peak_score[..., None]), 0.0)
    weight_sum = jnp.sum(weight_old, axis=-1) + jnp.sum(weight_new, axis=-1)
    mixed_out = jnp.einsum(
        "rhqc,rchd->rhqd",
        weight_old.astype(jnp.bfloat16),
        values_previous,
        preferred_element_type=jnp.float32,
    )
    mixed_out = mixed_out + jnp.einsum(
        "rhqs,rshd->rhqd",
        weight_new.astype(jnp.bfloat16),
        values_incoming,
        preferred_element_type=jnp.float32,
    )
    mixed_out = (mixed_out / weight_sum[..., None]).astype(jnp.bfloat16)
    return mixed_out.reshape(
        count_of_rows, KEY_VALUE_HEADS, steps, groups, HEAD_FEATURES
    ).transpose(2, 0, 1, 3, 4).reshape(steps, count_of_rows, -1)


def local(
    inputs,
    norm_gain,
    query_weight,
    key_weight,
    value_weight,
    output_weight,
    query_down,
    query_up,
    output_down,
    output_up,
    block_adapter,
    cache_lengths,
    cache_keys,
    cache_values,
):
    across_first = lax.axis_size("gx")
    across_second = lax.axis_size("gy")
    index_first = lax.axis_index("gx")
    index_second = lax.axis_index("gy")
    steps = inputs.shape[0]
    request_count = inputs.shape[1] * across_second
    width = inputs.shape[2] * across_first
    local_rows = cache_keys.shape[0]
    block_count = block_adapter.shape[0]
    block_rows = request_count // block_count
    query_width = query_weight.shape[1]
    key_width = key_weight.shape[1]
    norm_scale = norm_gain.astype(jnp.float32)
    query_first = tree_sum(pick_adapters(query_down, block_adapter, index_second), ("gy",))
    query_second = pick_adapters(query_up, block_adapter, index_first)
    output_first = tree_sum(pick_adapters(output_down, block_adapter, index_first), ("gx",))
    output_second = pick_adapters(output_up, block_adapter, index_second)

    own_wide = inputs.astype(jnp.float32)
    own_squares = tree_sum(jnp.sum(own_wide * own_wide, axis=2), ("gx",))
    squares = doubling_gather(own_squares, "gy", across_second, 1)
    rows_all = doubling_gather(inputs, "gy", across_second, 1)
    rows_wide = rows_all.astype(jnp.float32)
    factor_rows = lax.rsqrt(squares / width + EPS)
    normed = (rows_wide * factor_rows[..., None] * norm_scale).astype(jnp.bfloat16)

    blocked = normed.reshape(steps, block_count, block_rows, -1)
    rank_part = jnp.einsum(
        "tbnd,bdr->tbnr", blocked, query_first, preferred_element_type=jnp.float32
    )
    rank_query = tree_sum(rank_part, ("gx",)).astype(jnp.bfloat16)
    delta_query = jnp.einsum(
        "tbnr,bre->tbne", rank_query, query_second, preferred_element_type=jnp.float32
    ).reshape(steps, request_count, -1)
    part_query = (
        jnp.einsum("tnd,de->tne", normed, query_weight, preferred_element_type=jnp.float32)
        + delta_query
    )
    part_key = jnp.einsum("tnd,de->tne", normed, key_weight, preferred_element_type=jnp.float32)
    part_value = jnp.einsum(
        "tnd,de->tne", normed, value_weight, preferred_element_type=jnp.float32
    )
    joined = jnp.concatenate([part_query, part_key, part_value], axis=-1)
    summed = split_half_scatter_steps(joined, "gx", across_first).astype(jnp.bfloat16)
    chunk_rows = summed.shape[1] // across_second
    spread = lax.all_to_all(
        summed.reshape(steps, across_second, chunk_rows, -1), "gy", 1, 2, tiled=False
    )
    query_full = spread[..., :query_width].reshape(steps, local_rows, -1)
    key_full = spread[..., query_width : query_width + key_width].reshape(steps, local_rows, -1)
    value_full = spread[..., query_width + key_width :].reshape(steps, local_rows, -1)

    token_positions = (
        cache_lengths[None, :] + jnp.arange(steps, dtype=jnp.int32)[:, None]
    ).reshape(-1)
    query_rot = rotary_embedding(
        query_full.astype(jnp.float32).reshape(steps * local_rows, QUERY_HEADS, HEAD_FEATURES),
        token_positions,
    ).astype(jnp.bfloat16)
    key_rot = rotary_embedding(
        key_full.astype(jnp.float32).reshape(steps * local_rows, KEY_VALUE_HEADS, HEAD_FEATURES),
        token_positions,
    ).astype(jnp.bfloat16)
    mixed_local = attend(
        query_rot.reshape(steps, local_rows, -1),
        cache_keys,
        cache_values,
        key_rot.reshape(steps, local_rows, -1),
        value_full,
        cache_lengths,
    )
    head_group = lax.all_to_all(
        mixed_local.reshape(steps, local_rows, across_second, -1), "gy", 2, 1, tiled=False
    ).reshape(steps, across_second * local_rows, -1)
    mixed_all = split_half_gather_steps(head_group, "gx", across_first)
    rank_part_out = jnp.einsum(
        "tbnq,bqr->tbnr",
        mixed_all.reshape(steps, block_count, block_rows, -1),
        output_first,
        preferred_element_type=jnp.float32,
    )
    rank_output = tree_sum(rank_part_out, ("gy",)).astype(jnp.bfloat16)
    delta_output = jnp.einsum(
        "tbnr,bre->tbne", rank_output, output_second, preferred_element_type=jnp.float32
    ).reshape(steps, request_count, -1)
    partial_out = (
        jnp.einsum("tnq,qe->tne", mixed_all, output_weight, preferred_element_type=jnp.float32)
        + delta_output
    )
    return halving_scatter(partial_out, "gy", across_second).astype(jnp.bfloat16)


def solution(mesh):
    in_specs = (
        P(None, "gy", "gx"),
        P("gx"),
        P("gx", "gy"),
        P("gx", "gy"),
        P("gx", "gy"),
        P("gy", "gx"),
        P("gy", "gx", None),
        P("gx", None, "gy"),
        P("gx", "gy", None),
        P("gy", None, "gx"),
        P(),
        P(("gx", "gy")),
        P(("gx", "gy"), None, None),
        P(("gx", "gy"), None, None),
    )
    out_specs = P(None, "gy", "gx")
    return jax.shard_map(local, mesh=mesh, in_specs=in_specs, out_specs=out_specs, check_vma=False)
```

```python
import jax
import jax.numpy as jnp
from jax import lax
from jax.sharding import PartitionSpec as P

QUERY_HEADS = 64
KEY_VALUE_HEADS = 8
HEAD_FEATURES = 128
BLOCK = 128


EPS = 1e-05
THETA = 500000.0


def rotary_embedding(values_in, token_positions):
    half_size = values_in.shape[-1] // 2
    exponent = jnp.arange(half_size, dtype=jnp.float32) * 2.0 / values_in.shape[-1]
    frequency = THETA ** (-exponent)
    angles = token_positions.astype(jnp.float32)[:, None] * frequency[None, :]
    cosine = jnp.cos(angles)[:, None, :]
    sine_part = jnp.sin(angles)[:, None, :]
    lower = values_in[..., :half_size]
    upper = values_in[..., half_size:]
    return jnp.concatenate(
        [lower * cosine - upper * sine_part, upper * cosine + lower * sine_part], axis=-1
    )


def pick_adapters(table, adapter_ids, owner_index):
    table_count = table.shape[0]
    picked = []
    for block in range(adapter_ids.shape[0]):
        wanted = adapter_ids[block]
        owned = (wanted // table_count) == owner_index
        entry = lax.dynamic_index_in_dim(table, wanted % table_count, axis=0, keepdims=False)
        picked.append(jnp.where(owned, entry, jnp.zeros_like(entry)))
    return jnp.stack(picked)


def reduce_scatter_rows(partial, axis_name, axis_size):
    steps, rows, columns = partial.shape
    pieces = partial.astype(jnp.bfloat16).reshape(steps, axis_size, rows // axis_size, columns)
    received = lax.all_to_all(pieces, axis_name, 1, 1, tiled=False)
    return jnp.sum(received.astype(jnp.float32), axis=1)


def split_half_scatter_steps(partial, axis_name, axis_size):
    return jnp.concatenate(
        [
            split_half_scatter(partial[step : step + 1], axis_name, axis_size)
            for step in range(partial.shape[0])
        ]
    )


def split_half_gather_steps(value, axis_name, axis_size):
    return jnp.concatenate(
        [
            split_half_gather(value[step : step + 1], axis_name, axis_size)
            for step in range(value.shape[0])
        ]
    )


def split_half_scatter(partial, axis_name, axis_size):
    steps, rows, columns = partial.shape
    if axis_size < 4 or axis_size & (axis_size - 1):
        return reduce_scatter_rows(partial, axis_name, axis_size)
    half = axis_size // 2
    me = lax.axis_index(axis_name)
    chunks = partial.reshape(steps, axis_size, rows // axis_size, columns)
    narrow = chunks.astype(jnp.bfloat16)
    own = lax.dynamic_index_in_dim(chunks, me, axis=1, keepdims=False)
    mirror = lax.dynamic_index_in_dim(chunks, me ^ half, axis=1, keepdims=False)
    for offset in range(1, half):
        peer = me ^ offset
        outgoing = jnp.stack(
            [
                lax.dynamic_index_in_dim(narrow, peer, axis=1, keepdims=False),
                lax.dynamic_index_in_dim(narrow, peer ^ half, axis=1, keepdims=False),
            ]
        )
        incoming = lax.ppermute(
            outgoing, axis_name, [(i, i ^ offset) for i in range(axis_size)]
        ).astype(jnp.float32)
        own = own + incoming[0]
        mirror = mirror + incoming[1]
    across = lax.ppermute(
        mirror.astype(jnp.bfloat16), axis_name, [(i, i ^ half) for i in range(axis_size)]
    )
    return own + across.astype(jnp.float32)


def doubling_gather(value, axis_name, axis_size, axis):
    if axis_size & (axis_size - 1):
        return lax.all_gather(value, axis_name, axis=axis, tiled=True)
    me = lax.axis_index(axis_name)
    held = value
    distance = 1
    while distance < axis_size:
        other = lax.ppermute(held, axis_name, [(i, i ^ distance) for i in range(axis_size)])
        upper = (me // distance) % 2 == 1
        first = jnp.where(upper, other, held)
        second = jnp.where(upper, held, other)
        held = jnp.concatenate([first, second], axis=axis)
        distance *= 2
    return held


def split_half_gather(value, axis_name, axis_size):
    if axis_size < 4 or axis_size & (axis_size - 1):
        return lax.all_gather(value, axis_name, axis=1, tiled=True)
    half = axis_size // 2
    me = lax.axis_index(axis_name)
    mirror = lax.ppermute(value, axis_name, [(i, i ^ half) for i in range(axis_size)])
    pair = jnp.stack([value, mirror])
    slots = [None] * axis_size
    slots[0], slots[half] = value, mirror
    for offset in range(1, half):
        incoming = lax.ppermute(pair, axis_name, [(i, i ^ offset) for i in range(axis_size)])
        slots[offset], slots[offset + half] = incoming[0], incoming[1]
    stacked = jnp.stack(slots)
    order = jnp.arange(axis_size, dtype=jnp.int32) ^ me
    gathered = jnp.take(stacked, order, axis=0)
    steps, rows, columns = value.shape
    return gathered.transpose(1, 0, 2, 3).reshape(steps, axis_size * rows, columns)


def tree_sum(value, axes):
    for axis_name in axes:
        size = lax.axis_size(axis_name)
        if size & (size - 1):
            value = lax.psum(value, axis_name)
            continue
        distance = 1
        while distance < size:
            pairs = [(i, i ^ distance) for i in range(size)]
            value = value + lax.ppermute(value, axis_name, pairs)
            distance *= 2
    return value


def halving_scatter(partial, axis_name, axis_size):
    steps, rows, columns = partial.shape
    if axis_size & (axis_size - 1):
        return lax.psum_scatter(partial, axis_name, scatter_dimension=1, tiled=True)
    me = lax.axis_index(axis_name)
    held = partial.reshape(steps, axis_size, rows // axis_size, columns)
    distance = 1
    while distance < axis_size:
        count = held.shape[1]
        pairs = held.reshape(steps, count // 2, 2, rows // axis_size, columns)
        mine = (me // distance) % 2
        keep = lax.dynamic_index_in_dim(pairs, mine, axis=2, keepdims=False)
        give = lax.dynamic_index_in_dim(pairs, 1 - mine, axis=2, keepdims=False)
        swap = [(i, i ^ distance) for i in range(axis_size)]
        if distance > 1:
            give = give.astype(jnp.bfloat16)
        held = keep + lax.ppermute(give, axis_name, swap).astype(jnp.float32)
        distance *= 2
    return held.reshape(steps, rows // axis_size, columns)


def attend(query_rows, previous_keys, previous_values, incoming_keys, incoming_values, lengths):
    steps, count_of_rows = query_rows.shape[0], query_rows.shape[1]
    groups = QUERY_HEADS // KEY_VALUE_HEADS
    context_window = previous_keys.shape[1]
    grouped_heads = query_rows.reshape(
        steps, count_of_rows, KEY_VALUE_HEADS, groups, HEAD_FEATURES
    ).transpose(1, 2, 0, 3, 4).reshape(count_of_rows, KEY_VALUE_HEADS, steps * groups, HEAD_FEATURES)
    keys_previous = previous_keys.reshape(
        count_of_rows, context_window, KEY_VALUE_HEADS, HEAD_FEATURES
    )
    values_previous = previous_values.reshape(
        count_of_rows, context_window, KEY_VALUE_HEADS, HEAD_FEATURES
    )
    keys_incoming = incoming_keys.reshape(
        steps, count_of_rows, KEY_VALUE_HEADS, HEAD_FEATURES
    ).transpose(1, 0, 2, 3)
    values_incoming = incoming_values.reshape(
        steps, count_of_rows, KEY_VALUE_HEADS, HEAD_FEATURES
    ).transpose(1, 0, 2, 3)
    factor = HEAD_FEATURES ** (-0.5)
    score_old = (
        jnp.einsum(
            "rhqd,rchd->rhqc", grouped_heads, keys_previous, preferred_element_type=jnp.float32
        )
        * factor
    )
    score_new = (
        jnp.einsum(
            "rhqd,rshd->rhqs", grouped_heads, keys_incoming, preferred_element_type=jnp.float32
        )
        * factor
    )
    live_old = (jnp.arange(context_window, dtype=jnp.int32)[None, :] < lengths[:, None])[
        :, None, None, :
    ]
    query_step = jnp.arange(steps * groups, dtype=jnp.int32) // groups
    live_new = (jnp.arange(steps, dtype=jnp.int32)[None, :] <= query_step[:, None])[
        None, None, :, :
    ]
    score_old = jnp.where(live_old, score_old, -1e30)
    score_new = jnp.where(live_new, score_new, -1e30)
    peak_score = jnp.maximum(jnp.max(score_old, axis=-1), jnp.max(score_new, axis=-1))
    weight_old = jnp.where(live_old, jnp.exp(score_old - peak_score[..., None]), 0.0)
    weight_new = jnp.where(live_new, jnp.exp(score_new - peak_score[..., None]), 0.0)
    weight_sum = jnp.sum(weight_old, axis=-1) + jnp.sum(weight_new, axis=-1)
    mixed_out = jnp.einsum(
        "rhqc,rchd->rhqd",
        weight_old.astype(jnp.bfloat16),
        values_previous,
        preferred_element_type=jnp.float32,
    )
    mixed_out = mixed_out + jnp.einsum(
        "rhqs,rshd->rhqd",
        weight_new.astype(jnp.bfloat16),
        values_incoming,
        preferred_element_type=jnp.float32,
    )
    mixed_out = (mixed_out / weight_sum[..., None]).astype(jnp.bfloat16)
    return mixed_out.reshape(
        count_of_rows, KEY_VALUE_HEADS, steps, groups, HEAD_FEATURES
    ).transpose(2, 0, 1, 3, 4).reshape(steps, count_of_rows, -1)


def local(
    inputs,
    norm_gain,
    query_weight,
    key_weight,
    value_weight,
    output_weight,
    query_down,
    query_up,
    output_down,
    output_up,
    block_adapter,
    cache_lengths,
    cache_keys,
    cache_values,
):
    across_first = lax.axis_size("gx")
    across_second = lax.axis_size("gy")
    index_first = lax.axis_index("gx")
    index_second = lax.axis_index("gy")
    steps = inputs.shape[0]
    request_count = inputs.shape[1] * across_second
    width = inputs.shape[2] * across_first
    local_rows = cache_keys.shape[0]
    block_count = block_adapter.shape[0]
    block_rows = request_count // block_count
    query_width = query_weight.shape[1]
    key_width = key_weight.shape[1]
    norm_scale = norm_gain.astype(jnp.float32)
    query_first = pick_adapters(query_down, block_adapter, index_second)
    query_second = pick_adapters(query_up, block_adapter, index_first)
    output_first = tree_sum(pick_adapters(output_down, block_adapter, index_first), ("gx",))
    output_second = pick_adapters(output_up, block_adapter, index_second)

    rows_all = doubling_gather(inputs, "gy", across_second, 1)
    rows_wide = rows_all.astype(jnp.float32)
    squares = tree_sum(jnp.sum(rows_wide * rows_wide, axis=2), ("gx",))
    factor_rows = lax.rsqrt(squares / width + EPS)
    normed = (rows_wide * factor_rows[..., None] * norm_scale).astype(jnp.bfloat16)

    blocked = normed.reshape(steps, block_count, block_rows, -1)
    rank_part = jnp.einsum(
        "tbnd,bdr->tbnr", blocked, query_first, preferred_element_type=jnp.float32
    )
    rank_query = tree_sum(rank_part, ("gy", "gx")).astype(jnp.bfloat16)
    delta_query = jnp.einsum(
        "tbnr,bre->tbne", rank_query, query_second, preferred_element_type=jnp.float32
    ).reshape(steps, request_count, -1)
    part_query = (
        jnp.einsum("tnd,de->tne", normed, query_weight, preferred_element_type=jnp.float32)
        + delta_query
    )
    part_key = jnp.einsum("tnd,de->tne", normed, key_weight, preferred_element_type=jnp.float32)
    part_value = jnp.einsum(
        "tnd,de->tne", normed, value_weight, preferred_element_type=jnp.float32
    )
    joined = jnp.concatenate([part_query, part_key, part_value], axis=-1)
    output_first, joined = lax.optimization_barrier((output_first, joined))
    summed = split_half_scatter_steps(joined, "gx", across_first).astype(jnp.bfloat16)
    chunk_rows = summed.shape[1] // across_second
    spread = lax.all_to_all(
        summed.reshape(steps, across_second, chunk_rows, -1), "gy", 1, 2, tiled=False
    )
    query_full = spread[..., :query_width].reshape(steps, local_rows, -1)
    key_full = spread[..., query_width : query_width + key_width].reshape(steps, local_rows, -1)
    value_full = spread[..., query_width + key_width :].reshape(steps, local_rows, -1)

    token_positions = (
        cache_lengths[None, :] + jnp.arange(steps, dtype=jnp.int32)[:, None]
    ).reshape(-1)
    query_rot = rotary_embedding(
        query_full.astype(jnp.float32).reshape(steps * local_rows, QUERY_HEADS, HEAD_FEATURES),
        token_positions,
    ).astype(jnp.bfloat16)
    key_rot = rotary_embedding(
        key_full.astype(jnp.float32).reshape(steps * local_rows, KEY_VALUE_HEADS, HEAD_FEATURES),
        token_positions,
    ).astype(jnp.bfloat16)
    mixed_local = attend(
        query_rot.reshape(steps, local_rows, -1),
        cache_keys,
        cache_values,
        key_rot.reshape(steps, local_rows, -1),
        value_full,
        cache_lengths,
    )
    head_group = lax.all_to_all(
        mixed_local.reshape(steps, local_rows, across_second, -1), "gy", 2, 1, tiled=False
    ).reshape(steps, across_second * local_rows, -1)
    mixed_all = split_half_gather_steps(head_group, "gx", across_first)
    rank_part_out = jnp.einsum(
        "tbnq,bqr->tbnr",
        mixed_all.reshape(steps, block_count, block_rows, -1),
        output_first,
        preferred_element_type=jnp.float32,
    )
    rank_output = tree_sum(rank_part_out, ("gy",)).astype(jnp.bfloat16)
    delta_output = jnp.einsum(
        "tbnr,bre->tbne", rank_output, output_second, preferred_element_type=jnp.float32
    ).reshape(steps, request_count, -1)
    partial_out = (
        jnp.einsum("tnq,qe->tne", mixed_all, output_weight, preferred_element_type=jnp.float32)
        + delta_output
    )
    return halving_scatter(partial_out, "gy", across_second).astype(jnp.bfloat16)


def solution(mesh):
    in_specs = (
        P(None, "gy", "gx"),
        P("gx"),
        P("gx", "gy"),
        P("gx", "gy"),
        P("gx", "gy"),
        P("gy", "gx"),
        P("gy", "gx", None),
        P("gx", None, "gy"),
        P("gx", "gy", None),
        P("gy", None, "gx"),
        P(),
        P(("gx", "gy")),
        P(("gx", "gy"), None, None),
        P(("gx", "gy"), None, None),
    )
    out_specs = P(None, "gy", "gx")
    return jax.shard_map(local, mesh=mesh, in_specs=in_specs, out_specs=out_specs, check_vma=False)
```

```python
import jax
import jax.numpy as jnp
from jax import lax
from jax.sharding import PartitionSpec as P

QUERY_HEADS = 64
KEY_VALUE_HEADS = 8
HEAD_FEATURES = 128
BLOCK = 128


EPS = 1e-05
THETA = 500000.0


def rotary_embedding(values_in, token_positions):
    half_size = values_in.shape[-1] // 2
    exponent = jnp.arange(half_size, dtype=jnp.float32) * 2.0 / values_in.shape[-1]
    frequency = THETA ** (-exponent)
    angles = token_positions.astype(jnp.float32)[:, None] * frequency[None, :]
    cosine = jnp.cos(angles)[:, None, :]
    sine_part = jnp.sin(angles)[:, None, :]
    lower = values_in[..., :half_size]
    upper = values_in[..., half_size:]
    return jnp.concatenate(
        [lower * cosine - upper * sine_part, upper * cosine + lower * sine_part], axis=-1
    )


def pick_adapters(table, adapter_ids, owner_index):
    table_count = table.shape[0]
    picked = []
    for block in range(adapter_ids.shape[0]):
        wanted = adapter_ids[block]
        owned = (wanted // table_count) == owner_index
        entry = lax.dynamic_index_in_dim(table, wanted % table_count, axis=0, keepdims=False)
        picked.append(jnp.where(owned, entry, jnp.zeros_like(entry)))
    return jnp.stack(picked)


def reduce_scatter_rows(partial, axis_name, axis_size):
    steps, rows, columns = partial.shape
    pieces = partial.astype(jnp.bfloat16).reshape(steps, axis_size, rows // axis_size, columns)
    received = lax.all_to_all(pieces, axis_name, 1, 1, tiled=False)
    return jnp.sum(received.astype(jnp.float32), axis=1)


def split_half_scatter_steps(partial, axis_name, axis_size):
    return jnp.concatenate(
        [
            split_half_scatter(partial[step : step + 1], axis_name, axis_size)
            for step in range(partial.shape[0])
        ]
    )


def split_half_gather_steps(value, axis_name, axis_size):
    return jnp.concatenate(
        [
            split_half_gather(value[step : step + 1], axis_name, axis_size)
            for step in range(value.shape[0])
        ]
    )


def split_half_scatter(partial, axis_name, axis_size):
    steps, rows, columns = partial.shape
    if axis_size < 4 or axis_size & (axis_size - 1):
        return reduce_scatter_rows(partial, axis_name, axis_size)
    half = axis_size // 2
    me = lax.axis_index(axis_name)
    chunks = partial.reshape(steps, axis_size, rows // axis_size, columns)
    narrow = chunks.astype(jnp.bfloat16)
    own = lax.dynamic_index_in_dim(chunks, me, axis=1, keepdims=False)
    mirror = lax.dynamic_index_in_dim(chunks, me ^ half, axis=1, keepdims=False)
    for offset in range(1, half):
        peer = me ^ offset
        outgoing = jnp.stack(
            [
                lax.dynamic_index_in_dim(narrow, peer, axis=1, keepdims=False),
                lax.dynamic_index_in_dim(narrow, peer ^ half, axis=1, keepdims=False),
            ]
        )
        incoming = lax.ppermute(
            outgoing, axis_name, [(i, i ^ offset) for i in range(axis_size)]
        ).astype(jnp.float32)
        own = own + incoming[0]
        mirror = mirror + incoming[1]
    across = lax.ppermute(
        mirror.astype(jnp.bfloat16), axis_name, [(i, i ^ half) for i in range(axis_size)]
    )
    return own + across.astype(jnp.float32)


def doubling_gather(value, axis_name, axis_size, axis):
    if axis_size & (axis_size - 1):
        return lax.all_gather(value, axis_name, axis=axis, tiled=True)
    me = lax.axis_index(axis_name)
    held = value
    distance = 1
    while distance < axis_size:
        other = lax.ppermute(held, axis_name, [(i, i ^ distance) for i in range(axis_size)])
        upper = (me // distance) % 2 == 1
        first = jnp.where(upper, other, held)
        second = jnp.where(upper, held, other)
        held = jnp.concatenate([first, second], axis=axis)
        distance *= 2
    return held


def split_half_gather(value, axis_name, axis_size):
    if axis_size < 4 or axis_size & (axis_size - 1):
        return lax.all_gather(value, axis_name, axis=1, tiled=True)
    half = axis_size // 2
    me = lax.axis_index(axis_name)
    mirror = lax.ppermute(value, axis_name, [(i, i ^ half) for i in range(axis_size)])
    pair = jnp.stack([value, mirror])
    slots = [None] * axis_size
    slots[0], slots[half] = value, mirror
    for offset in range(1, half):
        incoming = lax.ppermute(pair, axis_name, [(i, i ^ offset) for i in range(axis_size)])
        slots[offset], slots[offset + half] = incoming[0], incoming[1]
    stacked = jnp.stack(slots)
    order = jnp.arange(axis_size, dtype=jnp.int32) ^ me
    gathered = jnp.take(stacked, order, axis=0)
    steps, rows, columns = value.shape
    return gathered.transpose(1, 0, 2, 3).reshape(steps, axis_size * rows, columns)


def tree_sum(value, axes):
    for axis_name in axes:
        size = lax.axis_size(axis_name)
        if size & (size - 1):
            value = lax.psum(value, axis_name)
            continue
        distance = 1
        while distance < size:
            pairs = [(i, i ^ distance) for i in range(size)]
            value = value + lax.ppermute(value, axis_name, pairs)
            distance *= 2
    return value


def sum_then_spread(value, sum_axes, spread_axes):
    return tree_sum(tree_sum(value, sum_axes).astype(jnp.bfloat16), spread_axes)


def halving_scatter(partial, axis_name, axis_size):
    steps, rows, columns = partial.shape
    if axis_size & (axis_size - 1):
        return lax.psum_scatter(partial, axis_name, scatter_dimension=1, tiled=True)
    me = lax.axis_index(axis_name)
    held = partial.reshape(steps, axis_size, rows // axis_size, columns)
    distance = 1
    while distance < axis_size:
        count = held.shape[1]
        pairs = held.reshape(steps, count // 2, 2, rows // axis_size, columns)
        mine = (me // distance) % 2
        keep = lax.dynamic_index_in_dim(pairs, mine, axis=2, keepdims=False)
        give = lax.dynamic_index_in_dim(pairs, 1 - mine, axis=2, keepdims=False)
        swap = [(i, i ^ distance) for i in range(axis_size)]
        if distance > 1:
            give = give.astype(jnp.bfloat16)
        held = keep + lax.ppermute(give, axis_name, swap).astype(jnp.float32)
        distance *= 2
    return held.reshape(steps, rows // axis_size, columns)


def attend(query_rows, previous_keys, previous_values, incoming_keys, incoming_values, lengths):
    steps, count_of_rows = query_rows.shape[0], query_rows.shape[1]
    groups = QUERY_HEADS // KEY_VALUE_HEADS
    context_window = previous_keys.shape[1]
    grouped_heads = query_rows.reshape(
        steps, count_of_rows, KEY_VALUE_HEADS, groups, HEAD_FEATURES
    ).transpose(1, 2, 0, 3, 4).reshape(count_of_rows, KEY_VALUE_HEADS, steps * groups, HEAD_FEATURES)
    keys_previous = previous_keys.reshape(
        count_of_rows, context_window, KEY_VALUE_HEADS, HEAD_FEATURES
    )
    values_previous = previous_values.reshape(
        count_of_rows, context_window, KEY_VALUE_HEADS, HEAD_FEATURES
    )
    keys_incoming = incoming_keys.reshape(
        steps, count_of_rows, KEY_VALUE_HEADS, HEAD_FEATURES
    ).transpose(1, 0, 2, 3)
    values_incoming = incoming_values.reshape(
        steps, count_of_rows, KEY_VALUE_HEADS, HEAD_FEATURES
    ).transpose(1, 0, 2, 3)
    factor = HEAD_FEATURES ** (-0.5)
    score_old = (
        jnp.einsum(
            "rhqd,rchd->rhqc", grouped_heads, keys_previous, preferred_element_type=jnp.float32
        )
        * factor
    )
    score_new = (
        jnp.einsum(
            "rhqd,rshd->rhqs", grouped_heads, keys_incoming, preferred_element_type=jnp.float32
        )
        * factor
    )
    live_old = (jnp.arange(context_window, dtype=jnp.int32)[None, :] < lengths[:, None])[
        :, None, None, :
    ]
    query_step = jnp.arange(steps * groups, dtype=jnp.int32) // groups
    live_new = (jnp.arange(steps, dtype=jnp.int32)[None, :] <= query_step[:, None])[
        None, None, :, :
    ]
    score_old = jnp.where(live_old, score_old, -1e30)
    score_new = jnp.where(live_new, score_new, -1e30)
    peak_score = jnp.maximum(jnp.max(score_old, axis=-1), jnp.max(score_new, axis=-1))
    weight_old = jnp.where(live_old, jnp.exp(score_old - peak_score[..., None]), 0.0)
    weight_new = jnp.where(live_new, jnp.exp(score_new - peak_score[..., None]), 0.0)
    weight_sum = jnp.sum(weight_old, axis=-1) + jnp.sum(weight_new, axis=-1)
    mixed_out = jnp.einsum(
        "rhqc,rchd->rhqd",
        weight_old.astype(jnp.bfloat16),
        values_previous,
        preferred_element_type=jnp.float32,
    )
    mixed_out = mixed_out + jnp.einsum(
        "rhqs,rshd->rhqd",
        weight_new.astype(jnp.bfloat16),
        values_incoming,
        preferred_element_type=jnp.float32,
    )
    mixed_out = (mixed_out / weight_sum[..., None]).astype(jnp.bfloat16)
    return mixed_out.reshape(
        count_of_rows, KEY_VALUE_HEADS, steps, groups, HEAD_FEATURES
    ).transpose(2, 0, 1, 3, 4).reshape(steps, count_of_rows, -1)


def local(
    inputs,
    norm_gain,
    query_weight,
    key_weight,
    value_weight,
    output_weight,
    query_down,
    query_up,
    output_down,
    output_up,
    block_adapter,
    cache_lengths,
    cache_keys,
    cache_values,
):
    across_first = lax.axis_size("gx")
    across_second = lax.axis_size("gy")
    index_first = lax.axis_index("gx")
    index_second = lax.axis_index("gy")
    steps = inputs.shape[0]
    request_count = inputs.shape[1] * across_second
    width = inputs.shape[2] * across_first
    local_rows = cache_keys.shape[0]
    block_count = block_adapter.shape[0]
    block_rows = request_count // block_count
    query_width = query_weight.shape[1]
    key_width = key_weight.shape[1]
    norm_scale = norm_gain.astype(jnp.float32)
    query_first = pick_adapters(query_down, block_adapter, index_second)
    query_second = pick_adapters(query_up, block_adapter, index_first)
    output_first = pick_adapters(output_down, block_adapter, index_first)
    output_second = pick_adapters(output_up, block_adapter, index_second)

    rows_all = doubling_gather(inputs, "gy", across_second, 1)
    rows_wide = rows_all.astype(jnp.float32)
    squares = tree_sum(jnp.sum(rows_wide * rows_wide, axis=2), ("gx",))
    factor_rows = lax.rsqrt(squares / width + EPS)
    normed = (rows_wide * factor_rows[..., None] * norm_scale).astype(jnp.bfloat16)

    blocked = normed.reshape(steps, block_count, block_rows, -1)
    rank_part = jnp.einsum(
        "tbnd,bdr->tbnr", blocked, query_first, preferred_element_type=jnp.float32
    )
    rank_query = sum_then_spread(rank_part, ("gx",), ("gy",))
    delta_query = jnp.einsum(
        "tbnr,bre->tbne", rank_query, query_second, preferred_element_type=jnp.float32
    ).reshape(steps, request_count, -1)
    part_query = (
        jnp.einsum("tnd,de->tne", normed, query_weight, preferred_element_type=jnp.float32)
        + delta_query
    )
    part_key = jnp.einsum("tnd,de->tne", normed, key_weight, preferred_element_type=jnp.float32)
    part_value = jnp.einsum(
        "tnd,de->tne", normed, value_weight, preferred_element_type=jnp.float32
    )
    joined = jnp.concatenate([part_query, part_key, part_value], axis=-1)
    summed = split_half_scatter_steps(joined, "gx", across_first).astype(jnp.bfloat16)
    chunk_rows = summed.shape[1] // across_second
    spread = lax.all_to_all(
        summed.reshape(steps, across_second, chunk_rows, -1), "gy", 1, 2, tiled=False
    )
    query_full = spread[..., :query_width].reshape(steps, local_rows, -1)
    key_full = spread[..., query_width : query_width + key_width].reshape(steps, local_rows, -1)
    value_full = spread[..., query_width + key_width :].reshape(steps, local_rows, -1)

    token_positions = (
        cache_lengths[None, :] + jnp.arange(steps, dtype=jnp.int32)[:, None]
    ).reshape(-1)
    query_rot = rotary_embedding(
        query_full.astype(jnp.float32).reshape(steps * local_rows, QUERY_HEADS, HEAD_FEATURES),
        token_positions,
    ).astype(jnp.bfloat16)
    key_rot = rotary_embedding(
        key_full.astype(jnp.float32).reshape(steps * local_rows, KEY_VALUE_HEADS, HEAD_FEATURES),
        token_positions,
    ).astype(jnp.bfloat16)
    mixed_local = attend(
        query_rot.reshape(steps, local_rows, -1),
        cache_keys,
        cache_values,
        key_rot.reshape(steps, local_rows, -1),
        value_full,
        cache_lengths,
    )
    head_group = lax.all_to_all(
        mixed_local.reshape(steps, local_rows, across_second, -1), "gy", 2, 1, tiled=False
    ).reshape(steps, across_second * local_rows, -1)
    mixed_all = split_half_gather_steps(head_group, "gx", across_first)
    rank_part_out = jnp.einsum(
        "tbnq,bqr->tbnr",
        mixed_all.reshape(steps, block_count, block_rows, -1),
        output_first,
        preferred_element_type=jnp.float32,
    )
    rank_output = sum_then_spread(rank_part_out, ("gy",), ("gx",))
    delta_output = jnp.einsum(
        "tbnr,bre->tbne", rank_output, output_second, preferred_element_type=jnp.float32
    ).reshape(steps, request_count, -1)
    partial_out = (
        jnp.einsum("tnq,qe->tne", mixed_all, output_weight, preferred_element_type=jnp.float32)
        + delta_output
    )
    return halving_scatter(partial_out, "gy", across_second).astype(jnp.bfloat16)


def solution(mesh):
    in_specs = (
        P(None, "gy", "gx"),
        P("gx"),
        P("gx", "gy"),
        P("gx", "gy"),
        P("gx", "gy"),
        P("gy", "gx"),
        P("gy", "gx", None),
        P("gx", None, "gy"),
        P("gx", "gy", None),
        P("gy", None, "gx"),
        P(),
        P(("gx", "gy")),
        P(("gx", "gy"), None, None),
        P(("gx", "gy"), None, None),
    )
    out_specs = P(None, "gy", "gx")
    return jax.shard_map(local, mesh=mesh, in_specs=in_specs, out_specs=out_specs, check_vma=False)
```

```python
import jax
import jax.numpy as jnp
from jax import lax
from jax.sharding import PartitionSpec as P

QUERY_HEADS = 64
KEY_VALUE_HEADS = 8
HEAD_FEATURES = 128
BLOCK = 128


EPS = 1e-05
THETA = 500000.0


def rotary_embedding(values_in, token_positions):
    half_size = values_in.shape[-1] // 2
    exponent = jnp.arange(half_size, dtype=jnp.float32) * 2.0 / values_in.shape[-1]
    frequency = THETA ** (-exponent)
    angles = token_positions.astype(jnp.float32)[:, None] * frequency[None, :]
    cosine = jnp.cos(angles)[:, None, :]
    sine_part = jnp.sin(angles)[:, None, :]
    lower = values_in[..., :half_size]
    upper = values_in[..., half_size:]
    return jnp.concatenate(
        [lower * cosine - upper * sine_part, upper * cosine + lower * sine_part], axis=-1
    )


def pick_adapters(table, adapter_ids, owner_index):
    table_count = table.shape[0]
    picked = []
    for block in range(adapter_ids.shape[0]):
        wanted = adapter_ids[block]
        owned = (wanted // table_count) == owner_index
        entry = lax.dynamic_index_in_dim(table, wanted % table_count, axis=0, keepdims=False)
        picked.append(jnp.where(owned, entry, jnp.zeros_like(entry)))
    return jnp.stack(picked)


def reduce_scatter_rows(partial, axis_name, axis_size):
    steps, rows, columns = partial.shape
    pieces = partial.astype(jnp.bfloat16).reshape(steps, axis_size, rows // axis_size, columns)
    received = lax.all_to_all(pieces, axis_name, 1, 1, tiled=False)
    return jnp.sum(received.astype(jnp.float32), axis=1)


def split_half_scatter_steps(partial, axis_name, axis_size):
    return jnp.concatenate(
        [
            split_half_scatter(partial[step : step + 1], axis_name, axis_size)
            for step in range(partial.shape[0])
        ]
    )


def split_half_gather_steps(value, axis_name, axis_size):
    return jnp.concatenate(
        [
            split_half_gather(value[step : step + 1], axis_name, axis_size)
            for step in range(value.shape[0])
        ]
    )


def ring_gather(value, axis_name, axis_size):
    if axis_size < 4 or axis_size % 2:
        return lax.all_gather(value, axis_name, axis=1, tiled=True)
    ring = list(range(0, axis_size, 2)) + list(range(axis_size - 1, 0, -2))
    place = [0] * axis_size
    for position, index in enumerate(ring):
        place[index] = position
    ahead = [(ring[p], ring[(p + 1) % axis_size]) for p in range(axis_size)]
    behind = [(ring[p], ring[(p - 1) % axis_size]) for p in range(axis_size)]
    slots = [None] * axis_size
    slots[0] = value
    forward = backward = value
    for hop in range(1, axis_size // 2 + 1):
        forward = lax.ppermute(forward, axis_name, ahead)
        slots[(-hop) % axis_size] = forward
        if hop < axis_size - hop:
            backward = lax.ppermute(backward, axis_name, behind)
            slots[hop] = backward
    stacked = jnp.stack(slots)
    places = jnp.asarray(place, dtype=jnp.int32)
    me = lax.axis_index(axis_name)
    order = (places - places[me]) % axis_size
    gathered = jnp.take(stacked, order, axis=0)
    steps, rows, columns = value.shape
    return gathered.transpose(1, 0, 2, 3).reshape(steps, axis_size * rows, columns)


def split_half_scatter(partial, axis_name, axis_size):
    steps, rows, columns = partial.shape
    if axis_size < 4 or axis_size & (axis_size - 1):
        return reduce_scatter_rows(partial, axis_name, axis_size)
    half = axis_size // 2
    me = lax.axis_index(axis_name)
    chunks = partial.reshape(steps, axis_size, rows // axis_size, columns)
    narrow = chunks.astype(jnp.bfloat16)
    own = lax.dynamic_index_in_dim(chunks, me, axis=1, keepdims=False)
    mirror = lax.dynamic_index_in_dim(chunks, me ^ half, axis=1, keepdims=False)
    for offset in range(1, half):
        peer = me ^ offset
        outgoing = jnp.stack(
            [
                lax.dynamic_index_in_dim(narrow, peer, axis=1, keepdims=False),
                lax.dynamic_index_in_dim(narrow, peer ^ half, axis=1, keepdims=False),
            ]
        )
        incoming = lax.ppermute(
            outgoing, axis_name, [(i, i ^ offset) for i in range(axis_size)]
        ).astype(jnp.float32)
        own = own + incoming[0]
        mirror = mirror + incoming[1]
    across = lax.ppermute(
        mirror.astype(jnp.bfloat16), axis_name, [(i, i ^ half) for i in range(axis_size)]
    )
    return own + across.astype(jnp.float32)


def doubling_gather(value, axis_name, axis_size, axis):
    if axis_size & (axis_size - 1):
        return lax.all_gather(value, axis_name, axis=axis, tiled=True)
    me = lax.axis_index(axis_name)
    held = value
    distance = 1
    while distance < axis_size:
        other = lax.ppermute(held, axis_name, [(i, i ^ distance) for i in range(axis_size)])
        upper = (me // distance) % 2 == 1
        first = jnp.where(upper, other, held)
        second = jnp.where(upper, held, other)
        held = jnp.concatenate([first, second], axis=axis)
        distance *= 2
    return held


def split_half_gather(value, axis_name, axis_size):
    if axis_size < 4 or axis_size & (axis_size - 1):
        return lax.all_gather(value, axis_name, axis=1, tiled=True)
    half = axis_size // 2
    me = lax.axis_index(axis_name)
    mirror = lax.ppermute(value, axis_name, [(i, i ^ half) for i in range(axis_size)])
    pair = jnp.stack([value, mirror])
    slots = [None] * axis_size
    slots[0], slots[half] = value, mirror
    for offset in range(1, half):
        incoming = lax.ppermute(pair, axis_name, [(i, i ^ offset) for i in range(axis_size)])
        slots[offset], slots[offset + half] = incoming[0], incoming[1]
    stacked = jnp.stack(slots)
    order = jnp.arange(axis_size, dtype=jnp.int32) ^ me
    gathered = jnp.take(stacked, order, axis=0)
    steps, rows, columns = value.shape
    return gathered.transpose(1, 0, 2, 3).reshape(steps, axis_size * rows, columns)


def tree_sum(value, axes):
    for axis_name in axes:
        size = lax.axis_size(axis_name)
        if size & (size - 1):
            value = lax.psum(value, axis_name)
            continue
        distance = 1
        while distance < size:
            pairs = [(i, i ^ distance) for i in range(size)]
            value = value + lax.ppermute(value, axis_name, pairs)
            distance *= 2
    return value


def sum_then_spread(value, sum_axes, spread_axes):
    return tree_sum(tree_sum(value, sum_axes).astype(jnp.bfloat16), spread_axes)


def halving_scatter(partial, axis_name, axis_size):
    steps, rows, columns = partial.shape
    if axis_size & (axis_size - 1):
        return lax.psum_scatter(partial, axis_name, scatter_dimension=1, tiled=True)
    me = lax.axis_index(axis_name)
    held = partial.reshape(steps, axis_size, rows // axis_size, columns)
    distance = 1
    while distance < axis_size:
        count = held.shape[1]
        pairs = held.reshape(steps, count // 2, 2, rows // axis_size, columns)
        mine = (me // distance) % 2
        keep = lax.dynamic_index_in_dim(pairs, mine, axis=2, keepdims=False)
        give = lax.dynamic_index_in_dim(pairs, 1 - mine, axis=2, keepdims=False)
        swap = [(i, i ^ distance) for i in range(axis_size)]
        if distance > 1:
            give = give.astype(jnp.bfloat16)
        held = keep + lax.ppermute(give, axis_name, swap).astype(jnp.float32)
        distance *= 2
    return held.reshape(steps, rows // axis_size, columns)


def attend(query_rows, previous_keys, previous_values, incoming_keys, incoming_values, lengths):
    steps, count_of_rows = query_rows.shape[0], query_rows.shape[1]
    groups = QUERY_HEADS // KEY_VALUE_HEADS
    context_window = previous_keys.shape[1]
    grouped_heads = query_rows.reshape(
        steps, count_of_rows, KEY_VALUE_HEADS, groups, HEAD_FEATURES
    ).transpose(1, 2, 0, 3, 4).reshape(count_of_rows, KEY_VALUE_HEADS, steps * groups, HEAD_FEATURES)
    keys_previous = previous_keys.reshape(
        count_of_rows, context_window, KEY_VALUE_HEADS, HEAD_FEATURES
    )
    values_previous = previous_values.reshape(
        count_of_rows, context_window, KEY_VALUE_HEADS, HEAD_FEATURES
    )
    keys_incoming = incoming_keys.reshape(
        steps, count_of_rows, KEY_VALUE_HEADS, HEAD_FEATURES
    ).transpose(1, 0, 2, 3)
    values_incoming = incoming_values.reshape(
        steps, count_of_rows, KEY_VALUE_HEADS, HEAD_FEATURES
    ).transpose(1, 0, 2, 3)
    factor = HEAD_FEATURES ** (-0.5)
    score_old = (
        jnp.einsum(
            "rhqd,rchd->rhqc", grouped_heads, keys_previous, preferred_element_type=jnp.float32
        )
        * factor
    )
    score_new = (
        jnp.einsum(
            "rhqd,rshd->rhqs", grouped_heads, keys_incoming, preferred_element_type=jnp.float32
        )
        * factor
    )
    live_old = (jnp.arange(context_window, dtype=jnp.int32)[None, :] < lengths[:, None])[
        :, None, None, :
    ]
    query_step = jnp.arange(steps * groups, dtype=jnp.int32) // groups
    live_new = (jnp.arange(steps, dtype=jnp.int32)[None, :] <= query_step[:, None])[
        None, None, :, :
    ]
    score_old = jnp.where(live_old, score_old, -1e30)
    score_new = jnp.where(live_new, score_new, -1e30)
    peak_score = jnp.maximum(jnp.max(score_old, axis=-1), jnp.max(score_new, axis=-1))
    weight_old = jnp.where(live_old, jnp.exp(score_old - peak_score[..., None]), 0.0)
    weight_new = jnp.where(live_new, jnp.exp(score_new - peak_score[..., None]), 0.0)
    weight_sum = jnp.sum(weight_old, axis=-1) + jnp.sum(weight_new, axis=-1)
    mixed_out = jnp.einsum(
        "rhqc,rchd->rhqd",
        weight_old.astype(jnp.bfloat16),
        values_previous,
        preferred_element_type=jnp.float32,
    )
    mixed_out = mixed_out + jnp.einsum(
        "rhqs,rshd->rhqd",
        weight_new.astype(jnp.bfloat16),
        values_incoming,
        preferred_element_type=jnp.float32,
    )
    mixed_out = (mixed_out / weight_sum[..., None]).astype(jnp.bfloat16)
    return mixed_out.reshape(
        count_of_rows, KEY_VALUE_HEADS, steps, groups, HEAD_FEATURES
    ).transpose(2, 0, 1, 3, 4).reshape(steps, count_of_rows, -1)


def local(
    inputs,
    norm_gain,
    query_weight,
    key_weight,
    value_weight,
    output_weight,
    query_down,
    query_up,
    output_down,
    output_up,
    block_adapter,
    cache_lengths,
    cache_keys,
    cache_values,
):
    across_first = lax.axis_size("gx")
    across_second = lax.axis_size("gy")
    index_first = lax.axis_index("gx")
    index_second = lax.axis_index("gy")
    steps = inputs.shape[0]
    request_count = inputs.shape[1] * across_second
    width = inputs.shape[2] * across_first
    local_rows = cache_keys.shape[0]
    block_count = block_adapter.shape[0]
    block_rows = request_count // block_count
    query_width = query_weight.shape[1]
    key_width = key_weight.shape[1]
    norm_scale = norm_gain.astype(jnp.float32)
    query_first = pick_adapters(query_down, block_adapter, index_second)
    query_second = pick_adapters(query_up, block_adapter, index_first)
    output_first = pick_adapters(output_down, block_adapter, index_first)
    output_second = pick_adapters(output_up, block_adapter, index_second)

    rows_all = doubling_gather(inputs, "gy", across_second, 1)
    rows_wide = rows_all.astype(jnp.float32)
    squares = tree_sum(jnp.sum(rows_wide * rows_wide, axis=2), ("gx",))
    factor_rows = lax.rsqrt(squares / width + EPS)
    normed = (rows_wide * factor_rows[..., None] * norm_scale).astype(jnp.bfloat16)

    blocked = normed.reshape(steps, block_count, block_rows, -1)
    rank_part = jnp.einsum(
        "tbnd,bdr->tbnr", blocked, query_first, preferred_element_type=jnp.float32
    )
    rank_query = sum_then_spread(rank_part, ("gx",), ("gy",))
    delta_query = jnp.einsum(
        "tbnr,bre->tbne", rank_query, query_second, preferred_element_type=jnp.float32
    ).reshape(steps, request_count, -1)
    part_query = (
        jnp.einsum("tnd,de->tne", normed, query_weight, preferred_element_type=jnp.float32)
        + delta_query
    )
    part_key = jnp.einsum("tnd,de->tne", normed, key_weight, preferred_element_type=jnp.float32)
    part_value = jnp.einsum(
        "tnd,de->tne", normed, value_weight, preferred_element_type=jnp.float32
    )
    joined = jnp.concatenate([part_query, part_key, part_value], axis=-1)
    summed = split_half_scatter_steps(joined, "gx", across_first).astype(jnp.bfloat16)
    chunk_rows = summed.shape[1] // across_second
    spread = lax.all_to_all(
        summed.reshape(steps, across_second, chunk_rows, -1), "gy", 1, 2, tiled=False
    )
    query_full = spread[..., :query_width].reshape(steps, local_rows, -1)
    key_full = spread[..., query_width : query_width + key_width].reshape(steps, local_rows, -1)
    value_full = spread[..., query_width + key_width :].reshape(steps, local_rows, -1)

    token_positions = (
        cache_lengths[None, :] + jnp.arange(steps, dtype=jnp.int32)[:, None]
    ).reshape(-1)
    query_rot = rotary_embedding(
        query_full.astype(jnp.float32).reshape(steps * local_rows, QUERY_HEADS, HEAD_FEATURES),
        token_positions,
    ).astype(jnp.bfloat16)
    key_rot = rotary_embedding(
        key_full.astype(jnp.float32).reshape(steps * local_rows, KEY_VALUE_HEADS, HEAD_FEATURES),
        token_positions,
    ).astype(jnp.bfloat16)
    mixed_local = attend(
        query_rot.reshape(steps, local_rows, -1),
        cache_keys,
        cache_values,
        key_rot.reshape(steps, local_rows, -1),
        value_full,
        cache_lengths,
    )
    head_group = lax.all_to_all(
        mixed_local.reshape(steps, local_rows, across_second, -1), "gy", 2, 1, tiled=False
    ).reshape(steps, across_second * local_rows, -1)
    mixed_all = ring_gather(head_group, "gx", across_first)
    rank_part_out = jnp.einsum(
        "tbnq,bqr->tbnr",
        mixed_all.reshape(steps, block_count, block_rows, -1),
        output_first,
        preferred_element_type=jnp.float32,
    )
    rank_output = sum_then_spread(rank_part_out, ("gy",), ("gx",))
    delta_output = jnp.einsum(
        "tbnr,bre->tbne", rank_output, output_second, preferred_element_type=jnp.float32
    ).reshape(steps, request_count, -1)
    partial_out = (
        jnp.einsum("tnq,qe->tne", mixed_all, output_weight, preferred_element_type=jnp.float32)
        + delta_output
    )
    return halving_scatter(partial_out, "gy", across_second).astype(jnp.bfloat16)


def solution(mesh):
    in_specs = (
        P(None, "gy", "gx"),
        P("gx"),
        P("gx", "gy"),
        P("gx", "gy"),
        P("gx", "gy"),
        P("gy", "gx"),
        P("gy", "gx", None),
        P("gx", None, "gy"),
        P("gx", "gy", None),
        P("gy", None, "gx"),
        P(),
        P(("gx", "gy")),
        P(("gx", "gy"), None, None),
        P(("gx", "gy"), None, None),
    )
    out_specs = P(None, "gy", "gx")
    return jax.shard_map(local, mesh=mesh, in_specs=in_specs, out_specs=out_specs, check_vma=False)
```

```python
import jax
import jax.numpy as jnp
from jax import lax
from jax.sharding import PartitionSpec as P

QUERY_HEADS = 64
KEY_VALUE_HEADS = 8
HEAD_FEATURES = 128
BLOCK = 128


EPS = 1e-05
THETA = 500000.0


def rotary_embedding(values_in, token_positions):
    half_size = values_in.shape[-1] // 2
    exponent = jnp.arange(half_size, dtype=jnp.float32) * 2.0 / values_in.shape[-1]
    frequency = THETA ** (-exponent)
    angles = token_positions.astype(jnp.float32)[:, None] * frequency[None, :]
    cosine = jnp.cos(angles)[:, None, :]
    sine_part = jnp.sin(angles)[:, None, :]
    lower = values_in[..., :half_size]
    upper = values_in[..., half_size:]
    return jnp.concatenate(
        [lower * cosine - upper * sine_part, upper * cosine + lower * sine_part], axis=-1
    )


def pick_adapters(table, adapter_ids, owner_index):
    table_count = table.shape[0]
    picked = []
    for block in range(adapter_ids.shape[0]):
        wanted = adapter_ids[block]
        owned = (wanted // table_count) == owner_index
        entry = lax.dynamic_index_in_dim(table, wanted % table_count, axis=0, keepdims=False)
        picked.append(jnp.where(owned, entry, jnp.zeros_like(entry)))
    return jnp.stack(picked)


def reduce_scatter_rows(partial, axis_name, axis_size):
    steps, rows, columns = partial.shape
    pieces = partial.astype(jnp.bfloat16).reshape(steps, axis_size, rows // axis_size, columns)
    received = lax.all_to_all(pieces, axis_name, 1, 1, tiled=False)
    return jnp.sum(received.astype(jnp.float32), axis=1)


def split_half_scatter_steps(partial, axis_name, axis_size):
    return jnp.concatenate(
        [
            split_half_scatter(partial[step : step + 1], axis_name, axis_size)
            for step in range(partial.shape[0])
        ]
    )


def split_half_gather_steps(value, axis_name, axis_size):
    return jnp.concatenate(
        [
            split_half_gather(value[step : step + 1], axis_name, axis_size)
            for step in range(value.shape[0])
        ]
    )


def permute_all_to_all(value, axis_name, axis_size, split_axis, concat_axis):
    if axis_size & (axis_size - 1):
        return lax.all_to_all(value, axis_name, split_axis, concat_axis, tiled=False)
    me = lax.axis_index(axis_name)
    received = []
    for offset in range(axis_size):
        piece = lax.dynamic_index_in_dim(value, me ^ offset, axis=split_axis, keepdims=False)
        if offset:
            piece = lax.ppermute(piece, axis_name, [(i, i ^ offset) for i in range(axis_size)])
        received.append(piece)
    stacked = jnp.stack(received)
    order = jnp.arange(axis_size, dtype=jnp.int32) ^ me
    return jnp.moveaxis(jnp.take(stacked, order, axis=0), 0, concat_axis)


def ring_gather(value, axis_name, axis_size):
    if axis_size < 4 or axis_size % 2:
        return lax.all_gather(value, axis_name, axis=1, tiled=True)
    ring = list(range(0, axis_size, 2)) + list(range(axis_size - 1, 0, -2))
    place = [0] * axis_size
    for position, index in enumerate(ring):
        place[index] = position
    ahead = [(ring[p], ring[(p + 1) % axis_size]) for p in range(axis_size)]
    behind = [(ring[p], ring[(p - 1) % axis_size]) for p in range(axis_size)]
    slots = [None] * axis_size
    slots[0] = value
    forward = backward = value
    for hop in range(1, axis_size // 2 + 1):
        forward = lax.ppermute(forward, axis_name, ahead)
        slots[(-hop) % axis_size] = forward
        if hop < axis_size - hop:
            backward = lax.ppermute(backward, axis_name, behind)
            slots[hop] = backward
    stacked = jnp.stack(slots)
    places = jnp.asarray(place, dtype=jnp.int32)
    me = lax.axis_index(axis_name)
    order = (places - places[me]) % axis_size
    gathered = jnp.take(stacked, order, axis=0)
    steps, rows, columns = value.shape
    return gathered.transpose(1, 0, 2, 3).reshape(steps, axis_size * rows, columns)


def split_half_scatter(partial, axis_name, axis_size):
    steps, rows, columns = partial.shape
    if axis_size < 4 or axis_size & (axis_size - 1):
        return reduce_scatter_rows(partial, axis_name, axis_size)
    half = axis_size // 2
    me = lax.axis_index(axis_name)
    chunks = partial.reshape(steps, axis_size, rows // axis_size, columns)
    narrow = chunks.astype(jnp.bfloat16)
    own = lax.dynamic_index_in_dim(chunks, me, axis=1, keepdims=False)
    mirror = lax.dynamic_index_in_dim(chunks, me ^ half, axis=1, keepdims=False)
    for offset in range(1, half):
        peer = me ^ offset
        outgoing = jnp.stack(
            [
                lax.dynamic_index_in_dim(narrow, peer, axis=1, keepdims=False),
                lax.dynamic_index_in_dim(narrow, peer ^ half, axis=1, keepdims=False),
            ]
        )
        incoming = lax.ppermute(
            outgoing, axis_name, [(i, i ^ offset) for i in range(axis_size)]
        ).astype(jnp.float32)
        own = own + incoming[0]
        mirror = mirror + incoming[1]
    across = lax.ppermute(
        mirror.astype(jnp.bfloat16), axis_name, [(i, i ^ half) for i in range(axis_size)]
    )
    return own + across.astype(jnp.float32)


def doubling_gather(value, axis_name, axis_size, axis):
    if axis_size & (axis_size - 1):
        return lax.all_gather(value, axis_name, axis=axis, tiled=True)
    me = lax.axis_index(axis_name)
    held = value
    distance = 1
    while distance < axis_size:
        other = lax.ppermute(held, axis_name, [(i, i ^ distance) for i in range(axis_size)])
        upper = (me // distance) % 2 == 1
        first = jnp.where(upper, other, held)
        second = jnp.where(upper, held, other)
        held = jnp.concatenate([first, second], axis=axis)
        distance *= 2
    return held


def split_half_gather(value, axis_name, axis_size):
    if axis_size < 4 or axis_size & (axis_size - 1):
        return lax.all_gather(value, axis_name, axis=1, tiled=True)
    half = axis_size // 2
    me = lax.axis_index(axis_name)
    mirror = lax.ppermute(value, axis_name, [(i, i ^ half) for i in range(axis_size)])
    pair = jnp.stack([value, mirror])
    slots = [None] * axis_size
    slots[0], slots[half] = value, mirror
    for offset in range(1, half):
        incoming = lax.ppermute(pair, axis_name, [(i, i ^ offset) for i in range(axis_size)])
        slots[offset], slots[offset + half] = incoming[0], incoming[1]
    stacked = jnp.stack(slots)
    order = jnp.arange(axis_size, dtype=jnp.int32) ^ me
    gathered = jnp.take(stacked, order, axis=0)
    steps, rows, columns = value.shape
    return gathered.transpose(1, 0, 2, 3).reshape(steps, axis_size * rows, columns)


def tree_sum(value, axes):
    for axis_name in axes:
        size = lax.axis_size(axis_name)
        if size & (size - 1):
            value = lax.psum(value, axis_name)
            continue
        distance = 1
        while distance < size:
            pairs = [(i, i ^ distance) for i in range(size)]
            value = value + lax.ppermute(value, axis_name, pairs)
            distance *= 2
    return value


def sum_then_spread(value, sum_axes, spread_axes):
    return tree_sum(tree_sum(value, sum_axes).astype(jnp.bfloat16), spread_axes)


def halving_scatter(partial, axis_name, axis_size):
    steps, rows, columns = partial.shape
    if axis_size & (axis_size - 1):
        return lax.psum_scatter(partial, axis_name, scatter_dimension=1, tiled=True)
    me = lax.axis_index(axis_name)
    held = partial.reshape(steps, axis_size, rows // axis_size, columns)
    distance = 1
    while distance < axis_size:
        count = held.shape[1]
        pairs = held.reshape(steps, count // 2, 2, rows // axis_size, columns)
        mine = (me // distance) % 2
        keep = lax.dynamic_index_in_dim(pairs, mine, axis=2, keepdims=False)
        give = lax.dynamic_index_in_dim(pairs, 1 - mine, axis=2, keepdims=False)
        swap = [(i, i ^ distance) for i in range(axis_size)]
        if distance > 1:
            give = give.astype(jnp.bfloat16)
        held = keep + lax.ppermute(give, axis_name, swap).astype(jnp.float32)
        distance *= 2
    return held.reshape(steps, rows // axis_size, columns)


def attend(query_rows, previous_keys, previous_values, incoming_keys, incoming_values, lengths):
    steps, count_of_rows = query_rows.shape[0], query_rows.shape[1]
    groups = QUERY_HEADS // KEY_VALUE_HEADS
    context_window = previous_keys.shape[1]
    grouped_heads = query_rows.reshape(
        steps, count_of_rows, KEY_VALUE_HEADS, groups, HEAD_FEATURES
    ).transpose(1, 2, 0, 3, 4).reshape(count_of_rows, KEY_VALUE_HEADS, steps * groups, HEAD_FEATURES)
    keys_previous = previous_keys.reshape(
        count_of_rows, context_window, KEY_VALUE_HEADS, HEAD_FEATURES
    )
    values_previous = previous_values.reshape(
        count_of_rows, context_window, KEY_VALUE_HEADS, HEAD_FEATURES
    )
    keys_incoming = incoming_keys.reshape(
        steps, count_of_rows, KEY_VALUE_HEADS, HEAD_FEATURES
    ).transpose(1, 0, 2, 3)
    values_incoming = incoming_values.reshape(
        steps, count_of_rows, KEY_VALUE_HEADS, HEAD_FEATURES
    ).transpose(1, 0, 2, 3)
    factor = HEAD_FEATURES ** (-0.5)
    score_old = (
        jnp.einsum(
            "rhqd,rchd->rhqc", grouped_heads, keys_previous, preferred_element_type=jnp.float32
        )
        * factor
    )
    score_new = (
        jnp.einsum(
            "rhqd,rshd->rhqs", grouped_heads, keys_incoming, preferred_element_type=jnp.float32
        )
        * factor
    )
    live_old = (jnp.arange(context_window, dtype=jnp.int32)[None, :] < lengths[:, None])[
        :, None, None, :
    ]
    query_step = jnp.arange(steps * groups, dtype=jnp.int32) // groups
    live_new = (jnp.arange(steps, dtype=jnp.int32)[None, :] <= query_step[:, None])[
        None, None, :, :
    ]
    score_old = jnp.where(live_old, score_old, -1e30)
    score_new = jnp.where(live_new, score_new, -1e30)
    peak_score = jnp.maximum(jnp.max(score_old, axis=-1), jnp.max(score_new, axis=-1))
    weight_old = jnp.where(live_old, jnp.exp(score_old - peak_score[..., None]), 0.0)
    weight_new = jnp.where(live_new, jnp.exp(score_new - peak_score[..., None]), 0.0)
    weight_sum = jnp.sum(weight_old, axis=-1) + jnp.sum(weight_new, axis=-1)
    mixed_out = jnp.einsum(
        "rhqc,rchd->rhqd",
        weight_old.astype(jnp.bfloat16),
        values_previous,
        preferred_element_type=jnp.float32,
    )
    mixed_out = mixed_out + jnp.einsum(
        "rhqs,rshd->rhqd",
        weight_new.astype(jnp.bfloat16),
        values_incoming,
        preferred_element_type=jnp.float32,
    )
    mixed_out = (mixed_out / weight_sum[..., None]).astype(jnp.bfloat16)
    return mixed_out.reshape(
        count_of_rows, KEY_VALUE_HEADS, steps, groups, HEAD_FEATURES
    ).transpose(2, 0, 1, 3, 4).reshape(steps, count_of_rows, -1)


def local(
    inputs,
    norm_gain,
    query_weight,
    key_weight,
    value_weight,
    output_weight,
    query_down,
    query_up,
    output_down,
    output_up,
    block_adapter,
    cache_lengths,
    cache_keys,
    cache_values,
):
    across_first = lax.axis_size("gx")
    across_second = lax.axis_size("gy")
    index_first = lax.axis_index("gx")
    index_second = lax.axis_index("gy")
    steps = inputs.shape[0]
    request_count = inputs.shape[1] * across_second
    width = inputs.shape[2] * across_first
    local_rows = cache_keys.shape[0]
    block_count = block_adapter.shape[0]
    block_rows = request_count // block_count
    query_width = query_weight.shape[1]
    key_width = key_weight.shape[1]
    norm_scale = norm_gain.astype(jnp.float32)
    query_first = pick_adapters(query_down, block_adapter, index_second)
    query_second = pick_adapters(query_up, block_adapter, index_first)
    output_first = pick_adapters(output_down, block_adapter, index_first)
    output_second = pick_adapters(output_up, block_adapter, index_second)

    rows_all = doubling_gather(inputs, "gy", across_second, 1)
    rows_wide = rows_all.astype(jnp.float32)
    squares = tree_sum(jnp.sum(rows_wide * rows_wide, axis=2), ("gx",))
    factor_rows = lax.rsqrt(squares / width + EPS)
    normed = (rows_wide * factor_rows[..., None] * norm_scale).astype(jnp.bfloat16)

    blocked = normed.reshape(steps, block_count, block_rows, -1)
    rank_part = jnp.einsum(
        "tbnd,bdr->tbnr", blocked, query_first, preferred_element_type=jnp.float32
    )
    rank_query = sum_then_spread(rank_part, ("gx",), ("gy",))
    delta_query = jnp.einsum(
        "tbnr,bre->tbne", rank_query, query_second, preferred_element_type=jnp.float32
    ).reshape(steps, request_count, -1)
    part_query = (
        jnp.einsum("tnd,de->tne", normed, query_weight, preferred_element_type=jnp.float32)
        + delta_query
    )
    part_key = jnp.einsum("tnd,de->tne", normed, key_weight, preferred_element_type=jnp.float32)
    part_value = jnp.einsum(
        "tnd,de->tne", normed, value_weight, preferred_element_type=jnp.float32
    )
    joined = jnp.concatenate([part_query, part_key, part_value], axis=-1)
    summed = split_half_scatter_steps(joined, "gx", across_first).astype(jnp.bfloat16)
    chunk_rows = summed.shape[1] // across_second
    spread = permute_all_to_all(
        summed.reshape(steps, across_second, chunk_rows, -1), "gy", across_second, 1, 2
    )
    query_full = spread[..., :query_width].reshape(steps, local_rows, -1)
    key_full = spread[..., query_width : query_width + key_width].reshape(steps, local_rows, -1)
    value_full = spread[..., query_width + key_width :].reshape(steps, local_rows, -1)

    token_positions = (
        cache_lengths[None, :] + jnp.arange(steps, dtype=jnp.int32)[:, None]
    ).reshape(-1)
    query_rot = rotary_embedding(
        query_full.astype(jnp.float32).reshape(steps * local_rows, QUERY_HEADS, HEAD_FEATURES),
        token_positions,
    ).astype(jnp.bfloat16)
    key_rot = rotary_embedding(
        key_full.astype(jnp.float32).reshape(steps * local_rows, KEY_VALUE_HEADS, HEAD_FEATURES),
        token_positions,
    ).astype(jnp.bfloat16)
    mixed_local = attend(
        query_rot.reshape(steps, local_rows, -1),
        cache_keys,
        cache_values,
        key_rot.reshape(steps, local_rows, -1),
        value_full,
        cache_lengths,
    )
    head_group = permute_all_to_all(
        mixed_local.reshape(steps, local_rows, across_second, -1), "gy", across_second, 2, 1
    ).reshape(steps, across_second * local_rows, -1)
    mixed_all = ring_gather(head_group, "gx", across_first)
    rank_part_out = jnp.einsum(
        "tbnq,bqr->tbnr",
        mixed_all.reshape(steps, block_count, block_rows, -1),
        output_first,
        preferred_element_type=jnp.float32,
    )
    rank_output = sum_then_spread(rank_part_out, ("gy",), ("gx",))
    delta_output = jnp.einsum(
        "tbnr,bre->tbne", rank_output, output_second, preferred_element_type=jnp.float32
    ).reshape(steps, request_count, -1)
    partial_out = (
        jnp.einsum("tnq,qe->tne", mixed_all, output_weight, preferred_element_type=jnp.float32)
        + delta_output
    )
    return halving_scatter(partial_out, "gy", across_second).astype(jnp.bfloat16)


def solution(mesh):
    in_specs = (
        P(None, "gy", "gx"),
        P("gx"),
        P("gx", "gy"),
        P("gx", "gy"),
        P("gx", "gy"),
        P("gy", "gx"),
        P("gy", "gx", None),
        P("gx", None, "gy"),
        P("gx", "gy", None),
        P("gy", None, "gx"),
        P(),
        P(("gx", "gy")),
        P(("gx", "gy"), None, None),
        P(("gx", "gy"), None, None),
    )
    out_specs = P(None, "gy", "gx")
    return jax.shard_map(local, mesh=mesh, in_specs=in_specs, out_specs=out_specs, check_vma=False)
```

```python
import jax
import jax.numpy as jnp
from jax import lax
from jax.sharding import PartitionSpec as P

QUERY_HEADS = 64
KEY_VALUE_HEADS = 8
HEAD_FEATURES = 128
BLOCK = 128


EPS = 1e-05
THETA = 500000.0


def rotary_embedding(values_in, token_positions):
    half_size = values_in.shape[-1] // 2
    exponent = jnp.arange(half_size, dtype=jnp.float32) * 2.0 / values_in.shape[-1]
    frequency = THETA ** (-exponent)
    angles = token_positions.astype(jnp.float32)[:, None] * frequency[None, :]
    cosine = jnp.cos(angles)[:, None, :]
    sine_part = jnp.sin(angles)[:, None, :]
    lower = values_in[..., :half_size]
    upper = values_in[..., half_size:]
    return jnp.concatenate(
        [lower * cosine - upper * sine_part, upper * cosine + lower * sine_part], axis=-1
    )


def pick_adapters(table, adapter_ids, owner_index):
    table_count = table.shape[0]
    picked = []
    for block in range(adapter_ids.shape[0]):
        wanted = adapter_ids[block]
        owned = (wanted // table_count) == owner_index
        entry = lax.dynamic_index_in_dim(table, wanted % table_count, axis=0, keepdims=False)
        picked.append(jnp.where(owned, entry, jnp.zeros_like(entry)))
    return jnp.stack(picked)


def reduce_scatter_rows(partial, axis_name, axis_size):
    steps, rows, columns = partial.shape
    pieces = partial.astype(jnp.bfloat16).reshape(steps, axis_size, rows // axis_size, columns)
    received = lax.all_to_all(pieces, axis_name, 1, 1, tiled=False)
    return jnp.sum(received.astype(jnp.float32), axis=1)


def split_half_scatter_steps(partial, axis_name, axis_size):
    return jnp.concatenate(
        [
            split_half_scatter(partial[step : step + 1], axis_name, axis_size)
            for step in range(partial.shape[0])
        ]
    )


def split_half_gather_steps(value, axis_name, axis_size):
    return jnp.concatenate(
        [
            split_half_gather(value[step : step + 1], axis_name, axis_size)
            for step in range(value.shape[0])
        ]
    )


def ring_gather(value, axis_name, axis_size):
    if axis_size < 4 or axis_size % 2:
        return lax.all_gather(value, axis_name, axis=1, tiled=True)
    ring = list(range(0, axis_size, 2)) + list(range(axis_size - 1, 0, -2))
    place = [0] * axis_size
    for position, index in enumerate(ring):
        place[index] = position
    ahead = [(ring[p], ring[(p + 1) % axis_size]) for p in range(axis_size)]
    behind = [(ring[p], ring[(p - 1) % axis_size]) for p in range(axis_size)]
    slots = [None] * axis_size
    slots[0] = value
    forward = backward = value
    for hop in range(1, axis_size // 2 + 1):
        forward = lax.ppermute(forward, axis_name, ahead)
        slots[(-hop) % axis_size] = forward
        if hop < axis_size - hop:
            backward = lax.ppermute(backward, axis_name, behind)
            slots[hop] = backward
    stacked = jnp.stack(slots)
    places = jnp.asarray(place, dtype=jnp.int32)
    me = lax.axis_index(axis_name)
    order = (places - places[me]) % axis_size
    gathered = jnp.take(stacked, order, axis=0)
    steps, rows, columns = value.shape
    return gathered.transpose(1, 0, 2, 3).reshape(steps, axis_size * rows, columns)


def split_half_scatter(partial, axis_name, axis_size):
    steps, rows, columns = partial.shape
    if axis_size < 4 or axis_size & (axis_size - 1):
        return reduce_scatter_rows(partial, axis_name, axis_size)
    half = axis_size // 2
    me = lax.axis_index(axis_name)
    chunks = partial.reshape(steps, axis_size, rows // axis_size, columns)
    narrow = chunks.astype(jnp.bfloat16)
    own = lax.dynamic_index_in_dim(chunks, me, axis=1, keepdims=False)
    mirror = lax.dynamic_index_in_dim(chunks, me ^ half, axis=1, keepdims=False)
    for offset in range(1, half):
        peer = me ^ offset
        outgoing = jnp.stack(
            [
                lax.dynamic_index_in_dim(narrow, peer, axis=1, keepdims=False),
                lax.dynamic_index_in_dim(narrow, peer ^ half, axis=1, keepdims=False),
            ]
        )
        incoming = lax.ppermute(
            outgoing, axis_name, [(i, i ^ offset) for i in range(axis_size)]
        ).astype(jnp.float32)
        own = own + incoming[0]
        mirror = mirror + incoming[1]
    across = lax.ppermute(
        mirror.astype(jnp.bfloat16), axis_name, [(i, i ^ half) for i in range(axis_size)]
    )
    return own + across.astype(jnp.float32)


def doubling_gather(value, axis_name, axis_size, axis):
    if axis_size & (axis_size - 1):
        return lax.all_gather(value, axis_name, axis=axis, tiled=True)
    me = lax.axis_index(axis_name)
    held = value
    distance = 1
    while distance < axis_size:
        other = lax.ppermute(held, axis_name, [(i, i ^ distance) for i in range(axis_size)])
        upper = (me // distance) % 2 == 1
        first = jnp.where(upper, other, held)
        second = jnp.where(upper, held, other)
        held = jnp.concatenate([first, second], axis=axis)
        distance *= 2
    return held


def split_half_gather(value, axis_name, axis_size):
    if axis_size < 4 or axis_size & (axis_size - 1):
        return lax.all_gather(value, axis_name, axis=1, tiled=True)
    half = axis_size // 2
    me = lax.axis_index(axis_name)
    mirror = lax.ppermute(value, axis_name, [(i, i ^ half) for i in range(axis_size)])
    pair = jnp.stack([value, mirror])
    slots = [None] * axis_size
    slots[0], slots[half] = value, mirror
    for offset in range(1, half):
        incoming = lax.ppermute(pair, axis_name, [(i, i ^ offset) for i in range(axis_size)])
        slots[offset], slots[offset + half] = incoming[0], incoming[1]
    stacked = jnp.stack(slots)
    order = jnp.arange(axis_size, dtype=jnp.int32) ^ me
    gathered = jnp.take(stacked, order, axis=0)
    steps, rows, columns = value.shape
    return gathered.transpose(1, 0, 2, 3).reshape(steps, axis_size * rows, columns)


def tree_sum(value, axes):
    for axis_name in axes:
        size = lax.axis_size(axis_name)
        if size & (size - 1):
            value = lax.psum(value, axis_name)
            continue
        distance = 1
        while distance < size:
            pairs = [(i, i ^ distance) for i in range(size)]
            value = value + lax.ppermute(value, axis_name, pairs)
            distance *= 2
    return value


def sum_then_spread(value, sum_axes, spread_axes):
    return tree_sum(tree_sum(value, sum_axes).astype(jnp.bfloat16), spread_axes)


def halving_scatter(partial, axis_name, axis_size):
    steps, rows, columns = partial.shape
    if axis_size & (axis_size - 1):
        return lax.psum_scatter(partial, axis_name, scatter_dimension=1, tiled=True)
    me = lax.axis_index(axis_name)
    held = partial.reshape(steps, axis_size, rows // axis_size, columns)
    distance = 1
    while distance < axis_size:
        count = held.shape[1]
        pairs = held.reshape(steps, count // 2, 2, rows // axis_size, columns)
        mine = (me // distance) % 2
        keep = lax.dynamic_index_in_dim(pairs, mine, axis=2, keepdims=False)
        give = lax.dynamic_index_in_dim(pairs, 1 - mine, axis=2, keepdims=False)
        swap = [(i, i ^ distance) for i in range(axis_size)]
        if distance > 1:
            give = give.astype(jnp.bfloat16)
        held = keep + lax.ppermute(give, axis_name, swap).astype(jnp.float32)
        distance *= 2
    return held.reshape(steps, rows // axis_size, columns)


def attend(query_rows, previous_keys, previous_values, incoming_keys, incoming_values, lengths):
    steps, count_of_rows = query_rows.shape[0], query_rows.shape[1]
    groups = QUERY_HEADS // KEY_VALUE_HEADS
    context_window = previous_keys.shape[1]
    grouped_heads = query_rows.reshape(
        steps, count_of_rows, KEY_VALUE_HEADS, groups, HEAD_FEATURES
    ).transpose(1, 2, 0, 3, 4).reshape(count_of_rows, KEY_VALUE_HEADS, steps * groups, HEAD_FEATURES)
    keys_previous = previous_keys.reshape(
        count_of_rows, context_window, KEY_VALUE_HEADS, HEAD_FEATURES
    )
    values_previous = previous_values.reshape(
        count_of_rows, context_window, KEY_VALUE_HEADS, HEAD_FEATURES
    )
    keys_incoming = incoming_keys.reshape(
        steps, count_of_rows, KEY_VALUE_HEADS, HEAD_FEATURES
    ).transpose(1, 0, 2, 3)
    values_incoming = incoming_values.reshape(
        steps, count_of_rows, KEY_VALUE_HEADS, HEAD_FEATURES
    ).transpose(1, 0, 2, 3)
    factor = HEAD_FEATURES ** (-0.5)
    score_old = (
        jnp.einsum(
            "rhqd,rchd->rhqc", grouped_heads, keys_previous, preferred_element_type=jnp.float32
        )
        * factor
    )
    score_new = (
        jnp.einsum(
            "rhqd,rshd->rhqs", grouped_heads, keys_incoming, preferred_element_type=jnp.float32
        )
        * factor
    )
    live_old = (jnp.arange(context_window, dtype=jnp.int32)[None, :] < lengths[:, None])[
        :, None, None, :
    ]
    query_step = jnp.arange(steps * groups, dtype=jnp.int32) // groups
    live_new = (jnp.arange(steps, dtype=jnp.int32)[None, :] <= query_step[:, None])[
        None, None, :, :
    ]
    score_old = jnp.where(live_old, score_old, -1e30)
    score_new = jnp.where(live_new, score_new, -1e30)
    peak_score = jnp.maximum(jnp.max(score_old, axis=-1), jnp.max(score_new, axis=-1))
    weight_old = jnp.where(live_old, jnp.exp(score_old - peak_score[..., None]), 0.0)
    weight_new = jnp.where(live_new, jnp.exp(score_new - peak_score[..., None]), 0.0)
    weight_sum = jnp.sum(weight_old, axis=-1) + jnp.sum(weight_new, axis=-1)
    mixed_out = jnp.einsum(
        "rhqc,rchd->rhqd",
        weight_old.astype(jnp.bfloat16),
        values_previous,
        preferred_element_type=jnp.float32,
    )
    mixed_out = mixed_out + jnp.einsum(
        "rhqs,rshd->rhqd",
        weight_new.astype(jnp.bfloat16),
        values_incoming,
        preferred_element_type=jnp.float32,
    )
    mixed_out = (mixed_out / weight_sum[..., None]).astype(jnp.bfloat16)
    return mixed_out.reshape(
        count_of_rows, KEY_VALUE_HEADS, steps, groups, HEAD_FEATURES
    ).transpose(2, 0, 1, 3, 4).reshape(steps, count_of_rows, -1)


def local(
    inputs,
    norm_gain,
    query_weight,
    key_weight,
    value_weight,
    output_weight,
    query_down,
    query_up,
    output_down,
    output_up,
    block_adapter,
    cache_lengths,
    cache_keys,
    cache_values,
):
    across_first = lax.axis_size("gx")
    across_second = lax.axis_size("gy")
    index_first = lax.axis_index("gx")
    index_second = lax.axis_index("gy")
    steps = inputs.shape[0]
    request_count = inputs.shape[1] * across_second
    width = inputs.shape[2] * across_first
    local_rows = cache_keys.shape[0]
    block_count = block_adapter.shape[0]
    block_rows = request_count // block_count
    query_width = query_weight.shape[1]
    key_width = key_weight.shape[1]
    norm_scale = norm_gain.astype(jnp.float32)
    query_first = pick_adapters(query_down, block_adapter, index_second)
    query_second = pick_adapters(query_up, block_adapter, index_first)
    output_first = pick_adapters(output_down, block_adapter, index_first)
    output_second = pick_adapters(output_up, block_adapter, index_second)

    rows_all = doubling_gather(inputs, "gy", across_second, 1)
    rows_wide = rows_all.astype(jnp.float32)
    squares = tree_sum(jnp.sum(rows_wide * rows_wide, axis=2), ("gx",))
    factor_rows = lax.rsqrt(squares / width + EPS)
    normed = (rows_wide * factor_rows[..., None] * norm_scale).astype(jnp.bfloat16)

    blocked = normed.reshape(steps, block_count, block_rows, -1)
    rank_part = jnp.einsum(
        "tbnd,bdr->tbnr", blocked, query_first, preferred_element_type=jnp.float32
    )
    rank_query = sum_then_spread(rank_part, ("gx",), ("gy",))
    delta_query = jnp.einsum(
        "tbnr,bre->tbne", rank_query, query_second, preferred_element_type=jnp.float32
    ).reshape(steps, request_count, -1)
    query_main = lax.optimization_barrier(
        jnp.einsum("tnd,de->tne", normed, query_weight, preferred_element_type=jnp.float32)
    )
    part_query = query_main + delta_query
    part_key = jnp.einsum("tnd,de->tne", normed, key_weight, preferred_element_type=jnp.float32)
    part_value = jnp.einsum(
        "tnd,de->tne", normed, value_weight, preferred_element_type=jnp.float32
    )
    joined = jnp.concatenate([part_query, part_key, part_value], axis=-1)
    summed = split_half_scatter_steps(joined, "gx", across_first).astype(jnp.bfloat16)
    chunk_rows = summed.shape[1] // across_second
    spread = lax.all_to_all(
        summed.reshape(steps, across_second, chunk_rows, -1), "gy", 1, 2, tiled=False
    )
    query_full = spread[..., :query_width].reshape(steps, local_rows, -1)
    key_full = spread[..., query_width : query_width + key_width].reshape(steps, local_rows, -1)
    value_full = spread[..., query_width + key_width :].reshape(steps, local_rows, -1)

    token_positions = (
        cache_lengths[None, :] + jnp.arange(steps, dtype=jnp.int32)[:, None]
    ).reshape(-1)
    query_rot = rotary_embedding(
        query_full.astype(jnp.float32).reshape(steps * local_rows, QUERY_HEADS, HEAD_FEATURES),
        token_positions,
    ).astype(jnp.bfloat16)
    key_rot = rotary_embedding(
        key_full.astype(jnp.float32).reshape(steps * local_rows, KEY_VALUE_HEADS, HEAD_FEATURES),
        token_positions,
    ).astype(jnp.bfloat16)
    mixed_local = attend(
        query_rot.reshape(steps, local_rows, -1),
        cache_keys,
        cache_values,
        key_rot.reshape(steps, local_rows, -1),
        value_full,
        cache_lengths,
    )
    head_group = lax.all_to_all(
        mixed_local.reshape(steps, local_rows, across_second, -1), "gy", 2, 1, tiled=False
    ).reshape(steps, across_second * local_rows, -1)
    mixed_all = ring_gather(head_group, "gx", across_first)
    rank_part_out = jnp.einsum(
        "tbnq,bqr->tbnr",
        mixed_all.reshape(steps, block_count, block_rows, -1),
        output_first,
        preferred_element_type=jnp.float32,
    )
    rank_output = sum_then_spread(rank_part_out, ("gy",), ("gx",))
    delta_output = jnp.einsum(
        "tbnr,bre->tbne", rank_output, output_second, preferred_element_type=jnp.float32
    ).reshape(steps, request_count, -1)
    output_main = lax.optimization_barrier(
        jnp.einsum("tnq,qe->tne", mixed_all, output_weight, preferred_element_type=jnp.float32)
    )
    partial_out = output_main + delta_output
    return halving_scatter(partial_out, "gy", across_second).astype(jnp.bfloat16)


def solution(mesh):
    in_specs = (
        P(None, "gy", "gx"),
        P("gx"),
        P("gx", "gy"),
        P("gx", "gy"),
        P("gx", "gy"),
        P("gy", "gx"),
        P("gy", "gx", None),
        P("gx", None, "gy"),
        P("gx", "gy", None),
        P("gy", None, "gx"),
        P(),
        P(("gx", "gy")),
        P(("gx", "gy"), None, None),
        P(("gx", "gy"), None, None),
    )
    out_specs = P(None, "gy", "gx")
    return jax.shard_map(local, mesh=mesh, in_specs=in_specs, out_specs=out_specs, check_vma=False)
```

```python
import jax
import jax.numpy as jnp
from jax import lax
from jax.sharding import PartitionSpec as P

QUERY_HEADS = 64
KEY_VALUE_HEADS = 8
HEAD_FEATURES = 128
BLOCK = 128


EPS = 1e-05
THETA = 500000.0


def rotary_embedding(values_in, token_positions):
    half_size = values_in.shape[-1] // 2
    exponent = jnp.arange(half_size, dtype=jnp.float32) * 2.0 / values_in.shape[-1]
    frequency = THETA ** (-exponent)
    angles = token_positions.astype(jnp.float32)[:, None] * frequency[None, :]
    cosine = jnp.cos(angles)[:, None, :]
    sine_part = jnp.sin(angles)[:, None, :]
    lower = values_in[..., :half_size]
    upper = values_in[..., half_size:]
    return jnp.concatenate(
        [lower * cosine - upper * sine_part, upper * cosine + lower * sine_part], axis=-1
    )


def pick_adapters(table, adapter_ids, owner_index):
    table_count = table.shape[0]
    picked = []
    for block in range(adapter_ids.shape[0]):
        wanted = adapter_ids[block]
        owned = (wanted // table_count) == owner_index
        entry = lax.dynamic_index_in_dim(table, wanted % table_count, axis=0, keepdims=False)
        picked.append(jnp.where(owned, entry, jnp.zeros_like(entry)))
    return jnp.stack(picked)


def reduce_scatter_rows(partial, axis_name, axis_size):
    steps, rows, columns = partial.shape
    pieces = partial.astype(jnp.bfloat16).reshape(steps, axis_size, rows // axis_size, columns)
    received = lax.all_to_all(pieces, axis_name, 1, 1, tiled=False)
    return jnp.sum(received.astype(jnp.float32), axis=1)


def split_half_scatter_steps(partial, axis_name, axis_size):
    return jnp.concatenate(
        [
            split_half_scatter(partial[step : step + 1], axis_name, axis_size)
            for step in range(partial.shape[0])
        ]
    )


def split_half_gather_steps(value, axis_name, axis_size):
    return jnp.concatenate(
        [
            split_half_gather(value[step : step + 1], axis_name, axis_size)
            for step in range(value.shape[0])
        ]
    )


def ring_gather(value, axis_name, axis_size):
    if axis_size < 4 or axis_size % 2:
        return lax.all_gather(value, axis_name, axis=1, tiled=True)
    ring = list(range(0, axis_size, 2)) + list(range(axis_size - 1, 0, -2))
    place = [0] * axis_size
    for position, index in enumerate(ring):
        place[index] = position
    ahead = [(ring[p], ring[(p + 1) % axis_size]) for p in range(axis_size)]
    behind = [(ring[p], ring[(p - 1) % axis_size]) for p in range(axis_size)]
    slots = [None] * axis_size
    slots[0] = value
    forward = backward = value
    for hop in range(1, axis_size // 2 + 1):
        forward = lax.ppermute(forward, axis_name, ahead)
        slots[(-hop) % axis_size] = forward
        if hop < axis_size - hop:
            backward = lax.ppermute(backward, axis_name, behind)
            slots[hop] = backward
    stacked = jnp.stack(slots)
    places = jnp.asarray(place, dtype=jnp.int32)
    me = lax.axis_index(axis_name)
    order = (places - places[me]) % axis_size
    gathered = jnp.take(stacked, order, axis=0)
    steps, rows, columns = value.shape
    return gathered.transpose(1, 0, 2, 3).reshape(steps, axis_size * rows, columns)


def split_half_scatter(partial, axis_name, axis_size):
    steps, rows, columns = partial.shape
    if axis_size < 4 or axis_size & (axis_size - 1):
        return reduce_scatter_rows(partial, axis_name, axis_size)
    half = axis_size // 2
    me = lax.axis_index(axis_name)
    chunks = partial.reshape(steps, axis_size, rows // axis_size, columns)
    narrow = chunks.astype(jnp.bfloat16)
    own = lax.dynamic_index_in_dim(chunks, me, axis=1, keepdims=False)
    mirror = lax.dynamic_index_in_dim(chunks, me ^ half, axis=1, keepdims=False)
    for offset in range(1, half):
        peer = me ^ offset
        outgoing = jnp.stack(
            [
                lax.dynamic_index_in_dim(narrow, peer, axis=1, keepdims=False),
                lax.dynamic_index_in_dim(narrow, peer ^ half, axis=1, keepdims=False),
            ]
        )
        incoming = lax.ppermute(
            outgoing, axis_name, [(i, i ^ offset) for i in range(axis_size)]
        ).astype(jnp.float32)
        own = own + incoming[0]
        mirror = mirror + incoming[1]
    across = lax.ppermute(
        mirror.astype(jnp.bfloat16), axis_name, [(i, i ^ half) for i in range(axis_size)]
    )
    return own + across.astype(jnp.float32)


def doubling_gather(value, axis_name, axis_size, axis):
    if axis_size & (axis_size - 1):
        return lax.all_gather(value, axis_name, axis=axis, tiled=True)
    me = lax.axis_index(axis_name)
    held = value
    distance = 1
    while distance < axis_size:
        other = lax.ppermute(held, axis_name, [(i, i ^ distance) for i in range(axis_size)])
        upper = (me // distance) % 2 == 1
        first = jnp.where(upper, other, held)
        second = jnp.where(upper, held, other)
        held = jnp.concatenate([first, second], axis=axis)
        distance *= 2
    return held


def split_half_gather(value, axis_name, axis_size):
    if axis_size < 4 or axis_size & (axis_size - 1):
        return lax.all_gather(value, axis_name, axis=1, tiled=True)
    half = axis_size // 2
    me = lax.axis_index(axis_name)
    mirror = lax.ppermute(value, axis_name, [(i, i ^ half) for i in range(axis_size)])
    pair = jnp.stack([value, mirror])
    slots = [None] * axis_size
    slots[0], slots[half] = value, mirror
    for offset in range(1, half):
        incoming = lax.ppermute(pair, axis_name, [(i, i ^ offset) for i in range(axis_size)])
        slots[offset], slots[offset + half] = incoming[0], incoming[1]
    stacked = jnp.stack(slots)
    order = jnp.arange(axis_size, dtype=jnp.int32) ^ me
    gathered = jnp.take(stacked, order, axis=0)
    steps, rows, columns = value.shape
    return gathered.transpose(1, 0, 2, 3).reshape(steps, axis_size * rows, columns)


def tree_sum(value, axes):
    for axis_name in axes:
        size = lax.axis_size(axis_name)
        if size & (size - 1):
            value = lax.psum(value, axis_name)
            continue
        distance = 1
        while distance < size:
            pairs = [(i, i ^ distance) for i in range(size)]
            value = value + lax.ppermute(value, axis_name, pairs)
            distance *= 2
    return value


def sum_then_spread(value, sum_axes, spread_axes):
    return tree_sum(tree_sum(value, sum_axes).astype(jnp.bfloat16), spread_axes)


def halving_scatter(partial, axis_name, axis_size):
    steps, rows, columns = partial.shape
    if axis_size & (axis_size - 1):
        return lax.psum_scatter(partial, axis_name, scatter_dimension=1, tiled=True)
    me = lax.axis_index(axis_name)
    held = partial.reshape(steps, axis_size, rows // axis_size, columns)
    distance = 1
    while distance < axis_size:
        count = held.shape[1]
        pairs = held.reshape(steps, count // 2, 2, rows // axis_size, columns)
        mine = (me // distance) % 2
        keep = lax.dynamic_index_in_dim(pairs, mine, axis=2, keepdims=False)
        give = lax.dynamic_index_in_dim(pairs, 1 - mine, axis=2, keepdims=False)
        swap = [(i, i ^ distance) for i in range(axis_size)]
        if distance > 1:
            give = give.astype(jnp.bfloat16)
        held = keep + lax.ppermute(give, axis_name, swap).astype(jnp.float32)
        distance *= 2
    return held.reshape(steps, rows // axis_size, columns)


def attend(query_rows, previous_keys, previous_values, incoming_keys, incoming_values, lengths):
    steps, count_of_rows = query_rows.shape[0], query_rows.shape[1]
    groups = QUERY_HEADS // KEY_VALUE_HEADS
    context_window = previous_keys.shape[1]
    grouped_heads = query_rows.reshape(
        steps, count_of_rows, KEY_VALUE_HEADS, groups, HEAD_FEATURES
    ).transpose(1, 2, 0, 3, 4).reshape(count_of_rows, KEY_VALUE_HEADS, steps * groups, HEAD_FEATURES)
    keys_previous = previous_keys.reshape(
        count_of_rows, context_window, KEY_VALUE_HEADS, HEAD_FEATURES
    )
    values_previous = previous_values.reshape(
        count_of_rows, context_window, KEY_VALUE_HEADS, HEAD_FEATURES
    )
    keys_incoming = incoming_keys.reshape(
        steps, count_of_rows, KEY_VALUE_HEADS, HEAD_FEATURES
    ).transpose(1, 0, 2, 3)
    values_incoming = incoming_values.reshape(
        steps, count_of_rows, KEY_VALUE_HEADS, HEAD_FEATURES
    ).transpose(1, 0, 2, 3)
    factor = HEAD_FEATURES ** (-0.5)
    score_old = (
        jnp.einsum(
            "rhqd,rchd->rhqc", grouped_heads, keys_previous, preferred_element_type=jnp.float32
        )
        * factor
    )
    score_new = (
        jnp.einsum(
            "rhqd,rshd->rhqs", grouped_heads, keys_incoming, preferred_element_type=jnp.float32
        )
        * factor
    )
    live_old = (jnp.arange(context_window, dtype=jnp.int32)[None, :] < lengths[:, None])[
        :, None, None, :
    ]
    query_step = jnp.arange(steps * groups, dtype=jnp.int32) // groups
    live_new = (jnp.arange(steps, dtype=jnp.int32)[None, :] <= query_step[:, None])[
        None, None, :, :
    ]
    score_old = jnp.where(live_old, score_old, -1e30)
    score_new = jnp.where(live_new, score_new, -1e30)
    peak_score = jnp.maximum(jnp.max(score_old, axis=-1), jnp.max(score_new, axis=-1))
    weight_old = jnp.where(live_old, jnp.exp(score_old - peak_score[..., None]), 0.0)
    weight_new = jnp.where(live_new, jnp.exp(score_new - peak_score[..., None]), 0.0)
    weight_sum = jnp.sum(weight_old, axis=-1) + jnp.sum(weight_new, axis=-1)
    mixed_out = jnp.einsum(
        "rhqc,rchd->rhqd",
        weight_old.astype(jnp.bfloat16),
        values_previous,
        preferred_element_type=jnp.float32,
    )
    mixed_out = mixed_out + jnp.einsum(
        "rhqs,rshd->rhqd",
        weight_new.astype(jnp.bfloat16),
        values_incoming,
        preferred_element_type=jnp.float32,
    )
    mixed_out = (mixed_out / weight_sum[..., None]).astype(jnp.bfloat16)
    return mixed_out.reshape(
        count_of_rows, KEY_VALUE_HEADS, steps, groups, HEAD_FEATURES
    ).transpose(2, 0, 1, 3, 4).reshape(steps, count_of_rows, -1)


def local(
    inputs,
    norm_gain,
    query_weight,
    key_weight,
    value_weight,
    output_weight,
    query_down,
    query_up,
    output_down,
    output_up,
    block_adapter,
    cache_lengths,
    cache_keys,
    cache_values,
):
    across_first = lax.axis_size("gx")
    across_second = lax.axis_size("gy")
    index_first = lax.axis_index("gx")
    index_second = lax.axis_index("gy")
    steps = inputs.shape[0]
    request_count = inputs.shape[1] * across_second
    width = inputs.shape[2] * across_first
    local_rows = cache_keys.shape[0]
    block_count = block_adapter.shape[0]
    block_rows = request_count // block_count
    query_width = query_weight.shape[1]
    key_width = key_weight.shape[1]
    norm_scale = norm_gain.astype(jnp.float32)
    query_first = pick_adapters(query_down, block_adapter, index_second)
    query_second = pick_adapters(query_up, block_adapter, index_first)
    output_first = pick_adapters(output_down, block_adapter, index_first)
    output_second = pick_adapters(output_up, block_adapter, index_second)

    rows_all = doubling_gather(inputs, "gy", across_second, 1)
    rows_wide = rows_all.astype(jnp.float32)
    squares = tree_sum(jnp.sum(rows_wide * rows_wide, axis=2), ("gx",))
    factor_rows = lax.rsqrt(squares / width + EPS)
    normed = (rows_wide * factor_rows[..., None] * norm_scale).astype(jnp.bfloat16)

    blocked = normed.reshape(steps, block_count, block_rows, -1)
    rank_part = jnp.einsum(
        "tbnd,bdr->tbnr", blocked, query_first, preferred_element_type=jnp.float32
    )
    rank_query = sum_then_spread(rank_part, ("gx",), ("gy",))
    delta_query = jnp.einsum(
        "tbnr,bre->tbne", rank_query, query_second, preferred_element_type=jnp.float32
    ).reshape(steps, request_count, -1)
    query_main = lax.optimization_barrier(
        jnp.einsum("tnd,de->tne", normed, query_weight, preferred_element_type=jnp.float32)
    )
    part_query = query_main + delta_query
    part_key = jnp.einsum("tnd,de->tne", normed, key_weight, preferred_element_type=jnp.float32)
    part_value = jnp.einsum(
        "tnd,de->tne", normed, value_weight, preferred_element_type=jnp.float32
    )
    joined = jnp.concatenate([part_query, part_key, part_value], axis=-1)
    summed = split_half_scatter_steps(joined, "gx", across_first).astype(jnp.bfloat16)
    chunk_rows = summed.shape[1] // across_second
    spread = lax.all_to_all(
        summed.reshape(steps, across_second, chunk_rows, -1), "gy", 1, 2, tiled=False
    )
    query_full = spread[..., :query_width].reshape(steps, local_rows, -1)
    key_full = spread[..., query_width : query_width + key_width].reshape(steps, local_rows, -1)
    value_full = spread[..., query_width + key_width :].reshape(steps, local_rows, -1)

    token_positions = (
        cache_lengths[None, :] + jnp.arange(steps, dtype=jnp.int32)[:, None]
    ).reshape(-1)
    query_rot = rotary_embedding(
        query_full.astype(jnp.float32).reshape(steps * local_rows, QUERY_HEADS, HEAD_FEATURES),
        token_positions,
    ).astype(jnp.bfloat16)
    key_rot = rotary_embedding(
        key_full.astype(jnp.float32).reshape(steps * local_rows, KEY_VALUE_HEADS, HEAD_FEATURES),
        token_positions,
    ).astype(jnp.bfloat16)
    mixed_local = attend(
        query_rot.reshape(steps, local_rows, -1),
        cache_keys,
        cache_values,
        key_rot.reshape(steps, local_rows, -1),
        value_full,
        cache_lengths,
    )
    head_group = lax.all_to_all(
        mixed_local.reshape(steps, local_rows, across_second, -1), "gy", 2, 1, tiled=False
    ).reshape(steps, across_second * local_rows, -1)
    mixed_all = ring_gather(head_group, "gx", across_first)
    rank_part_out = jnp.einsum(
        "tbnq,bqr->tbnr",
        mixed_all.reshape(steps, block_count, block_rows, -1),
        output_first,
        preferred_element_type=jnp.float32,
    )
    rank_output = sum_then_spread(rank_part_out, ("gy",), ("gx",))
    delta_output = jnp.einsum(
        "tbnr,bre->tbne", rank_output, output_second, preferred_element_type=jnp.float32
    ).reshape(steps, request_count, -1)
    output_main = lax.optimization_barrier(
        jnp.einsum("tnq,qe->tne", mixed_all, output_weight, preferred_element_type=jnp.float32)
    )
    partial_out = output_main + delta_output
    return jnp.concatenate(
        [
            halving_scatter(partial_out[step : step + 1], "gy", across_second)
            for step in range(steps)
        ]
    ).astype(jnp.bfloat16)


def solution(mesh):
    in_specs = (
        P(None, "gy", "gx"),
        P("gx"),
        P("gx", "gy"),
        P("gx", "gy"),
        P("gx", "gy"),
        P("gy", "gx"),
        P("gy", "gx", None),
        P("gx", None, "gy"),
        P("gx", "gy", None),
        P("gy", None, "gx"),
        P(),
        P(("gx", "gy")),
        P(("gx", "gy"), None, None),
        P(("gx", "gy"), None, None),
    )
    out_specs = P(None, "gy", "gx")
    return jax.shard_map(local, mesh=mesh, in_specs=in_specs, out_specs=out_specs, check_vma=False)
```

```python
import jax
import jax.numpy as jnp
from jax import lax
from jax.sharding import PartitionSpec as P

QUERY_HEADS = 64
KEY_VALUE_HEADS = 8
HEAD_FEATURES = 128
BLOCK = 128


EPS = 1e-05
THETA = 500000.0


def rotary_embedding(values_in, token_positions):
    half_size = values_in.shape[-1] // 2
    exponent = jnp.arange(half_size, dtype=jnp.float32) * 2.0 / values_in.shape[-1]
    frequency = THETA ** (-exponent)
    angles = token_positions.astype(jnp.float32)[:, None] * frequency[None, :]
    cosine = jnp.cos(angles)[:, None, :]
    sine_part = jnp.sin(angles)[:, None, :]
    lower = values_in[..., :half_size]
    upper = values_in[..., half_size:]
    return jnp.concatenate(
        [lower * cosine - upper * sine_part, upper * cosine + lower * sine_part], axis=-1
    )


def pick_adapters(table, adapter_ids, owner_index):
    table_count = table.shape[0]
    picked = []
    for block in range(adapter_ids.shape[0]):
        wanted = adapter_ids[block]
        owned = (wanted // table_count) == owner_index
        entry = lax.dynamic_index_in_dim(table, wanted % table_count, axis=0, keepdims=False)
        picked.append(jnp.where(owned, entry, jnp.zeros_like(entry)))
    return jnp.stack(picked)


def reduce_scatter_rows(partial, axis_name, axis_size):
    steps, rows, columns = partial.shape
    pieces = partial.astype(jnp.bfloat16).reshape(steps, axis_size, rows // axis_size, columns)
    received = lax.all_to_all(pieces, axis_name, 1, 1, tiled=False)
    return jnp.sum(received.astype(jnp.float32), axis=1)


def split_half_scatter_steps(partial, axis_name, axis_size):
    return jnp.concatenate(
        [
            split_half_scatter(partial[step : step + 1], axis_name, axis_size)
            for step in range(partial.shape[0])
        ]
    )


def split_half_gather_steps(value, axis_name, axis_size):
    return jnp.concatenate(
        [
            split_half_gather(value[step : step + 1], axis_name, axis_size)
            for step in range(value.shape[0])
        ]
    )


def ring_gather(value, axis_name, axis_size):
    if axis_size < 4 or axis_size % 2:
        return lax.all_gather(value, axis_name, axis=1, tiled=True)
    ring = list(range(0, axis_size, 2)) + list(range(axis_size - 1, 0, -2))
    place = [0] * axis_size
    for position, index in enumerate(ring):
        place[index] = position
    ahead = [(ring[p], ring[(p + 1) % axis_size]) for p in range(axis_size)]
    behind = [(ring[p], ring[(p - 1) % axis_size]) for p in range(axis_size)]
    slots = [None] * axis_size
    slots[0] = value
    forward = backward = value
    for hop in range(1, axis_size // 2 + 1):
        forward = lax.ppermute(forward, axis_name, ahead)
        slots[(-hop) % axis_size] = forward
        if hop < axis_size - hop:
            backward = lax.ppermute(backward, axis_name, behind)
            slots[hop] = backward
    stacked = jnp.stack(slots)
    places = jnp.asarray(place, dtype=jnp.int32)
    me = lax.axis_index(axis_name)
    order = (places - places[me]) % axis_size
    gathered = jnp.take(stacked, order, axis=0)
    steps, rows, columns = value.shape
    return gathered.transpose(1, 0, 2, 3).reshape(steps, axis_size * rows, columns)


def split_half_scatter(partial, axis_name, axis_size):
    steps, rows, columns = partial.shape
    if axis_size < 4 or axis_size & (axis_size - 1):
        return reduce_scatter_rows(partial, axis_name, axis_size)
    half = axis_size // 2
    me = lax.axis_index(axis_name)
    chunks = partial.reshape(steps, axis_size, rows // axis_size, columns)
    narrow = chunks.astype(jnp.bfloat16)
    own = lax.dynamic_index_in_dim(chunks, me, axis=1, keepdims=False)
    mirror = lax.dynamic_index_in_dim(chunks, me ^ half, axis=1, keepdims=False)
    for offset in range(1, half):
        peer = me ^ offset
        outgoing = jnp.stack(
            [
                lax.dynamic_index_in_dim(narrow, peer, axis=1, keepdims=False),
                lax.dynamic_index_in_dim(narrow, peer ^ half, axis=1, keepdims=False),
            ]
        )
        incoming = lax.ppermute(
            outgoing, axis_name, [(i, i ^ offset) for i in range(axis_size)]
        ).astype(jnp.float32)
        own = own + incoming[0]
        mirror = mirror + incoming[1]
    across = lax.ppermute(
        mirror.astype(jnp.bfloat16), axis_name, [(i, i ^ half) for i in range(axis_size)]
    )
    return own + across.astype(jnp.float32)


def doubling_gather(value, axis_name, axis_size, axis):
    if axis_size & (axis_size - 1):
        return lax.all_gather(value, axis_name, axis=axis, tiled=True)
    me = lax.axis_index(axis_name)
    held = value
    distance = 1
    while distance < axis_size:
        other = lax.ppermute(held, axis_name, [(i, i ^ distance) for i in range(axis_size)])
        upper = (me // distance) % 2 == 1
        first = jnp.where(upper, other, held)
        second = jnp.where(upper, held, other)
        held = jnp.concatenate([first, second], axis=axis)
        distance *= 2
    return held


def split_half_gather(value, axis_name, axis_size):
    if axis_size < 4 or axis_size & (axis_size - 1):
        return lax.all_gather(value, axis_name, axis=1, tiled=True)
    half = axis_size // 2
    me = lax.axis_index(axis_name)
    mirror = lax.ppermute(value, axis_name, [(i, i ^ half) for i in range(axis_size)])
    pair = jnp.stack([value, mirror])
    slots = [None] * axis_size
    slots[0], slots[half] = value, mirror
    for offset in range(1, half):
        incoming = lax.ppermute(pair, axis_name, [(i, i ^ offset) for i in range(axis_size)])
        slots[offset], slots[offset + half] = incoming[0], incoming[1]
    stacked = jnp.stack(slots)
    order = jnp.arange(axis_size, dtype=jnp.int32) ^ me
    gathered = jnp.take(stacked, order, axis=0)
    steps, rows, columns = value.shape
    return gathered.transpose(1, 0, 2, 3).reshape(steps, axis_size * rows, columns)


def tree_sum(value, axes):
    for axis_name in axes:
        size = lax.axis_size(axis_name)
        if size & (size - 1):
            value = lax.psum(value, axis_name)
            continue
        distance = 1
        while distance < size:
            pairs = [(i, i ^ distance) for i in range(size)]
            value = value + lax.ppermute(value, axis_name, pairs)
            distance *= 2
    return value


def sum_then_spread(value, sum_axes, spread_axes):
    return tree_sum(tree_sum(value, sum_axes).astype(jnp.bfloat16), spread_axes)


def halving_scatter(partial, axis_name, axis_size):
    steps, rows, columns = partial.shape
    if axis_size & (axis_size - 1):
        return lax.psum_scatter(partial, axis_name, scatter_dimension=1, tiled=True)
    me = lax.axis_index(axis_name)
    held = partial.reshape(steps, axis_size, rows // axis_size, columns)
    distance = 1
    while distance < axis_size:
        count = held.shape[1]
        pairs = held.reshape(steps, count // 2, 2, rows // axis_size, columns)
        mine = (me // distance) % 2
        keep = lax.dynamic_index_in_dim(pairs, mine, axis=2, keepdims=False)
        give = lax.dynamic_index_in_dim(pairs, 1 - mine, axis=2, keepdims=False)
        swap = [(i, i ^ distance) for i in range(axis_size)]
        if distance > 1:
            give = give.astype(jnp.bfloat16)
        held = keep + lax.ppermute(give, axis_name, swap).astype(jnp.float32)
        distance *= 2
    return held.reshape(steps, rows // axis_size, columns)


def attend(query_rows, previous_keys, previous_values, incoming_keys, incoming_values, lengths):
    steps, count_of_rows = query_rows.shape[0], query_rows.shape[1]
    groups = QUERY_HEADS // KEY_VALUE_HEADS
    context_window = previous_keys.shape[1]
    grouped_heads = query_rows.reshape(
        steps, count_of_rows, KEY_VALUE_HEADS, groups, HEAD_FEATURES
    ).transpose(1, 2, 0, 3, 4).reshape(count_of_rows, KEY_VALUE_HEADS, steps * groups, HEAD_FEATURES)
    keys_previous = previous_keys.reshape(
        count_of_rows, context_window, KEY_VALUE_HEADS, HEAD_FEATURES
    )
    values_previous = previous_values.reshape(
        count_of_rows, context_window, KEY_VALUE_HEADS, HEAD_FEATURES
    )
    keys_incoming = incoming_keys.reshape(
        steps, count_of_rows, KEY_VALUE_HEADS, HEAD_FEATURES
    ).transpose(1, 0, 2, 3)
    values_incoming = incoming_values.reshape(
        steps, count_of_rows, KEY_VALUE_HEADS, HEAD_FEATURES
    ).transpose(1, 0, 2, 3)
    factor = HEAD_FEATURES ** (-0.5)
    score_old = (
        jnp.einsum(
            "rhqd,rchd->rhqc", grouped_heads, keys_previous, preferred_element_type=jnp.float32
        )
        * factor
    )
    score_new = (
        jnp.einsum(
            "rhqd,rshd->rhqs", grouped_heads, keys_incoming, preferred_element_type=jnp.float32
        )
        * factor
    )
    live_old = (jnp.arange(context_window, dtype=jnp.int32)[None, :] < lengths[:, None])[
        :, None, None, :
    ]
    query_step = jnp.arange(steps * groups, dtype=jnp.int32) // groups
    live_new = (jnp.arange(steps, dtype=jnp.int32)[None, :] <= query_step[:, None])[
        None, None, :, :
    ]
    score_old = jnp.where(live_old, score_old, -1e30)
    score_new = jnp.where(live_new, score_new, -1e30)
    peak_score = jnp.maximum(jnp.max(score_old, axis=-1), jnp.max(score_new, axis=-1))
    weight_old = jnp.where(live_old, jnp.exp(score_old - peak_score[..., None]), 0.0)
    weight_new = jnp.where(live_new, jnp.exp(score_new - peak_score[..., None]), 0.0)
    weight_sum = jnp.sum(weight_old, axis=-1) + jnp.sum(weight_new, axis=-1)
    mixed_out = jnp.einsum(
        "rhqc,rchd->rhqd",
        weight_old.astype(jnp.bfloat16),
        values_previous,
        preferred_element_type=jnp.float32,
    )
    mixed_out = mixed_out + jnp.einsum(
        "rhqs,rshd->rhqd",
        weight_new.astype(jnp.bfloat16),
        values_incoming,
        preferred_element_type=jnp.float32,
    )
    mixed_out = (mixed_out / weight_sum[..., None]).astype(jnp.bfloat16)
    return mixed_out.reshape(
        count_of_rows, KEY_VALUE_HEADS, steps, groups, HEAD_FEATURES
    ).transpose(2, 0, 1, 3, 4).reshape(steps, count_of_rows, -1)


def local(
    inputs,
    norm_gain,
    query_weight,
    key_weight,
    value_weight,
    output_weight,
    query_down,
    query_up,
    output_down,
    output_up,
    block_adapter,
    cache_lengths,
    cache_keys,
    cache_values,
):
    across_first = lax.axis_size("gx")
    across_second = lax.axis_size("gy")
    index_first = lax.axis_index("gx")
    index_second = lax.axis_index("gy")
    steps = inputs.shape[0]
    request_count = inputs.shape[1] * across_second
    width = inputs.shape[2] * across_first
    local_rows = cache_keys.shape[0]
    block_count = block_adapter.shape[0]
    block_rows = request_count // block_count
    query_width = query_weight.shape[1]
    key_width = key_weight.shape[1]
    norm_scale = norm_gain.astype(jnp.float32)
    query_first = pick_adapters(query_down, block_adapter, index_second)
    query_second = pick_adapters(query_up, block_adapter, index_first)
    output_first = pick_adapters(output_down, block_adapter, index_first)
    output_second = pick_adapters(output_up, block_adapter, index_second)

    rows_all = doubling_gather(inputs, "gy", across_second, 1)
    rows_wide = rows_all.astype(jnp.float32)
    squares = tree_sum(jnp.sum(rows_wide * rows_wide, axis=2), ("gx",))
    factor_rows = lax.rsqrt(squares / width + EPS)
    normed = (rows_wide * factor_rows[..., None] * norm_scale).astype(jnp.bfloat16)

    blocked = normed.reshape(steps, block_count, block_rows, -1)
    rank_part = jnp.einsum(
        "tbnd,bdr->tbnr", blocked, query_first, preferred_element_type=jnp.float32
    )
    rank_query = sum_then_spread(rank_part, ("gx",), ("gy",))
    delta_query = jnp.einsum(
        "tbnr,bre->tbne", rank_query, query_second, preferred_element_type=jnp.float32
    ).reshape(steps, request_count, -1)
    query_main = lax.optimization_barrier(
        jnp.einsum("tnd,de->tne", normed, query_weight, preferred_element_type=jnp.float32)
    )
    part_query = query_main + delta_query
    part_key = jnp.einsum("tnd,de->tne", normed, key_weight, preferred_element_type=jnp.float32)
    part_value = jnp.einsum(
        "tnd,de->tne", normed, value_weight, preferred_element_type=jnp.float32
    )
    summed_kv = split_half_scatter_steps(
        jnp.concatenate([part_key, part_value], axis=-1), "gx", across_first
    )
    summed_q = split_half_scatter_steps(part_query, "gx", across_first)
    summed = jnp.concatenate([summed_q, summed_kv], axis=-1).astype(jnp.bfloat16)
    chunk_rows = summed.shape[1] // across_second
    spread = lax.all_to_all(
        summed.reshape(steps, across_second, chunk_rows, -1), "gy", 1, 2, tiled=False
    )
    query_full = spread[..., :query_width].reshape(steps, local_rows, -1)
    key_full = spread[..., query_width : query_width + key_width].reshape(steps, local_rows, -1)
    value_full = spread[..., query_width + key_width :].reshape(steps, local_rows, -1)

    token_positions = (
        cache_lengths[None, :] + jnp.arange(steps, dtype=jnp.int32)[:, None]
    ).reshape(-1)
    query_rot = rotary_embedding(
        query_full.astype(jnp.float32).reshape(steps * local_rows, QUERY_HEADS, HEAD_FEATURES),
        token_positions,
    ).astype(jnp.bfloat16)
    key_rot = rotary_embedding(
        key_full.astype(jnp.float32).reshape(steps * local_rows, KEY_VALUE_HEADS, HEAD_FEATURES),
        token_positions,
    ).astype(jnp.bfloat16)
    mixed_local = attend(
        query_rot.reshape(steps, local_rows, -1),
        cache_keys,
        cache_values,
        key_rot.reshape(steps, local_rows, -1),
        value_full,
        cache_lengths,
    )
    head_group = lax.all_to_all(
        mixed_local.reshape(steps, local_rows, across_second, -1), "gy", 2, 1, tiled=False
    ).reshape(steps, across_second * local_rows, -1)
    mixed_all = ring_gather(head_group, "gx", across_first)
    rank_part_out = jnp.einsum(
        "tbnq,bqr->tbnr",
        mixed_all.reshape(steps, block_count, block_rows, -1),
        output_first,
        preferred_element_type=jnp.float32,
    )
    rank_output = sum_then_spread(rank_part_out, ("gy",), ("gx",))
    delta_output = jnp.einsum(
        "tbnr,bre->tbne", rank_output, output_second, preferred_element_type=jnp.float32
    ).reshape(steps, request_count, -1)
    output_main = lax.optimization_barrier(
        jnp.einsum("tnq,qe->tne", mixed_all, output_weight, preferred_element_type=jnp.float32)
    )
    partial_out = output_main + delta_output
    return jnp.concatenate(
        [
            halving_scatter(partial_out[step : step + 1], "gy", across_second)
            for step in range(steps)
        ]
    ).astype(jnp.bfloat16)


def solution(mesh):
    in_specs = (
        P(None, "gy", "gx"),
        P("gx"),
        P("gx", "gy"),
        P("gx", "gy"),
        P("gx", "gy"),
        P("gy", "gx"),
        P("gy", "gx", None),
        P("gx", None, "gy"),
        P("gx", "gy", None),
        P("gy", None, "gx"),
        P(),
        P(("gx", "gy")),
        P(("gx", "gy"), None, None),
        P(("gx", "gy"), None, None),
    )
    out_specs = P(None, "gy", "gx")
    return jax.shard_map(local, mesh=mesh, in_specs=in_specs, out_specs=out_specs, check_vma=False)
```

```python
import jax
import jax.numpy as jnp
from jax import lax
from jax.sharding import PartitionSpec as P

QUERY_HEADS = 64
KEY_VALUE_HEADS = 8
HEAD_FEATURES = 128
BLOCK = 128


EPS = 1e-05
THETA = 500000.0


def rotary_embedding(values_in, token_positions):
    half_size = values_in.shape[-1] // 2
    exponent = jnp.arange(half_size, dtype=jnp.float32) * 2.0 / values_in.shape[-1]
    frequency = THETA ** (-exponent)
    angles = token_positions.astype(jnp.float32)[:, None] * frequency[None, :]
    cosine = jnp.cos(angles)[:, None, :]
    sine_part = jnp.sin(angles)[:, None, :]
    lower = values_in[..., :half_size]
    upper = values_in[..., half_size:]
    return jnp.concatenate(
        [lower * cosine - upper * sine_part, upper * cosine + lower * sine_part], axis=-1
    )


def pick_adapters(table, adapter_ids, owner_index):
    table_count = table.shape[0]
    picked = []
    for block in range(adapter_ids.shape[0]):
        wanted = adapter_ids[block]
        owned = (wanted // table_count) == owner_index
        entry = lax.dynamic_index_in_dim(table, wanted % table_count, axis=0, keepdims=False)
        picked.append(jnp.where(owned, entry, jnp.zeros_like(entry)))
    return jnp.stack(picked)


def reduce_scatter_rows(partial, axis_name, axis_size):
    steps, rows, columns = partial.shape
    pieces = partial.astype(jnp.bfloat16).reshape(steps, axis_size, rows // axis_size, columns)
    received = lax.all_to_all(pieces, axis_name, 1, 1, tiled=False)
    return jnp.sum(received.astype(jnp.float32), axis=1)


def split_half_scatter_steps(partial, axis_name, axis_size):
    return jnp.concatenate(
        [
            split_half_scatter(partial[step : step + 1], axis_name, axis_size)
            for step in range(partial.shape[0])
        ]
    )


def split_half_gather_steps(value, axis_name, axis_size):
    return jnp.concatenate(
        [
            split_half_gather(value[step : step + 1], axis_name, axis_size)
            for step in range(value.shape[0])
        ]
    )


def ring_gather(value, axis_name, axis_size):
    if axis_size < 4 or axis_size % 2:
        return lax.all_gather(value, axis_name, axis=1, tiled=True)
    ring = list(range(0, axis_size, 2)) + list(range(axis_size - 1, 0, -2))
    place = [0] * axis_size
    for position, index in enumerate(ring):
        place[index] = position
    ahead = [(ring[p], ring[(p + 1) % axis_size]) for p in range(axis_size)]
    behind = [(ring[p], ring[(p - 1) % axis_size]) for p in range(axis_size)]
    slots = [None] * axis_size
    slots[0] = value
    forward = backward = value
    for hop in range(1, axis_size // 2 + 1):
        forward = lax.ppermute(forward, axis_name, ahead)
        slots[(-hop) % axis_size] = forward
        if hop < axis_size - hop:
            backward = lax.ppermute(backward, axis_name, behind)
            slots[hop] = backward
    stacked = jnp.stack(slots)
    places = jnp.asarray(place, dtype=jnp.int32)
    me = lax.axis_index(axis_name)
    order = (places - places[me]) % axis_size
    gathered = jnp.take(stacked, order, axis=0)
    steps, rows, columns = value.shape
    return gathered.transpose(1, 0, 2, 3).reshape(steps, axis_size * rows, columns)


def split_half_scatter(partial, axis_name, axis_size):
    steps, rows, columns = partial.shape
    if axis_size < 4 or axis_size & (axis_size - 1):
        return reduce_scatter_rows(partial, axis_name, axis_size)
    half = axis_size // 2
    me = lax.axis_index(axis_name)
    chunks = partial.reshape(steps, axis_size, rows // axis_size, columns)
    narrow = chunks.astype(jnp.bfloat16)
    own = lax.dynamic_index_in_dim(chunks, me, axis=1, keepdims=False)
    mirror = lax.dynamic_index_in_dim(chunks, me ^ half, axis=1, keepdims=False)
    for offset in range(1, half):
        peer = me ^ offset
        outgoing = jnp.stack(
            [
                lax.dynamic_index_in_dim(narrow, peer, axis=1, keepdims=False),
                lax.dynamic_index_in_dim(narrow, peer ^ half, axis=1, keepdims=False),
            ]
        )
        incoming = lax.ppermute(
            outgoing, axis_name, [(i, i ^ offset) for i in range(axis_size)]
        ).astype(jnp.float32)
        own = own + incoming[0]
        mirror = mirror + incoming[1]
    across = lax.ppermute(
        mirror.astype(jnp.bfloat16), axis_name, [(i, i ^ half) for i in range(axis_size)]
    )
    return own + across.astype(jnp.float32)


def doubling_gather(value, axis_name, axis_size, axis):
    if axis_size & (axis_size - 1):
        return lax.all_gather(value, axis_name, axis=axis, tiled=True)
    me = lax.axis_index(axis_name)
    held = value
    distance = 1
    while distance < axis_size:
        other = lax.ppermute(held, axis_name, [(i, i ^ distance) for i in range(axis_size)])
        upper = (me // distance) % 2 == 1
        first = jnp.where(upper, other, held)
        second = jnp.where(upper, held, other)
        held = jnp.concatenate([first, second], axis=axis)
        distance *= 2
    return held


def split_half_gather(value, axis_name, axis_size):
    if axis_size < 4 or axis_size & (axis_size - 1):
        return lax.all_gather(value, axis_name, axis=1, tiled=True)
    half = axis_size // 2
    me = lax.axis_index(axis_name)
    mirror = lax.ppermute(value, axis_name, [(i, i ^ half) for i in range(axis_size)])
    pair = jnp.stack([value, mirror])
    slots = [None] * axis_size
    slots[0], slots[half] = value, mirror
    for offset in range(1, half):
        incoming = lax.ppermute(pair, axis_name, [(i, i ^ offset) for i in range(axis_size)])
        slots[offset], slots[offset + half] = incoming[0], incoming[1]
    stacked = jnp.stack(slots)
    order = jnp.arange(axis_size, dtype=jnp.int32) ^ me
    gathered = jnp.take(stacked, order, axis=0)
    steps, rows, columns = value.shape
    return gathered.transpose(1, 0, 2, 3).reshape(steps, axis_size * rows, columns)


def tree_sum(value, axes):
    for axis_name in axes:
        size = lax.axis_size(axis_name)
        if size & (size - 1):
            value = lax.psum(value, axis_name)
            continue
        distance = 1
        while distance < size:
            pairs = [(i, i ^ distance) for i in range(size)]
            value = value + lax.ppermute(value, axis_name, pairs)
            distance *= 2
    return value


def sum_then_spread(value, sum_axes, spread_axes):
    return tree_sum(tree_sum(value, sum_axes).astype(jnp.bfloat16), spread_axes)


def halving_scatter(partial, axis_name, axis_size):
    steps, rows, columns = partial.shape
    if axis_size & (axis_size - 1):
        return lax.psum_scatter(partial, axis_name, scatter_dimension=1, tiled=True)
    me = lax.axis_index(axis_name)
    held = partial.reshape(steps, axis_size, rows // axis_size, columns)
    distance = 1
    while distance < axis_size:
        count = held.shape[1]
        pairs = held.reshape(steps, count // 2, 2, rows // axis_size, columns)
        mine = (me // distance) % 2
        keep = lax.dynamic_index_in_dim(pairs, mine, axis=2, keepdims=False)
        give = lax.dynamic_index_in_dim(pairs, 1 - mine, axis=2, keepdims=False)
        swap = [(i, i ^ distance) for i in range(axis_size)]
        if distance > 1:
            give = give.astype(jnp.bfloat16)
        held = keep + lax.ppermute(give, axis_name, swap).astype(jnp.float32)
        distance *= 2
    return held.reshape(steps, rows // axis_size, columns)


def attend(query_rows, previous_keys, previous_values, incoming_keys, incoming_values, lengths):
    steps, count_of_rows = query_rows.shape[0], query_rows.shape[1]
    groups = QUERY_HEADS // KEY_VALUE_HEADS
    context_window = previous_keys.shape[1]
    grouped_heads = query_rows.reshape(
        steps, count_of_rows, KEY_VALUE_HEADS, groups, HEAD_FEATURES
    ).transpose(1, 2, 0, 3, 4).reshape(count_of_rows, KEY_VALUE_HEADS, steps * groups, HEAD_FEATURES)
    keys_previous = previous_keys.reshape(
        count_of_rows, context_window, KEY_VALUE_HEADS, HEAD_FEATURES
    )
    values_previous = previous_values.reshape(
        count_of_rows, context_window, KEY_VALUE_HEADS, HEAD_FEATURES
    )
    keys_incoming = incoming_keys.reshape(
        steps, count_of_rows, KEY_VALUE_HEADS, HEAD_FEATURES
    ).transpose(1, 0, 2, 3)
    values_incoming = incoming_values.reshape(
        steps, count_of_rows, KEY_VALUE_HEADS, HEAD_FEATURES
    ).transpose(1, 0, 2, 3)
    factor = HEAD_FEATURES ** (-0.5)
    score_old = (
        jnp.einsum(
            "rhqd,rchd->rhqc", grouped_heads, keys_previous, preferred_element_type=jnp.float32
        )
        * factor
    )
    score_new = (
        jnp.einsum(
            "rhqd,rshd->rhqs", grouped_heads, keys_incoming, preferred_element_type=jnp.float32
        )
        * factor
    )
    live_old = (jnp.arange(context_window, dtype=jnp.int32)[None, :] < lengths[:, None])[
        :, None, None, :
    ]
    query_step = jnp.arange(steps * groups, dtype=jnp.int32) // groups
    live_new = (jnp.arange(steps, dtype=jnp.int32)[None, :] <= query_step[:, None])[
        None, None, :, :
    ]
    score_old = jnp.where(live_old, score_old, -1e30)
    score_new = jnp.where(live_new, score_new, -1e30)
    peak_score = jnp.maximum(jnp.max(score_old, axis=-1), jnp.max(score_new, axis=-1))
    weight_old = jnp.where(live_old, jnp.exp(score_old - peak_score[..., None]), 0.0)
    weight_new = jnp.where(live_new, jnp.exp(score_new - peak_score[..., None]), 0.0)
    weight_sum = jnp.sum(weight_old, axis=-1) + jnp.sum(weight_new, axis=-1)
    mixed_out = jnp.einsum(
        "rhqc,rchd->rhqd",
        weight_old.astype(jnp.bfloat16),
        values_previous,
        preferred_element_type=jnp.float32,
    )
    mixed_out = mixed_out + jnp.einsum(
        "rhqs,rshd->rhqd",
        weight_new.astype(jnp.bfloat16),
        values_incoming,
        preferred_element_type=jnp.float32,
    )
    mixed_out = (mixed_out / weight_sum[..., None]).astype(jnp.bfloat16)
    return mixed_out.reshape(
        count_of_rows, KEY_VALUE_HEADS, steps, groups, HEAD_FEATURES
    ).transpose(2, 0, 1, 3, 4).reshape(steps, count_of_rows, -1)


def local(
    inputs,
    norm_gain,
    query_weight,
    key_weight,
    value_weight,
    output_weight,
    query_down,
    query_up,
    output_down,
    output_up,
    block_adapter,
    cache_lengths,
    cache_keys,
    cache_values,
):
    across_first = lax.axis_size("gx")
    across_second = lax.axis_size("gy")
    index_first = lax.axis_index("gx")
    index_second = lax.axis_index("gy")
    steps = inputs.shape[0]
    request_count = inputs.shape[1] * across_second
    width = inputs.shape[2] * across_first
    local_rows = cache_keys.shape[0]
    block_count = block_adapter.shape[0]
    block_rows = request_count // block_count
    query_width = query_weight.shape[1]
    key_width = key_weight.shape[1]
    norm_scale = norm_gain.astype(jnp.float32)
    query_first = pick_adapters(query_down, block_adapter, index_second)
    query_second = pick_adapters(query_up, block_adapter, index_first)
    output_first = pick_adapters(output_down, block_adapter, index_first)
    output_second = pick_adapters(output_up, block_adapter, index_second)

    own_wide = inputs.astype(jnp.float32)
    own_squares = tree_sum(jnp.sum(own_wide * own_wide, axis=2), ("gx",))
    squares = doubling_gather(own_squares, "gy", across_second, 1)
    rows_all = doubling_gather(inputs, "gy", across_second, 1)
    rows_wide = rows_all.astype(jnp.float32)
    factor_rows = lax.rsqrt(squares / width + EPS)
    normed = (rows_wide * factor_rows[..., None] * norm_scale).astype(jnp.bfloat16)

    blocked = normed.reshape(steps, block_count, block_rows, -1)
    rank_part = jnp.einsum(
        "tbnd,bdr->tbnr", blocked, query_first, preferred_element_type=jnp.float32
    )
    rank_query = sum_then_spread(rank_part, ("gx",), ("gy",))
    delta_query = jnp.einsum(
        "tbnr,bre->tbne", rank_query, query_second, preferred_element_type=jnp.float32
    ).reshape(steps, request_count, -1)
    query_main = lax.optimization_barrier(
        jnp.einsum("tnd,de->tne", normed, query_weight, preferred_element_type=jnp.float32)
    )
    part_query = query_main + delta_query
    part_key = jnp.einsum("tnd,de->tne", normed, key_weight, preferred_element_type=jnp.float32)
    part_value = jnp.einsum(
        "tnd,de->tne", normed, value_weight, preferred_element_type=jnp.float32
    )
    joined = jnp.concatenate([part_query, part_key, part_value], axis=-1)
    summed = split_half_scatter_steps(joined, "gx", across_first).astype(jnp.bfloat16)
    chunk_rows = summed.shape[1] // across_second
    spread = lax.all_to_all(
        summed.reshape(steps, across_second, chunk_rows, -1), "gy", 1, 2, tiled=False
    )
    query_full = spread[..., :query_width].reshape(steps, local_rows, -1)
    key_full = spread[..., query_width : query_width + key_width].reshape(steps, local_rows, -1)
    value_full = spread[..., query_width + key_width :].reshape(steps, local_rows, -1)

    token_positions = (
        cache_lengths[None, :] + jnp.arange(steps, dtype=jnp.int32)[:, None]
    ).reshape(-1)
    query_rot = rotary_embedding(
        query_full.astype(jnp.float32).reshape(steps * local_rows, QUERY_HEADS, HEAD_FEATURES),
        token_positions,
    ).astype(jnp.bfloat16)
    key_rot = rotary_embedding(
        key_full.astype(jnp.float32).reshape(steps * local_rows, KEY_VALUE_HEADS, HEAD_FEATURES),
        token_positions,
    ).astype(jnp.bfloat16)
    mixed_local = attend(
        query_rot.reshape(steps, local_rows, -1),
        cache_keys,
        cache_values,
        key_rot.reshape(steps, local_rows, -1),
        value_full,
        cache_lengths,
    )
    head_group = lax.all_to_all(
        mixed_local.reshape(steps, local_rows, across_second, -1), "gy", 2, 1, tiled=False
    ).reshape(steps, across_second * local_rows, -1)
    mixed_all = ring_gather(head_group, "gx", across_first)
    rank_part_out = jnp.einsum(
        "tbnq,bqr->tbnr",
        mixed_all.reshape(steps, block_count, block_rows, -1),
        output_first,
        preferred_element_type=jnp.float32,
    )
    rank_output = sum_then_spread(rank_part_out, ("gy",), ("gx",))
    delta_output = jnp.einsum(
        "tbnr,bre->tbne", rank_output, output_second, preferred_element_type=jnp.float32
    ).reshape(steps, request_count, -1)
    output_main = lax.optimization_barrier(
        jnp.einsum("tnq,qe->tne", mixed_all, output_weight, preferred_element_type=jnp.float32)
    )
    partial_out = output_main + delta_output
    return jnp.concatenate(
        [
            halving_scatter(partial_out[step : step + 1], "gy", across_second)
            for step in range(steps)
        ]
    ).astype(jnp.bfloat16)


def solution(mesh):
    in_specs = (
        P(None, "gy", "gx"),
        P("gx"),
        P("gx", "gy"),
        P("gx", "gy"),
        P("gx", "gy"),
        P("gy", "gx"),
        P("gy", "gx", None),
        P("gx", None, "gy"),
        P("gx", "gy", None),
        P("gy", None, "gx"),
        P(),
        P(("gx", "gy")),
        P(("gx", "gy"), None, None),
        P(("gx", "gy"), None, None),
    )
    out_specs = P(None, "gy", "gx")
    return jax.shard_map(local, mesh=mesh, in_specs=in_specs, out_specs=out_specs, check_vma=False)
```

```python
import jax
import jax.numpy as jnp
from jax import lax
from jax.sharding import PartitionSpec as P

QUERY_HEADS = 64
KEY_VALUE_HEADS = 8
HEAD_FEATURES = 128
BLOCK = 128


EPS = 1e-05
THETA = 500000.0


def rotary_embedding(values_in, token_positions):
    half_size = values_in.shape[-1] // 2
    exponent = jnp.arange(half_size, dtype=jnp.float32) * 2.0 / values_in.shape[-1]
    frequency = THETA ** (-exponent)
    angles = token_positions.astype(jnp.float32)[:, None] * frequency[None, :]
    cosine = jnp.cos(angles)[:, None, :]
    sine_part = jnp.sin(angles)[:, None, :]
    lower = values_in[..., :half_size]
    upper = values_in[..., half_size:]
    return jnp.concatenate(
        [lower * cosine - upper * sine_part, upper * cosine + lower * sine_part], axis=-1
    )


def pick_adapters(table, adapter_ids, owner_index):
    table_count = table.shape[0]
    picked = []
    for block in range(adapter_ids.shape[0]):
        wanted = adapter_ids[block]
        owned = (wanted // table_count) == owner_index
        entry = lax.dynamic_index_in_dim(table, wanted % table_count, axis=0, keepdims=False)
        picked.append(jnp.where(owned, entry, jnp.zeros_like(entry)))
    return jnp.stack(picked)


def reduce_scatter_rows(partial, axis_name, axis_size):
    steps, rows, columns = partial.shape
    pieces = partial.astype(jnp.bfloat16).reshape(steps, axis_size, rows // axis_size, columns)
    received = lax.all_to_all(pieces, axis_name, 1, 1, tiled=False)
    return jnp.sum(received.astype(jnp.float32), axis=1)


def split_half_scatter_steps(partial, axis_name, axis_size):
    return jnp.concatenate(
        [
            split_half_scatter(partial[step : step + 1], axis_name, axis_size)
            for step in range(partial.shape[0])
        ]
    )


def split_half_gather_steps(value, axis_name, axis_size):
    return jnp.concatenate(
        [
            split_half_gather(value[step : step + 1], axis_name, axis_size)
            for step in range(value.shape[0])
        ]
    )


def ring_gather(value, axis_name, axis_size):
    if axis_size < 4 or axis_size % 2:
        return lax.all_gather(value, axis_name, axis=1, tiled=True)
    ring = list(range(0, axis_size, 2)) + list(range(axis_size - 1, 0, -2))
    place = [0] * axis_size
    for position, index in enumerate(ring):
        place[index] = position
    ahead = [(ring[p], ring[(p + 1) % axis_size]) for p in range(axis_size)]
    behind = [(ring[p], ring[(p - 1) % axis_size]) for p in range(axis_size)]
    slots = [None] * axis_size
    slots[0] = value
    forward = backward = value
    for hop in range(1, axis_size // 2 + 1):
        forward = lax.ppermute(forward, axis_name, ahead)
        slots[(-hop) % axis_size] = forward
        if hop < axis_size - hop:
            backward = lax.ppermute(backward, axis_name, behind)
            slots[hop] = backward
    stacked = jnp.stack(slots)
    places = jnp.asarray(place, dtype=jnp.int32)
    me = lax.axis_index(axis_name)
    order = (places - places[me]) % axis_size
    gathered = jnp.take(stacked, order, axis=0)
    steps, rows, columns = value.shape
    return gathered.transpose(1, 0, 2, 3).reshape(steps, axis_size * rows, columns)


def split_half_scatter(partial, axis_name, axis_size):
    steps, rows, columns = partial.shape
    if axis_size < 4 or axis_size & (axis_size - 1):
        return reduce_scatter_rows(partial, axis_name, axis_size)
    half = axis_size // 2
    me = lax.axis_index(axis_name)
    chunks = partial.reshape(steps, axis_size, rows // axis_size, columns)
    narrow = chunks.astype(jnp.bfloat16)
    own = lax.dynamic_index_in_dim(chunks, me, axis=1, keepdims=False)
    mirror = lax.dynamic_index_in_dim(chunks, me ^ half, axis=1, keepdims=False)
    for offset in range(1, half):
        peer = me ^ offset
        outgoing = jnp.stack(
            [
                lax.dynamic_index_in_dim(narrow, peer, axis=1, keepdims=False),
                lax.dynamic_index_in_dim(narrow, peer ^ half, axis=1, keepdims=False),
            ]
        )
        incoming = lax.ppermute(
            outgoing, axis_name, [(i, i ^ offset) for i in range(axis_size)]
        ).astype(jnp.float32)
        own = own + incoming[0]
        mirror = mirror + incoming[1]
    across = lax.ppermute(
        mirror.astype(jnp.bfloat16), axis_name, [(i, i ^ half) for i in range(axis_size)]
    )
    return own + across.astype(jnp.float32)


def doubling_gather(value, axis_name, axis_size, axis):
    if axis_size & (axis_size - 1):
        return lax.all_gather(value, axis_name, axis=axis, tiled=True)
    me = lax.axis_index(axis_name)
    held = value
    distance = 1
    while distance < axis_size:
        other = lax.ppermute(held, axis_name, [(i, i ^ distance) for i in range(axis_size)])
        upper = (me // distance) % 2 == 1
        first = jnp.where(upper, other, held)
        second = jnp.where(upper, held, other)
        held = jnp.concatenate([first, second], axis=axis)
        distance *= 2
    return held


def split_half_gather(value, axis_name, axis_size):
    if axis_size < 4 or axis_size & (axis_size - 1):
        return lax.all_gather(value, axis_name, axis=1, tiled=True)
    half = axis_size // 2
    me = lax.axis_index(axis_name)
    mirror = lax.ppermute(value, axis_name, [(i, i ^ half) for i in range(axis_size)])
    pair = jnp.stack([value, mirror])
    slots = [None] * axis_size
    slots[0], slots[half] = value, mirror
    for offset in range(1, half):
        incoming = lax.ppermute(pair, axis_name, [(i, i ^ offset) for i in range(axis_size)])
        slots[offset], slots[offset + half] = incoming[0], incoming[1]
    stacked = jnp.stack(slots)
    order = jnp.arange(axis_size, dtype=jnp.int32) ^ me
    gathered = jnp.take(stacked, order, axis=0)
    steps, rows, columns = value.shape
    return gathered.transpose(1, 0, 2, 3).reshape(steps, axis_size * rows, columns)


def tree_sum(value, axes):
    for axis_name in axes:
        size = lax.axis_size(axis_name)
        if size & (size - 1):
            value = lax.psum(value, axis_name)
            continue
        distance = 1
        while distance < size:
            pairs = [(i, i ^ distance) for i in range(size)]
            value = value + lax.ppermute(value, axis_name, pairs)
            distance *= 2
    return value


def sum_then_spread(value, sum_axes, spread_axes):
    return tree_sum(tree_sum(value, sum_axes).astype(jnp.bfloat16), spread_axes)


def halving_scatter(partial, axis_name, axis_size):
    steps, rows, columns = partial.shape
    if axis_size & (axis_size - 1):
        return lax.psum_scatter(partial, axis_name, scatter_dimension=1, tiled=True)
    me = lax.axis_index(axis_name)
    held = partial.reshape(steps, axis_size, rows // axis_size, columns)
    distance = 1
    while distance < axis_size:
        count = held.shape[1]
        pairs = held.reshape(steps, count // 2, 2, rows // axis_size, columns)
        mine = (me // distance) % 2
        keep = lax.dynamic_index_in_dim(pairs, mine, axis=2, keepdims=False)
        give = lax.dynamic_index_in_dim(pairs, 1 - mine, axis=2, keepdims=False)
        swap = [(i, i ^ distance) for i in range(axis_size)]
        give = give.astype(jnp.bfloat16)
        held = keep + lax.ppermute(give, axis_name, swap).astype(jnp.float32)
        distance *= 2
    return held.reshape(steps, rows // axis_size, columns)


def attend(query_rows, previous_keys, previous_values, incoming_keys, incoming_values, lengths):
    steps, count_of_rows = query_rows.shape[0], query_rows.shape[1]
    groups = QUERY_HEADS // KEY_VALUE_HEADS
    context_window = previous_keys.shape[1]
    grouped_heads = query_rows.reshape(
        steps, count_of_rows, KEY_VALUE_HEADS, groups, HEAD_FEATURES
    ).transpose(1, 2, 0, 3, 4).reshape(count_of_rows, KEY_VALUE_HEADS, steps * groups, HEAD_FEATURES)
    keys_previous = previous_keys.reshape(
        count_of_rows, context_window, KEY_VALUE_HEADS, HEAD_FEATURES
    )
    values_previous = previous_values.reshape(
        count_of_rows, context_window, KEY_VALUE_HEADS, HEAD_FEATURES
    )
    keys_incoming = incoming_keys.reshape(
        steps, count_of_rows, KEY_VALUE_HEADS, HEAD_FEATURES
    ).transpose(1, 0, 2, 3)
    values_incoming = incoming_values.reshape(
        steps, count_of_rows, KEY_VALUE_HEADS, HEAD_FEATURES
    ).transpose(1, 0, 2, 3)
    factor = HEAD_FEATURES ** (-0.5)
    score_old = (
        jnp.einsum(
            "rhqd,rchd->rhqc", grouped_heads, keys_previous, preferred_element_type=jnp.float32
        )
        * factor
    )
    score_new = (
        jnp.einsum(
            "rhqd,rshd->rhqs", grouped_heads, keys_incoming, preferred_element_type=jnp.float32
        )
        * factor
    )
    live_old = (jnp.arange(context_window, dtype=jnp.int32)[None, :] < lengths[:, None])[
        :, None, None, :
    ]
    query_step = jnp.arange(steps * groups, dtype=jnp.int32) // groups
    live_new = (jnp.arange(steps, dtype=jnp.int32)[None, :] <= query_step[:, None])[
        None, None, :, :
    ]
    score_old = jnp.where(live_old, score_old, -1e30)
    score_new = jnp.where(live_new, score_new, -1e30)
    peak_score = jnp.maximum(jnp.max(score_old, axis=-1), jnp.max(score_new, axis=-1))
    weight_old = jnp.where(live_old, jnp.exp(score_old - peak_score[..., None]), 0.0)
    weight_new = jnp.where(live_new, jnp.exp(score_new - peak_score[..., None]), 0.0)
    weight_sum = jnp.sum(weight_old, axis=-1) + jnp.sum(weight_new, axis=-1)
    mixed_out = jnp.einsum(
        "rhqc,rchd->rhqd",
        weight_old.astype(jnp.bfloat16),
        values_previous,
        preferred_element_type=jnp.float32,
    )
    mixed_out = mixed_out + jnp.einsum(
        "rhqs,rshd->rhqd",
        weight_new.astype(jnp.bfloat16),
        values_incoming,
        preferred_element_type=jnp.float32,
    )
    mixed_out = (mixed_out / weight_sum[..., None]).astype(jnp.bfloat16)
    return mixed_out.reshape(
        count_of_rows, KEY_VALUE_HEADS, steps, groups, HEAD_FEATURES
    ).transpose(2, 0, 1, 3, 4).reshape(steps, count_of_rows, -1)


def local(
    inputs,
    norm_gain,
    query_weight,
    key_weight,
    value_weight,
    output_weight,
    query_down,
    query_up,
    output_down,
    output_up,
    block_adapter,
    cache_lengths,
    cache_keys,
    cache_values,
):
    across_first = lax.axis_size("gx")
    across_second = lax.axis_size("gy")
    index_first = lax.axis_index("gx")
    index_second = lax.axis_index("gy")
    steps = inputs.shape[0]
    request_count = inputs.shape[1] * across_second
    width = inputs.shape[2] * across_first
    local_rows = cache_keys.shape[0]
    block_count = block_adapter.shape[0]
    block_rows = request_count // block_count
    query_width = query_weight.shape[1]
    key_width = key_weight.shape[1]
    norm_scale = norm_gain.astype(jnp.float32)
    query_first = pick_adapters(query_down, block_adapter, index_second)
    query_second = pick_adapters(query_up, block_adapter, index_first)
    output_first = pick_adapters(output_down, block_adapter, index_first)
    output_second = pick_adapters(output_up, block_adapter, index_second)

    rows_all = doubling_gather(inputs, "gy", across_second, 1)
    rows_wide = rows_all.astype(jnp.float32)
    squares = tree_sum(jnp.sum(rows_wide * rows_wide, axis=2), ("gx",))
    factor_rows = lax.rsqrt(squares / width + EPS)
    normed = (rows_wide * factor_rows[..., None] * norm_scale).astype(jnp.bfloat16)

    blocked = normed.reshape(steps, block_count, block_rows, -1)
    rank_part = jnp.einsum(
        "tbnd,bdr->tbnr", blocked, query_first, preferred_element_type=jnp.float32
    )
    rank_query = sum_then_spread(rank_part, ("gx",), ("gy",))
    delta_query = jnp.einsum(
        "tbnr,bre->tbne", rank_query, query_second, preferred_element_type=jnp.float32
    ).reshape(steps, request_count, -1)
    query_main = lax.optimization_barrier(
        jnp.einsum("tnd,de->tne", normed, query_weight, preferred_element_type=jnp.float32)
    )
    part_query = query_main + delta_query
    part_key = jnp.einsum("tnd,de->tne", normed, key_weight, preferred_element_type=jnp.float32)
    part_value = jnp.einsum(
        "tnd,de->tne", normed, value_weight, preferred_element_type=jnp.float32
    )
    joined = jnp.concatenate([part_query, part_key, part_value], axis=-1)
    summed = split_half_scatter_steps(joined, "gx", across_first).astype(jnp.bfloat16)
    chunk_rows = summed.shape[1] // across_second
    spread = lax.all_to_all(
        summed.reshape(steps, across_second, chunk_rows, -1), "gy", 1, 2, tiled=False
    )
    query_full = spread[..., :query_width].reshape(steps, local_rows, -1)
    key_full = spread[..., query_width : query_width + key_width].reshape(steps, local_rows, -1)
    value_full = spread[..., query_width + key_width :].reshape(steps, local_rows, -1)

    token_positions = (
        cache_lengths[None, :] + jnp.arange(steps, dtype=jnp.int32)[:, None]
    ).reshape(-1)
    query_rot = rotary_embedding(
        query_full.astype(jnp.float32).reshape(steps * local_rows, QUERY_HEADS, HEAD_FEATURES),
        token_positions,
    ).astype(jnp.bfloat16)
    key_rot = rotary_embedding(
        key_full.astype(jnp.float32).reshape(steps * local_rows, KEY_VALUE_HEADS, HEAD_FEATURES),
        token_positions,
    ).astype(jnp.bfloat16)
    mixed_local = attend(
        query_rot.reshape(steps, local_rows, -1),
        cache_keys,
        cache_values,
        key_rot.reshape(steps, local_rows, -1),
        value_full,
        cache_lengths,
    )
    head_group = lax.all_to_all(
        mixed_local.reshape(steps, local_rows, across_second, -1), "gy", 2, 1, tiled=False
    ).reshape(steps, across_second * local_rows, -1)
    mixed_all = ring_gather(head_group, "gx", across_first)
    rank_part_out = jnp.einsum(
        "tbnq,bqr->tbnr",
        mixed_all.reshape(steps, block_count, block_rows, -1),
        output_first,
        preferred_element_type=jnp.float32,
    )
    rank_output = sum_then_spread(rank_part_out, ("gy",), ("gx",))
    delta_output = jnp.einsum(
        "tbnr,bre->tbne", rank_output, output_second, preferred_element_type=jnp.float32
    ).reshape(steps, request_count, -1)
    output_main = lax.optimization_barrier(
        jnp.einsum("tnq,qe->tne", mixed_all, output_weight, preferred_element_type=jnp.float32)
    )
    partial_out = output_main + delta_output
    return jnp.concatenate(
        [
            halving_scatter(partial_out[step : step + 1], "gy", across_second)
            for step in range(steps)
        ]
    ).astype(jnp.bfloat16)


def solution(mesh):
    in_specs = (
        P(None, "gy", "gx"),
        P("gx"),
        P("gx", "gy"),
        P("gx", "gy"),
        P("gx", "gy"),
        P("gy", "gx"),
        P("gy", "gx", None),
        P("gx", None, "gy"),
        P("gx", "gy", None),
        P("gy", None, "gx"),
        P(),
        P(("gx", "gy")),
        P(("gx", "gy"), None, None),
        P(("gx", "gy"), None, None),
    )
    out_specs = P(None, "gy", "gx")
    return jax.shard_map(local, mesh=mesh, in_specs=in_specs, out_specs=out_specs, check_vma=False)
```
